32 devices in a mesh: groups: 2 (over x), node: 16 (over z, y, core).
Axes of the slice: x: 2, y: 2, z: 4, core: 2. Of those that a mesh axis runs over, the one named last changes fastest.
Arguments:
- features: bfloat16 [32768, 1024], P(('groups', 'node')), parts along dimension 0, may hold values from -6 to 6
- filter_gate_weight: bfloat16 [64, 64], replicated, may hold values from -0.75 to 0.75
- skip_weight: bfloat16 [32, 256], replicated, may hold values from -1 to 1
- mix_weight: bfloat16 [96, 32], replicated, may hold values from -0.625 to 0.625
- band_weight: bfloat16 [16384, 192], P('node'), may hold values from -0.4375 to 0.4375
- far_weight: bfloat16 [64, 15360], P(None, 'node'), may hold values from -0.75 to 0.75
- far_ptr: int32 [16, 17], P('node'), may hold values from 0 to 15, as said below
- far_col: int32 [16, 15], P('node'), may hold values from 0 to 31, as said below
- export_block: int32 [16, 2], replicated, may hold values from 0 to 15, as said below
Outputs:
- residual_output: bfloat16 [32768, 512], P(('groups', 'node')), parts along dimension 0
- skip_out: bfloat16 [32768, 4096], P(('groups', 'node')), parts along dimension 0
The draws below stay inside these ranges and needn't reach their ends.
There are 2 independent parts, one for each index of `groups`. The reference program is written for one: setup_inputs(seed, part) draws one part's arguments, and reference() takes and returns one part's arrays. A program takes and returns all parts, laid end to end along the dimension named above; an argument that names none is the same for every part. Nothing has to cross between parts.
Inputs may be any that keep to these rules, and one draw needn't show every extreme that they name: Each row of export_block holds 2 different local block numbers, each below 16. `far_ptr`: each row starts at 0 and never falls; its last entry is the number of used far-block slots of that device, and some device uses all 15. `far_col`: slots below far_ptr[d][16] name blocks of devices other than d, at most one slot for each other device; the other slots hold 0 and belong to no block row. The device that uses all slots reads entry 0 of device 0 and the last entry of the last device.
All inputs are finite; a program needn't handle non-finite values.
Results may differ from the reference program's by a relative error of at most 0.0052.
Values may be sent and summed in bfloat16 or wider, within the bound.
No kernel may reach another device: no remote copies, remote signals or barrier semaphores. Data moves between devices by JAX's collectives and lax.ppermute only.
A program may use at most 128 MiB of HBM per device.

```python
import jax
import jax.numpy as jnp
from jax import lax

BLK = 64
BLK_DEV = 16
TOUT = 16
DILATION_STEP = 16
EXPORT = 2
CHANNEL_WIDTH = 32
S = 256
TIN = 32
NODES = 16384
FAR_CAP = 15
N_NODE = 16


def far_plan(key):
    peer_count = FAR_CAP + 1
    key_list = jax.random.split(jax.random.fold_in(key, 17), 7)
    exports = jax.vmap(lambda subkey: jax.random.permutation(subkey, BLK_DEV)[:EXPORT])(jax.random.split(key_list[0], peer_count)).astype(jnp.int32)
    count_left = jax.random.randint(key_list[1], (peer_count,), 0, FAR_CAP + 1)
    count_right = jax.random.randint(key_list[2], (peer_count,), 0, FAR_CAP + 1)
    counts = FAR_CAP - count_left * count_right // (2 * FAR_CAP)
    busiest = jax.random.randint(key_list[3], (), 1, peer_count - 1)
    owners = jnp.arange(peer_count, dtype=jnp.int32)
    counts = jnp.where(owners == busiest, FAR_CAP, counts)
    orders = jax.vmap(lambda subkey: jax.random.permutation(subkey, FAR_CAP))(jax.random.split(key_list[4], peer_count)).astype(jnp.int32)
    sources = orders + (orders >= owners[:, None]).astype(jnp.int32)
    slot_pick = jax.random.randint(key_list[5], (peer_count, FAR_CAP), 0, EXPORT)
    forced_pick = jnp.where(sources == 0, 0, EXPORT - 1)
    slot_pick = jnp.where((owners == busiest)[:, None], forced_pick, slot_pick)
    slot_ids = jnp.arange(FAR_CAP, dtype=jnp.int32)[None, :]
    in_use = slot_ids < counts[:, None]
    columns = jnp.where(in_use, sources * EXPORT + slot_pick, 0).astype(jnp.int32)
    row_ids = jax.random.randint(key_list[6], (peer_count, FAR_CAP), 0, BLK_DEV)
    row_ids = jnp.sort(jnp.where(in_use, row_ids, BLK_DEV), axis=1)
    limits = jnp.arange(BLK_DEV + 1, dtype=jnp.int32)
    pointers = jnp.sum((row_ids[:, None, :] < limits[None, :, None]).astype(jnp.int32), axis=2).astype(jnp.int32)
    return (exports, columns, pointers)


def draw_far_ptr(key, part):
    return far_plan(key)[2]


def draw_far_col(key, part):
    return far_plan(key)[1]


def draw_export_block(key, part):
    return far_plan(key)[0]


def block_scale(rng, extent, cuts, smallest, largest):
    def one(axis_at, blocks):
        steps = jax.random.uniform(jax.random.fold_in(jax.random.fold_in(rng, 6), axis_at), (blocks,), jnp.float32, smallest / len(cuts), largest / len(cuts))
        return jnp.repeat(jnp.exp(steps), extent[axis_at] // blocks).reshape((-1,) + (1,) * (len(extent) - axis_at - 1))

    gain = one(*cuts[0])
    for cut in cuts[1:]:
        gain = gain * one(*cut)
    return gain


def noise(stream_key, dims, spread, bound, shards=(), kind=jnp.bfloat16):
    array = jax.random.normal(stream_key, dims, jnp.float32) * spread
    if len(shards) > 0:
        array = block_scale(stream_key, dims, shards, -0.22, 0.18) * array
    return jnp.clip(array, min=-bound, max=bound).astype(kind)


def setup_inputs(seed: int = 0, part: int = 0) -> dict:
    keys = jax.random.split(jax.random.key(seed), 10)
    part_splits = jax.random.split(jax.random.fold_in(keys[9], part), 10)
    features = noise(part_splits[0], (NODES, TIN * CHANNEL_WIDTH), 1.0, 6.0, ((0, 16),))
    filter_gate_weight = noise(keys[1], (2 * CHANNEL_WIDTH, 2 * CHANNEL_WIDTH), (2 * CHANNEL_WIDTH) ** -0.5, 0.75)
    skip_weight = noise(keys[2], (CHANNEL_WIDTH, S), CHANNEL_WIDTH ** -0.5, 1.0)
    mix_weight = noise(keys[3], (3 * CHANNEL_WIDTH, CHANNEL_WIDTH), (3 * CHANNEL_WIDTH) ** -0.5, 0.625)
    band_weight = noise(keys[4], (NODES, 3 * BLK), (3 * BLK) ** -0.5, 0.4375, ((0, 16),))
    far_weight = noise(keys[5], (BLK, N_NODE * FAR_CAP * BLK), BLK ** -0.5, 0.75, ((1, 16),))
    far_ptr = draw_far_ptr(jax.random.fold_in(keys[9], 71), part)
    far_col = draw_far_col(jax.random.fold_in(keys[9], 71), part)
    export_block = draw_export_block(jax.random.fold_in(keys[9], 71), part)
    return dict(features=features, filter_gate_weight=filter_gate_weight, skip_weight=skip_weight, mix_weight=mix_weight, band_weight=band_weight, far_weight=far_weight, far_ptr=far_ptr, far_col=far_col, export_block=export_block)


def front_part(args):
    series_input, filter_gate_weight, skip_weight = args
    earlier = series_input[:, :TOUT].astype(jnp.float32)
    later_taps = series_input[:, DILATION_STEP:].astype(jnp.float32)
    preact = jnp.einsum('myv,vi->myi', earlier, filter_gate_weight[:CHANNEL_WIDTH].astype(jnp.float32))
    preact = preact + jnp.einsum('myv,vi->myi', later_taps, filter_gate_weight[CHANNEL_WIDTH:].astype(jnp.float32))
    hidden = (jnp.tanh(preact[..., :CHANNEL_WIDTH]) * jax.nn.sigmoid(preact[..., CHANNEL_WIDTH:])).astype(jnp.bfloat16)
    skip_rows = jnp.einsum('ntc,cs->nts', hidden.astype(jnp.float32), skip_weight.astype(jnp.float32))
    return hidden, skip_rows.astype(jnp.bfloat16)


def diffuse(field_blocks, band_weight, far_weight, far_ptr, far_col, export_block):
    block_total = field_blocks.shape[0]
    width = field_blocks.shape[2]
    zero_block = jnp.zeros((1, BLK, width), jnp.bfloat16)
    padded = jnp.concatenate([zero_block, field_blocks, zero_block], axis=0).astype(jnp.float32)
    band_blocks = band_weight.reshape(block_total, BLK, 3 * BLK).astype(jnp.float32)
    summed = jnp.zeros((block_total, BLK, width), jnp.float32)
    for shift_pos in range(3):
        summed = summed + jnp.einsum('rij,rjm->rim', band_blocks[:, :, shift_pos * BLK:(shift_pos + 1) * BLK], padded[shift_pos:shift_pos + block_total])
    device_count = far_ptr.shape[0]
    far_cap = far_col.shape[1]
    weights_all = far_weight.reshape(BLK, device_count, far_cap, BLK).transpose(1, 2, 0, 3)

    def per_device(args):
        weights, columns, pointers = args
        owners = columns // EXPORT
        entries = columns % EXPORT
        block_ids = export_block[owners, entries]
        global_blocks = (owners * BLK_DEV + block_ids).astype(jnp.int32)
        pieces = field_blocks[global_blocks].astype(jnp.float32)
        products = jnp.einsum('kij,kjm->kim', weights.astype(jnp.float32), pieces, precision=lax.Precision.HIGHEST)
        slot_ids = jnp.arange(far_cap, dtype=jnp.int32)
        assign = ((pointers[:-1, None] <= slot_ids[None, :]) & (slot_ids[None, :] < pointers[1:, None])).astype(jnp.float32)
        return jnp.einsum('rk,kim->rim', assign, products, precision=lax.Precision.HIGHEST)

    far_terms = lax.map(per_device, (weights_all, far_col, far_ptr))
    summed = summed + far_terms.reshape(block_total, BLK, width)
    return summed.astype(jnp.bfloat16)


def reference(features, filter_gate_weight, skip_weight, mix_weight, band_weight, far_weight, far_ptr, far_col, export_block):
    device_count = far_ptr.shape[0]
    node_local = BLK_DEV * BLK
    series_all = features.reshape(device_count, node_local, TIN, CHANNEL_WIDTH)
    hidden_all, skip_all = lax.map(lambda series_input: front_part((series_input, filter_gate_weight, skip_weight)), series_all)
    block_total = device_count * BLK_DEV
    hidden_blocks = hidden_all.reshape(block_total, BLK, TOUT * CHANNEL_WIDTH)
    hop_one = diffuse(hidden_blocks, band_weight, far_weight, far_ptr, far_col, export_block)
    hop_two = diffuse(hop_one, band_weight, far_weight, far_ptr, far_col, export_block)

    def mix_part(args):
        series_input, hidden, first_hop, second_hop = args
        joined = jnp.concatenate([hidden, first_hop.reshape(node_local, TOUT, CHANNEL_WIDTH), second_hop.reshape(node_local, TOUT, CHANNEL_WIDTH)], axis=-1)
        mixed_state = jnp.einsum('myv,vi->myi', joined.astype(jnp.float32), mix_weight.astype(jnp.float32))
        return (series_input[:, DILATION_STEP:].astype(jnp.float32) + mixed_state).astype(jnp.bfloat16)

    residual_all = lax.map(mix_part, (series_all, hidden_all, hop_one.reshape(device_count, node_local, TOUT * CHANNEL_WIDTH), hop_two.reshape(device_count, node_local, TOUT * CHANNEL_WIDTH)))
    residual_output = residual_all.reshape(device_count * node_local, TOUT * CHANNEL_WIDTH)
    skip_out = skip_all.reshape(device_count * node_local, TOUT * S)
    return residual_output, skip_out
```

```python
import jax
import jax.numpy as jnp
from jax import lax
from jax.experimental import pallas as pl
from jax.experimental.pallas import tpu as pltpu
from jax.sharding import PartitionSpec as P

BLK = 64
TOUT = 16
DILATION_STEP = 16
EXPORT = 2
CHANNEL_WIDTH = 32
S = 256
TIN = 32
CHUNK = 256
ROW_TILE = 256

f32 = jnp.float32
bf16 = jnp.bfloat16


def front_kernel(x_ref, wlo_ref, whi_ref, ws_ref, h_ref, s_ref):
    half = x_ref.shape[1] // 2
    chunks = half // CHUNK
    skip_w = ws_ref.shape[1]
    for j in range(chunks):
        x0 = x_ref[:, j * CHUNK : (j + 1) * CHUNK]
        x1 = x_ref[:, half + j * CHUNK : half + (j + 1) * CHUNK]
        pre = jnp.dot(x0, wlo_ref[...], preferred_element_type=f32)
        pre = pre + jnp.dot(x1, whi_ref[...], preferred_element_type=f32)
        h = (jnp.tanh(pre[:, :CHUNK]) * jax.nn.sigmoid(pre[:, CHUNK:])).astype(bf16)
        h_ref[:, j * CHUNK : (j + 1) * CHUNK] = h
        s_ref[:, j * skip_w : (j + 1) * skip_w] = jnp.dot(
            h, ws_ref[...], preferred_element_type=f32
        ).astype(bf16)


def front(features, wlo, whi, ws):
    rows, cols = features.shape
    half = cols // 2
    skip_cols = ws.shape[1] * (half // CHUNK)
    tile = min(ROW_TILE, rows)
    return pl.pallas_call(
        front_kernel,
        grid=(rows // tile,),
        in_specs=[
            pl.BlockSpec((tile, cols), lambda i: (i, 0)),
            pl.BlockSpec(wlo.shape, lambda i: (0, 0)),
            pl.BlockSpec(whi.shape, lambda i: (0, 0)),
            pl.BlockSpec(ws.shape, lambda i: (0, 0)),
        ],
        out_specs=[
            pl.BlockSpec((tile, half), lambda i: (i, 0)),
            pl.BlockSpec((tile, skip_cols), lambda i: (i, 0)),
        ],
        out_shape=[
            jax.ShapeDtypeStruct((rows, half), bf16),
            jax.ShapeDtypeStruct((rows, skip_cols), bf16),
        ],
        compiler_params=pltpu.CompilerParams(vmem_limit_bytes=48 * 1024 * 1024),
        cost_estimate=pl.CostEstimate(
            flops=2 * rows * CHUNK * (4 * CHUNK + ws.shape[1]) * (half // CHUNK),
            transcendentals=rows * half * 2,
            bytes_accessed=2 * rows * (cols + half + skip_cols),
        ),
    )(features, wlo, whi, ws)


def accumulate(src_ref, row_ref, field_ref, lo_ref, hi_ref, arr_ref, band_ref, farw_ref, acc):
    nblk = field_ref.shape[0] // BLK
    far_cap = farw_ref.shape[0]
    for r in range(nblk):
        prev = lo_ref[...] if r == 0 else field_ref[(r - 1) * BLK : r * BLK, :]
        nxt = hi_ref[...] if r == nblk - 1 else field_ref[(r + 1) * BLK : (r + 2) * BLK, :]
        own = field_ref[r * BLK : (r + 1) * BLK, :]
        v = jnp.dot(band_ref[0, r * BLK : (r + 1) * BLK, :], prev, preferred_element_type=f32)
        v = v + jnp.dot(band_ref[1, r * BLK : (r + 1) * BLK, :], own, preferred_element_type=f32)
        v = v + jnp.dot(band_ref[2, r * BLK : (r + 1) * BLK, :], nxt, preferred_element_type=f32)
        acc[r * BLK : (r + 1) * BLK, :] = v
    acc[nblk * BLK :, :] = jnp.zeros((BLK, acc.shape[1]), f32)

    def slot(k, carry):
        row = row_ref[k]
        piece = arr_ref[src_ref[k]]
        start = pl.multiple_of(row * BLK, BLK)
        acc[pl.ds(start, BLK), :] += jnp.dot(farw_ref[k], piece, preferred_element_type=f32)
        return carry

    lax.fori_loop(0, far_cap, slot, 0)


def hop1_kernel(
    src_ref, row_ref, send_ref, field_ref, lo_ref, hi_ref, arr_ref, band_ref, farw_ref,
    out_ref, out_send_ref, acc,
):
    accumulate(src_ref, row_ref, field_ref, lo_ref, hi_ref, arr_ref, band_ref, farw_ref, acc)
    nrows = field_ref.shape[0]
    out_ref[...] = acc[:nrows, :].astype(bf16)
    for p in range(out_send_ref.shape[0]):
        start = pl.multiple_of(send_ref[p] * BLK, BLK)
        out_send_ref[p] = out_ref[pl.ds(start, BLK), :]


def hop2_kernel(
    src_ref, row_ref, field_ref, lo_ref, hi_ref, arr_ref, band_ref, farw_ref,
    x_ref, h_ref, mix_ref, out_ref, acc,
):
    accumulate(src_ref, row_ref, field_ref, lo_ref, hi_ref, arr_ref, band_ref, farw_ref, acc)
    nrows, width = field_ref.shape
    half = x_ref.shape[1] // 2
    for j in range(width // CHUNK):
        cols = slice(j * CHUNK, (j + 1) * CHUNK)
        two = acc[:nrows, cols].astype(bf16)
        v = x_ref[:, half + j * CHUNK : half + (j + 1) * CHUNK].astype(f32)
        v = v + jnp.dot(h_ref[:, cols], mix_ref[0], preferred_element_type=f32)
        v = v + jnp.dot(field_ref[:, cols], mix_ref[1], preferred_element_type=f32)
        v = v + jnp.dot(two, mix_ref[2], preferred_element_type=f32)
        out_ref[:, cols] = v.astype(bf16)


def vmem():
    return pl.BlockSpec(memory_space=pltpu.VMEM)


def smem():
    return pl.BlockSpec(memory_space=pltpu.SMEM)


def hop1(src, rows, send_rows, field, lo, hi, arrived, band3, farw3):
    nrows, width = field.shape
    return pl.pallas_call(
        hop1_kernel,
        in_specs=[smem(), smem(), smem()] + [vmem()] * 6,
        out_specs=[vmem(), vmem()],
        out_shape=[
            jax.ShapeDtypeStruct((nrows, width), bf16),
            jax.ShapeDtypeStruct(arrived.shape, bf16),
        ],
        scratch_shapes=[pltpu.VMEM((nrows + BLK, width), f32)],
        compiler_params=pltpu.CompilerParams(vmem_limit_bytes=48 * 1024 * 1024),
        cost_estimate=pl.CostEstimate(
            flops=2 * BLK * BLK * width * (3 * nrows // BLK + farw3.shape[0]),
            transcendentals=0,
            bytes_accessed=2 * width * (nrows * 2 + 2 * arrived.shape[0] * BLK),
        ),
    )(src, rows, send_rows, field, lo, hi, arrived, band3, farw3)


def hop2(src, rows, field, lo, hi, arrived, band3, farw3, features, hidden, mix3):
    nrows, width = field.shape
    return pl.pallas_call(
        hop2_kernel,
        in_specs=[smem(), smem()] + [vmem()] * 9,
        out_specs=vmem(),
        out_shape=jax.ShapeDtypeStruct((nrows, width), bf16),
        scratch_shapes=[pltpu.VMEM((nrows + BLK, width), f32)],
        compiler_params=pltpu.CompilerParams(vmem_limit_bytes=48 * 1024 * 1024),
        cost_estimate=pl.CostEstimate(
            flops=2 * BLK * BLK * width * (3 * nrows // BLK + farw3.shape[0])
            + 2 * nrows * width * CHUNK * 3,
            transcendentals=0,
            bytes_accessed=2 * width * (nrows * 6 + arrived.shape[0] * BLK),
        ),
    )(src, rows, field, lo, hi, arrived, band3, farw3, features, hidden, mix3)


def halo(field):
    count = lax.axis_size("node")
    forward = [(i, i + 1) for i in range(count - 1)]
    backward = [(t, s) for s, t in forward]
    lo = lax.ppermute(field[field.shape[0] - BLK :], "node", forward)
    hi = lax.ppermute(field[:BLK], "node", backward)
    return lo, hi


def local(
    features,
    filter_gate_weight,
    skip_weight,
    mix_weight,
    band_weight,
    far_weight,
    far_ptr,
    far_col,
    export_block,
):
    node_rows = features.shape[0]
    blocks = node_rows // BLK
    far_cap = far_col.shape[1]
    peer_count = far_cap + 1
    cw = CHANNEL_WIDTH
    per = CHUNK // cw

    eye = jnp.eye(per, dtype=bf16)
    fgw = filter_gate_weight
    wlo = jnp.concatenate([jnp.kron(eye, fgw[:cw, :cw]), jnp.kron(eye, fgw[:cw, cw:])], axis=1)
    whi = jnp.concatenate([jnp.kron(eye, fgw[cw:, :cw]), jnp.kron(eye, fgw[cw:, cw:])], axis=1)
    ws = jnp.kron(eye, skip_weight)
    mix3 = jnp.stack([jnp.kron(eye, mix_weight[i * cw : (i + 1) * cw]) for i in range(3)])

    hidden, skip_out = front(features, wlo, whi, ws)

    own_index = lax.axis_index("node")
    own_exports = lax.dynamic_slice_in_dim(export_block, own_index, 1, 0)[0]
    columns = far_col[0]
    sources = columns // EXPORT
    slot_export = columns % EXPORT
    pointers = far_ptr[0]
    slot_ids = jnp.arange(far_cap, dtype=jnp.int32)
    slot_rows = jnp.sum(
        (pointers[1:, None] <= slot_ids[None, :]).astype(jnp.int32), axis=0
    ).astype(jnp.int32)
    in_use = slot_ids < pointers[-1]
    matches = (sources[None, :] == jnp.arange(peer_count, dtype=jnp.int32)[:, None]) & in_use[
        None, :
    ]
    wanted = jnp.sum(jnp.where(matches, slot_export[None, :], 0), axis=1)
    requested = lax.all_to_all(wanted[:, None], "node", split_axis=0, concat_axis=0, tiled=True)[
        :, 0
    ]
    send_rows = own_exports[requested].astype(jnp.int32)

    width = hidden.shape[1]
    band3 = band_weight.reshape(node_rows, 3, BLK).transpose(1, 0, 2)
    farw3 = far_weight.reshape(BLK, far_cap, BLK).transpose(1, 0, 2)

    def exchange(send):
        return lax.all_to_all(send, "node", split_axis=0, concat_axis=0, tiled=True)

    send1 = hidden.reshape(blocks, BLK, width)[send_rows]
    arrived1 = exchange(send1)
    lo1, hi1 = halo(hidden)
    hop_one, send2 = hop1(sources, slot_rows, send_rows, hidden, lo1, hi1, arrived1, band3, farw3)
    arrived2 = exchange(send2)
    lo2, hi2 = halo(hop_one)
    residual = hop2(
        sources, slot_rows, hop_one, lo2, hi2, arrived2, band3, farw3, features, hidden, mix3
    )
    return residual, skip_out


def solution(mesh):
    placed = (
        P(("groups", "node"), None),
        P(),
        P(),
        P(),
        P("node", None),
        P(None, "node"),
        P("node", None),
        P("node", None),
        P(),
    )
    return jax.shard_map(
        local,
        mesh=mesh,
        in_specs=placed,
        out_specs=(P(("groups", "node"), None), P(("groups", "node"), None)),
        check_vma=False,
    )
```

```python
import jax
import jax.numpy as jnp
from jax import lax
from jax.experimental import pallas as pl
from jax.experimental.pallas import tpu as pltpu
from jax.sharding import PartitionSpec as P

BLK = 64
TOUT = 16
DILATION_STEP = 16
EXPORT = 2
CHANNEL_WIDTH = 32
S = 256
TIN = 32
CHUNK = 256
ROW_TILE = 256

f32 = jnp.float32
bf16 = jnp.bfloat16


def hidden_kernel(x_ref, wlo_ref, whi_ref, h_ref):
    half = x_ref.shape[1] // 2
    for j in range(half // CHUNK):
        x0 = x_ref[:, j * CHUNK : (j + 1) * CHUNK]
        x1 = x_ref[:, half + j * CHUNK : half + (j + 1) * CHUNK]
        pre = jnp.dot(x0, wlo_ref[...], preferred_element_type=f32)
        pre = pre + jnp.dot(x1, whi_ref[...], preferred_element_type=f32)
        h = (jnp.tanh(pre[:, :CHUNK]) * jax.nn.sigmoid(pre[:, CHUNK:])).astype(bf16)
        h_ref[:, j * CHUNK : (j + 1) * CHUNK] = h


def skip_kernel(h_ref, ws_ref, s_ref):
    skip_w = ws_ref.shape[1]
    for j in range(h_ref.shape[1] // CHUNK):
        s_ref[:, j * skip_w : (j + 1) * skip_w] = jnp.dot(
            h_ref[:, j * CHUNK : (j + 1) * CHUNK], ws_ref[...], preferred_element_type=f32
        ).astype(bf16)


def front_hidden(features, wlo, whi):
    rows, cols = features.shape
    half = cols // 2
    tile = min(ROW_TILE, rows)
    return pl.pallas_call(
        hidden_kernel,
        grid=(rows // tile,),
        in_specs=[
            pl.BlockSpec((tile, cols), lambda i: (i, 0)),
            pl.BlockSpec(wlo.shape, lambda i: (0, 0)),
            pl.BlockSpec(whi.shape, lambda i: (0, 0)),
        ],
        out_specs=pl.BlockSpec((tile, half), lambda i: (i, 0)),
        out_shape=jax.ShapeDtypeStruct((rows, half), bf16),
        compiler_params=pltpu.CompilerParams(vmem_limit_bytes=48 * 1024 * 1024),
        cost_estimate=pl.CostEstimate(
            flops=2 * rows * CHUNK * 4 * CHUNK * (half // CHUNK),
            transcendentals=rows * half * 2,
            bytes_accessed=2 * rows * (cols + half),
        ),
    )(features, wlo, whi)


def front_skip(hidden, ws):
    rows, half = hidden.shape
    skip_cols = ws.shape[1] * (half // CHUNK)
    tile = min(ROW_TILE, rows)
    return pl.pallas_call(
        skip_kernel,
        grid=(rows // tile,),
        in_specs=[
            pl.BlockSpec((tile, half), lambda i: (i, 0)),
            pl.BlockSpec(ws.shape, lambda i: (0, 0)),
        ],
        out_specs=pl.BlockSpec((tile, skip_cols), lambda i: (i, 0)),
        out_shape=jax.ShapeDtypeStruct((rows, skip_cols), bf16),
        compiler_params=pltpu.CompilerParams(vmem_limit_bytes=48 * 1024 * 1024),
        cost_estimate=pl.CostEstimate(
            flops=2 * rows * CHUNK * ws.shape[1] * (half // CHUNK),
            transcendentals=0,
            bytes_accessed=2 * rows * (half + skip_cols),
        ),
    )(hidden, ws)


def accumulate(src_ref, row_ref, field_ref, lo_ref, hi_ref, arr_ref, band_ref, farw_ref, acc):
    nblk = field_ref.shape[0] // BLK
    far_cap = farw_ref.shape[0]
    for r in range(nblk):
        prev = lo_ref[...] if r == 0 else field_ref[(r - 1) * BLK : r * BLK, :]
        nxt = hi_ref[...] if r == nblk - 1 else field_ref[(r + 1) * BLK : (r + 2) * BLK, :]
        own = field_ref[r * BLK : (r + 1) * BLK, :]
        v = jnp.dot(band_ref[0, r * BLK : (r + 1) * BLK, :], prev, preferred_element_type=f32)
        v = v + jnp.dot(band_ref[1, r * BLK : (r + 1) * BLK, :], own, preferred_element_type=f32)
        v = v + jnp.dot(band_ref[2, r * BLK : (r + 1) * BLK, :], nxt, preferred_element_type=f32)
        acc[r * BLK : (r + 1) * BLK, :] = v
    acc[nblk * BLK :, :] = jnp.zeros((BLK, acc.shape[1]), f32)

    def slot(k, carry):
        row = row_ref[k]
        piece = arr_ref[src_ref[k]]
        start = pl.multiple_of(row * BLK, BLK)
        acc[pl.ds(start, BLK), :] += jnp.dot(farw_ref[k], piece, preferred_element_type=f32)
        return carry

    lax.fori_loop(0, far_cap, slot, 0)


def hop1_kernel(
    src_ref, row_ref, send_ref, field_ref, lo_ref, hi_ref, arr_ref, band_ref, farw_ref,
    out_ref, out_send_ref, acc,
):
    accumulate(src_ref, row_ref, field_ref, lo_ref, hi_ref, arr_ref, band_ref, farw_ref, acc)
    nrows = field_ref.shape[0]
    out_ref[...] = acc[:nrows, :].astype(bf16)
    for p in range(out_send_ref.shape[0]):
        start = pl.multiple_of(send_ref[p] * BLK, BLK)
        out_send_ref[p] = out_ref[pl.ds(start, BLK), :]


def hop2_kernel(
    src_ref, row_ref, field_ref, lo_ref, hi_ref, arr_ref, band_ref, farw_ref,
    x_ref, h_ref, mix_ref, out_ref, acc,
):
    accumulate(src_ref, row_ref, field_ref, lo_ref, hi_ref, arr_ref, band_ref, farw_ref, acc)
    nrows, width = field_ref.shape
    half = x_ref.shape[1] // 2
    for j in range(width // CHUNK):
        cols = slice(j * CHUNK, (j + 1) * CHUNK)
        two = acc[:nrows, cols].astype(bf16)
        v = x_ref[:, half + j * CHUNK : half + (j + 1) * CHUNK].astype(f32)
        v = v + jnp.dot(h_ref[:, cols], mix_ref[0], preferred_element_type=f32)
        v = v + jnp.dot(field_ref[:, cols], mix_ref[1], preferred_element_type=f32)
        v = v + jnp.dot(two, mix_ref[2], preferred_element_type=f32)
        out_ref[:, cols] = v.astype(bf16)


def vmem():
    return pl.BlockSpec(memory_space=pltpu.VMEM)


def smem():
    return pl.BlockSpec(memory_space=pltpu.SMEM)


def hop1(src, rows, send_rows, field, lo, hi, arrived, band3, farw3):
    nrows, width = field.shape
    return pl.pallas_call(
        hop1_kernel,
        in_specs=[smem(), smem(), smem()] + [vmem()] * 6,
        out_specs=[vmem(), vmem()],
        out_shape=[
            jax.ShapeDtypeStruct((nrows, width), bf16),
            jax.ShapeDtypeStruct((send_rows.shape[0], BLK, width), bf16),
        ],
        scratch_shapes=[pltpu.VMEM((nrows + BLK, width), f32)],
        compiler_params=pltpu.CompilerParams(vmem_limit_bytes=48 * 1024 * 1024),
        cost_estimate=pl.CostEstimate(
            flops=2 * BLK * BLK * width * (3 * nrows // BLK + farw3.shape[0]),
            transcendentals=0,
            bytes_accessed=2 * width * (nrows * 2 + arrived.shape[0] * BLK),
        ),
    )(src, rows, send_rows, field, lo, hi, arrived, band3, farw3)


def hop2(src, rows, field, lo, hi, arrived, band3, farw3, features, hidden, mix3):
    nrows, width = field.shape
    return pl.pallas_call(
        hop2_kernel,
        in_specs=[smem(), smem()] + [vmem()] * 9,
        out_specs=vmem(),
        out_shape=jax.ShapeDtypeStruct((nrows, width), bf16),
        scratch_shapes=[pltpu.VMEM((nrows + BLK, width), f32)],
        compiler_params=pltpu.CompilerParams(vmem_limit_bytes=48 * 1024 * 1024),
        cost_estimate=pl.CostEstimate(
            flops=2 * BLK * BLK * width * (3 * nrows // BLK + farw3.shape[0])
            + 2 * nrows * width * CHUNK * 3,
            transcendentals=0,
            bytes_accessed=2 * width * (nrows * 6 + arrived.shape[0] * BLK),
        ),
    )(src, rows, field, lo, hi, arrived, band3, farw3, features, hidden, mix3)


def halo(field):
    count = lax.axis_size("node")
    forward = [(i, i + 1) for i in range(count - 1)]
    backward = [(t, s) for s, t in forward]
    lo = lax.ppermute(field[field.shape[0] - BLK :], "node", forward)
    hi = lax.ppermute(field[:BLK], "node", backward)
    return lo, hi


def local(
    features,
    filter_gate_weight,
    skip_weight,
    mix_weight,
    band_weight,
    far_weight,
    far_ptr,
    far_col,
    export_block,
):
    node_rows = features.shape[0]
    blocks = node_rows // BLK
    far_cap = far_col.shape[1]
    peer_count = far_cap + 1
    cw = CHANNEL_WIDTH
    per = CHUNK // cw

    def block_diag(w, reps):
        r, c = w.shape
        tiled = jnp.tile(w, (reps, reps))
        ri = lax.broadcasted_iota(jnp.int32, tiled.shape, 0) // r
        ci = lax.broadcasted_iota(jnp.int32, tiled.shape, 1) // c
        return jnp.where(ri == ci, tiled, jnp.zeros_like(tiled))

    fgw = filter_gate_weight
    wlo = jnp.concatenate([block_diag(fgw[:cw, :cw], per), block_diag(fgw[:cw, cw:], per)], axis=1)
    whi = jnp.concatenate([block_diag(fgw[cw:, :cw], per), block_diag(fgw[cw:, cw:], per)], axis=1)
    ws = block_diag(skip_weight, per)
    mix3 = jnp.stack([block_diag(mix_weight[i * cw : (i + 1) * cw], per) for i in range(3)])

    hidden = front_hidden(features, wlo, whi)

    own_index = lax.axis_index("node")
    own_exports = lax.dynamic_slice_in_dim(export_block, own_index, 1, 0)[0].astype(jnp.int32)
    columns = far_col[0].astype(jnp.int32)
    pointers = far_ptr[0]
    slot_ids = jnp.arange(far_cap, dtype=jnp.int32)
    slot_rows = jnp.sum(
        (pointers[1:, None] <= slot_ids[None, :]).astype(jnp.int32), axis=0
    ).astype(jnp.int32)

    width = hidden.shape[1]
    band3 = band_weight.reshape(node_rows, 3, BLK).transpose(1, 0, 2)
    farw3 = far_weight.reshape(BLK, far_cap, BLK).transpose(1, 0, 2)

    def exchange(send):
        gathered = lax.all_gather(send, "node", axis=0, tiled=True)
        return gathered

    send1 = hidden.reshape(blocks, BLK, width)[own_exports]
    arrived1 = exchange(send1)
    lo1, hi1 = halo(hidden)
    skip_out = front_skip(hidden, ws)
    hop_one, send2 = hop1(columns, slot_rows, own_exports, hidden, lo1, hi1, arrived1, band3, farw3)
    arrived2 = exchange(send2)
    lo2, hi2 = halo(hop_one)
    residual = hop2(
        columns, slot_rows, hop_one, lo2, hi2, arrived2, band3, farw3, features, hidden, mix3
    )
    return residual, skip_out


def solution(mesh):
    placed = (
        P(("groups", "node"), None),
        P(),
        P(),
        P(),
        P("node", None),
        P(None, "node"),
        P("node", None),
        P("node", None),
        P(),
    )
    return jax.shard_map(
        local,
        mesh=mesh,
        in_specs=placed,
        out_specs=(P(("groups", "node"), None), P(("groups", "node"), None)),
        check_vma=False,
    )
```

```python
import functools

import jax
import jax.numpy as jnp
from jax import lax
from jax.experimental import pallas as pl
from jax.experimental.pallas import tpu as pltpu
from jax.sharding import PartitionSpec as P

BLK = 64
TOUT = 16
DILATION_STEP = 16
EXPORT = 2
CHANNEL_WIDTH = 32
S = 256
TIN = 32
CHUNK = 256
ROW_TILE = 256

f32 = jnp.float32
bf16 = jnp.bfloat16


def hidden_kernel(x_ref, wlo_ref, whi_ref, h_ref):
    half = x_ref.shape[1] // 2
    for j in range(half // CHUNK):
        x0 = x_ref[:, j * CHUNK : (j + 1) * CHUNK]
        x1 = x_ref[:, half + j * CHUNK : half + (j + 1) * CHUNK]
        pre = jnp.dot(x0, wlo_ref[...], preferred_element_type=f32)
        pre = pre + jnp.dot(x1, whi_ref[...], preferred_element_type=f32)
        h_ref[j] = (jnp.tanh(pre[:, :CHUNK]) * jax.nn.sigmoid(pre[:, CHUNK:])).astype(bf16)


def skip_kernel(h_ref, ws_ref, s_ref):
    skip_w = ws_ref.shape[1]
    for j in range(h_ref.shape[0]):
        s_ref[:, j * skip_w : (j + 1) * skip_w] = jnp.dot(
            h_ref[j], ws_ref[...], preferred_element_type=f32
        ).astype(bf16)


def front_hidden(features, wlo, whi):
    rows, cols = features.shape
    chunks = cols // 2 // CHUNK
    tile = min(ROW_TILE, rows)
    return pl.pallas_call(
        hidden_kernel,
        grid=(rows // tile,),
        in_specs=[
            pl.BlockSpec((tile, cols), lambda i: (i, 0)),
            pl.BlockSpec(wlo.shape, lambda i: (0, 0)),
            pl.BlockSpec(whi.shape, lambda i: (0, 0)),
        ],
        out_specs=pl.BlockSpec((chunks, tile, CHUNK), lambda i: (0, i, 0)),
        out_shape=jax.ShapeDtypeStruct((chunks, rows, CHUNK), bf16),
        compiler_params=pltpu.CompilerParams(vmem_limit_bytes=48 * 1024 * 1024),
        cost_estimate=pl.CostEstimate(
            flops=2 * rows * CHUNK * 4 * CHUNK * chunks,
            transcendentals=rows * CHUNK * chunks * 2,
            bytes_accessed=2 * rows * (cols + CHUNK * chunks),
        ),
    )(features, wlo, whi)


def front_skip(hidden, ws):
    chunks, rows, _ = hidden.shape
    skip_cols = ws.shape[1] * chunks
    tile = min(ROW_TILE, rows)
    return pl.pallas_call(
        skip_kernel,
        grid=(rows // tile,),
        in_specs=[
            pl.BlockSpec((chunks, tile, CHUNK), lambda i: (0, i, 0)),
            pl.BlockSpec(ws.shape, lambda i: (0, 0)),
        ],
        out_specs=pl.BlockSpec((tile, skip_cols), lambda i: (i, 0)),
        out_shape=jax.ShapeDtypeStruct((rows, skip_cols), bf16),
        compiler_params=pltpu.CompilerParams(vmem_limit_bytes=48 * 1024 * 1024),
        cost_estimate=pl.CostEstimate(
            flops=2 * rows * CHUNK * ws.shape[1] * chunks,
            transcendentals=0,
            bytes_accessed=2 * rows * (CHUNK * chunks + skip_cols),
        ),
    )(hidden, ws)


def accumulate(src_ref, row_ref, field, lo_ref, hi_ref, arr_ref, band_ref, farw_ref, acc):
    nblk = field.shape[0] // BLK
    far_cap = farw_ref.shape[0]
    for r in range(nblk):
        prev = lo_ref[...] if r == 0 else field[(r - 1) * BLK : r * BLK, :]
        nxt = hi_ref[...] if r == nblk - 1 else field[(r + 1) * BLK : (r + 2) * BLK, :]
        own = field[r * BLK : (r + 1) * BLK, :]
        v = jnp.dot(band_ref[0, r * BLK : (r + 1) * BLK, :], prev, preferred_element_type=f32)
        v = v + jnp.dot(band_ref[1, r * BLK : (r + 1) * BLK, :], own, preferred_element_type=f32)
        v = v + jnp.dot(band_ref[2, r * BLK : (r + 1) * BLK, :], nxt, preferred_element_type=f32)
        acc[r * BLK : (r + 1) * BLK, :] = v
    acc[nblk * BLK :, :] = jnp.zeros((BLK, acc.shape[1]), f32)

    def slot(k, carry):
        row = row_ref[k]
        piece = arr_ref[src_ref[k]]
        start = pl.multiple_of(row * BLK, BLK)
        acc[pl.ds(start, BLK), :] += jnp.dot(farw_ref[k], piece, preferred_element_type=f32)
        return carry

    lax.fori_loop(0, far_cap, slot, 0)


def hop1_kernel(
    chunk, src_ref, row_ref, send_ref, field_ref, lo_ref, hi_ref, arr_ref, band_ref, farw_ref,
    out_ref, out_send_ref, acc,
):
    field = field_ref.at[chunk]
    accumulate(src_ref, row_ref, field, lo_ref, hi_ref, arr_ref, band_ref, farw_ref, acc)
    nrows = field.shape[0]
    out_ref[...] = acc[:nrows, :].astype(bf16)
    for p in range(out_send_ref.shape[0]):
        start = pl.multiple_of(send_ref[p] * BLK, BLK)
        out_send_ref[p] = out_ref[pl.ds(start, BLK), :]


def hop2_kernel(
    chunk, src_ref, row_ref, field_ref, lo_ref, hi_ref, arr_ref, band_ref, farw_ref,
    x_ref, h_ref, mix_ref, out_ref, acc,
):
    accumulate(src_ref, row_ref, field_ref, lo_ref, hi_ref, arr_ref, band_ref, farw_ref, acc)
    nrows = field_ref.shape[0]
    half = x_ref.shape[1] // 2
    two = acc[:nrows, :].astype(bf16)
    v = x_ref[:, half + chunk * CHUNK : half + (chunk + 1) * CHUNK].astype(f32)
    v = v + jnp.dot(h_ref[chunk], mix_ref[0], preferred_element_type=f32)
    v = v + jnp.dot(field_ref[...], mix_ref[1], preferred_element_type=f32)
    v = v + jnp.dot(two, mix_ref[2], preferred_element_type=f32)
    out_ref[...] = v.astype(bf16)


def vmem():
    return pl.BlockSpec(memory_space=pltpu.VMEM)


def smem():
    return pl.BlockSpec(memory_space=pltpu.SMEM)


def hop1(chunk, src, rows, send_rows, hidden, lo, hi, arrived, band3, farw3):
    _, nrows, width = hidden.shape
    return pl.pallas_call(
        functools.partial(hop1_kernel, chunk),
        in_specs=[smem(), smem(), smem()] + [vmem()] * 6,
        out_specs=[vmem(), vmem()],
        out_shape=[
            jax.ShapeDtypeStruct((nrows, width), bf16),
            jax.ShapeDtypeStruct((send_rows.shape[0], BLK, width), bf16),
        ],
        scratch_shapes=[pltpu.VMEM((nrows + BLK, width), f32)],
        compiler_params=pltpu.CompilerParams(vmem_limit_bytes=48 * 1024 * 1024),
        cost_estimate=pl.CostEstimate(
            flops=2 * BLK * BLK * width * (3 * nrows // BLK + farw3.shape[0]),
            transcendentals=0,
            bytes_accessed=2 * width * (nrows * 2 + 2 * arrived.shape[0] * BLK),
        ),
    )(src, rows, send_rows, hidden, lo, hi, arrived, band3, farw3)


def hop2(chunk, src, rows, field, lo, hi, arrived, band3, farw3, features, hidden, mix3):
    nrows, width = field.shape
    return pl.pallas_call(
        functools.partial(hop2_kernel, chunk),
        in_specs=[smem(), smem()] + [vmem()] * 9,
        out_specs=vmem(),
        out_shape=jax.ShapeDtypeStruct((nrows, width), bf16),
        scratch_shapes=[pltpu.VMEM((nrows + BLK, width), f32)],
        compiler_params=pltpu.CompilerParams(vmem_limit_bytes=48 * 1024 * 1024),
        cost_estimate=pl.CostEstimate(
            flops=2 * BLK * BLK * width * (3 * nrows // BLK + farw3.shape[0])
            + 2 * nrows * width * CHUNK * 3,
            transcendentals=0,
            bytes_accessed=2 * width * (nrows * 5 + arrived.shape[0] * BLK),
        ),
    )(src, rows, field, lo, hi, arrived, band3, farw3, features, hidden, mix3)


def halo(field):
    count = lax.axis_size("node")
    forward = [(i, i + 1) for i in range(count - 1)]
    backward = [(t, s) for s, t in forward]
    lo = lax.ppermute(field[field.shape[0] - BLK :], "node", forward)
    hi = lax.ppermute(field[:BLK], "node", backward)
    return lo, hi


def block_diag(w, reps):
    r, c = w.shape
    shape_r = (reps * r, r)
    rep_r = (
        lax.broadcasted_iota(jnp.int32, shape_r, 0) % r == lax.broadcasted_iota(jnp.int32, shape_r, 1)
    ).astype(bf16)
    shape_c = (c, reps * c)
    rep_c = (
        lax.broadcasted_iota(jnp.int32, shape_c, 1) % c == lax.broadcasted_iota(jnp.int32, shape_c, 0)
    ).astype(bf16)
    rows = jnp.dot(rep_r, w, preferred_element_type=f32).astype(bf16)
    tiled = jnp.dot(rows, rep_c, preferred_element_type=f32)
    shape = tiled.shape
    mask = lax.broadcasted_iota(jnp.int32, shape, 0) // r == lax.broadcasted_iota(jnp.int32, shape, 1) // c
    return jnp.where(mask, tiled, 0.0).astype(bf16)


def local(
    features,
    filter_gate_weight,
    skip_weight,
    mix_weight,
    band_weight,
    far_weight,
    far_ptr,
    far_col,
    export_block,
):
    node_rows = features.shape[0]
    blocks = node_rows // BLK
    far_cap = far_col.shape[1]
    cw = CHANNEL_WIDTH
    per = CHUNK // cw

    fgw = filter_gate_weight
    wlo = jnp.concatenate([block_diag(fgw[:cw, :cw], per), block_diag(fgw[:cw, cw:], per)], axis=1)
    whi = jnp.concatenate([block_diag(fgw[cw:, :cw], per), block_diag(fgw[cw:, cw:], per)], axis=1)
    ws = block_diag(skip_weight, per)
    mix3 = jnp.stack([block_diag(mix_weight[i * cw : (i + 1) * cw], per) for i in range(3)])

    own_index = lax.axis_index("node")
    own_exports = lax.dynamic_slice_in_dim(export_block, own_index, 1, 0)[0].astype(jnp.int32)
    columns = far_col[0].astype(jnp.int32)
    sources = columns // EXPORT
    pointers = far_ptr[0].astype(jnp.int32)
    slot_ids = jnp.arange(far_cap, dtype=jnp.int32)
    slot_rows = jnp.sum(
        (pointers[1:, None] <= slot_ids[None, :]).astype(jnp.int32), axis=0
    ).astype(jnp.int32)
    info = jnp.concatenate([columns, pointers[-1:]])
    info_all = lax.all_gather(info, "node", axis=0)
    cols_all = info_all[:, :far_cap]
    used_all = info_all[:, far_cap]
    hits = (cols_all // EXPORT == own_index) & (slot_ids[None, :] < used_all[:, None])
    requested = jnp.sum(jnp.where(hits, cols_all % EXPORT, 0), axis=1)
    send_rows = own_exports[requested].astype(jnp.int32)

    hidden = front_hidden(features, wlo, whi)
    chunks, _, width = hidden.shape
    band3 = band_weight.reshape(node_rows, 3, BLK).transpose(1, 0, 2)
    farw3 = far_weight.reshape(BLK, far_cap, BLK).transpose(1, 0, 2)

    def exchange(send):
        return lax.all_to_all(send, "node", split_axis=0, concat_axis=0, tiled=True)

    arrived1 = [exchange(hidden[c].reshape(blocks, BLK, width)[send_rows]) for c in range(chunks)]
    halos1 = [halo(hidden[c]) for c in range(chunks)]
    skip_out = front_skip(hidden, ws)
    parts = []
    for c in range(chunks):
        lo1, hi1 = halos1[c]
        hop_one, send2 = hop1(c, sources, slot_rows, send_rows, hidden, lo1, hi1, arrived1[c], band3, farw3)
        arrived2 = exchange(send2)
        lo2, hi2 = halo(hop_one)
        parts.append(
            hop2(c, sources, slot_rows, hop_one, lo2, hi2, arrived2, band3, farw3, features, hidden, mix3)
        )
    residual = jnp.concatenate(parts, axis=1)
    return residual, skip_out


def solution(mesh):
    placed = (
        P(("groups", "node"), None),
        P(),
        P(),
        P(),
        P("node", None),
        P(None, "node"),
        P("node", None),
        P("node", None),
        P(),
    )
    return jax.shard_map(
        local,
        mesh=mesh,
        in_specs=placed,
        out_specs=(P(("groups", "node"), None), P(("groups", "node"), None)),
        check_vma=False,
    )
```

```python
import functools

import jax
import jax.numpy as jnp
from jax import lax
from jax.experimental import pallas as pl
from jax.experimental.pallas import tpu as pltpu
from jax.sharding import PartitionSpec as P

BLK = 64
TOUT = 16
DILATION_STEP = 16
EXPORT = 2
CHANNEL_WIDTH = 32
S = 256
TIN = 32
CHUNK = 256
ROW_TILE = 256

f32 = jnp.float32
bf16 = jnp.bfloat16


def bd_inkernel(w, reps):
    r, c = w.shape
    shape_r = (reps * r, r)
    rep_r = jnp.where(
        lax.broadcasted_iota(jnp.int32, shape_r, 0) % r == lax.broadcasted_iota(jnp.int32, shape_r, 1),
        1.0, 0.0,
    ).astype(bf16)
    shape_c = (c, reps * c)
    rep_c = jnp.where(
        lax.broadcasted_iota(jnp.int32, shape_c, 1) % c == lax.broadcasted_iota(jnp.int32, shape_c, 0),
        1.0, 0.0,
    ).astype(bf16)
    rows = jnp.dot(rep_r, w, preferred_element_type=f32).astype(bf16)
    tiled = jnp.dot(rows, rep_c, preferred_element_type=f32)
    shape = tiled.shape
    mask = lax.broadcasted_iota(jnp.int32, shape, 0) // r == lax.broadcasted_iota(jnp.int32, shape, 1) // c
    return jnp.where(mask, tiled, 0.0).astype(bf16)


def hidden_kernel(x_ref, fgw_ref, h_ref, wlo, whi):
    half = x_ref.shape[1] // 2
    cw = fgw_ref.shape[0] // 2
    per = CHUNK // cw

    @pl.when(pl.program_id(0) == 0)
    def _():
        w = fgw_ref[...]
        wlo[:, :CHUNK] = bd_inkernel(w[:cw, :cw], per)
        wlo[:, CHUNK:] = bd_inkernel(w[:cw, cw:], per)
        whi[:, :CHUNK] = bd_inkernel(w[cw:, :cw], per)
        whi[:, CHUNK:] = bd_inkernel(w[cw:, cw:], per)

    for j in range(half // CHUNK):
        x0 = x_ref[:, j * CHUNK : (j + 1) * CHUNK]
        x1 = x_ref[:, half + j * CHUNK : half + (j + 1) * CHUNK]
        pre = jnp.dot(x0, wlo[...], preferred_element_type=f32)
        pre = pre + jnp.dot(x1, whi[...], preferred_element_type=f32)
        h_ref[:, j * CHUNK : (j + 1) * CHUNK] = (
            jnp.tanh(pre[:, :CHUNK]) * jax.nn.sigmoid(pre[:, CHUNK:])
        ).astype(bf16)


def skip_kernel(h_ref, sw_ref, s_ref, ws):
    cw = sw_ref.shape[0]

    @pl.when(pl.program_id(0) == 0)
    def _():
        ws[...] = bd_inkernel(sw_ref[...], CHUNK // cw)

    skip_w = ws.shape[1]
    for j in range(h_ref.shape[1] // CHUNK):
        s_ref[:, j * skip_w : (j + 1) * skip_w] = jnp.dot(
            h_ref[:, j * CHUNK : (j + 1) * CHUNK], ws[...], preferred_element_type=f32
        ).astype(bf16)


def front_hidden(features, fgw):
    rows, cols = features.shape
    chunks = cols // 2 // CHUNK
    tile = min(ROW_TILE, rows)
    return pl.pallas_call(
        hidden_kernel,
        grid=(rows // tile,),
        in_specs=[
            pl.BlockSpec((tile, cols), lambda i: (i, 0)),
            pl.BlockSpec(fgw.shape, lambda i: (0, 0)),
        ],
        out_specs=pl.BlockSpec((tile, chunks * CHUNK), lambda i: (i, 0)),
        out_shape=jax.ShapeDtypeStruct((rows, chunks * CHUNK), bf16),
        scratch_shapes=[pltpu.VMEM((CHUNK, 2 * CHUNK), bf16), pltpu.VMEM((CHUNK, 2 * CHUNK), bf16)],
        compiler_params=pltpu.CompilerParams(vmem_limit_bytes=48 * 1024 * 1024),
        cost_estimate=pl.CostEstimate(
            flops=2 * rows * CHUNK * 4 * CHUNK * chunks,
            transcendentals=rows * CHUNK * chunks * 2,
            bytes_accessed=2 * rows * (cols + CHUNK * chunks),
        ),
    )(features, fgw)


def front_skip(hidden, skip_weight):
    rows, width = hidden.shape
    chunks = width // CHUNK
    cw, s = skip_weight.shape
    per = CHUNK // cw
    skip_cols = s * per * chunks
    tile = min(ROW_TILE, rows)
    return pl.pallas_call(
        skip_kernel,
        grid=(rows // tile,),
        in_specs=[
            pl.BlockSpec((tile, width), lambda i: (i, 0)),
            pl.BlockSpec(skip_weight.shape, lambda i: (0, 0)),
        ],
        out_specs=pl.BlockSpec((tile, skip_cols), lambda i: (i, 0)),
        out_shape=jax.ShapeDtypeStruct((rows, skip_cols), bf16),
        scratch_shapes=[pltpu.VMEM((CHUNK, s * per), bf16)],
        compiler_params=pltpu.CompilerParams(vmem_limit_bytes=48 * 1024 * 1024),
        cost_estimate=pl.CostEstimate(
            flops=2 * rows * CHUNK * s * per * chunks,
            transcendentals=0,
            bytes_accessed=2 * rows * (CHUNK * chunks + skip_cols),
        ),
    )(hidden, skip_weight)


def accumulate(src_ref, row_ref, field, lo_ref, hi_ref, arr_ref, band_ref, farw_ref, acc):
    nblk = field.shape[0] // BLK
    far_cap = farw_ref.shape[0]
    for r in range(nblk):
        prev = lo_ref[...] if r == 0 else field[(r - 1) * BLK : r * BLK, :]
        nxt = hi_ref[...] if r == nblk - 1 else field[(r + 1) * BLK : (r + 2) * BLK, :]
        own = field[r * BLK : (r + 1) * BLK, :]
        v = jnp.dot(band_ref[0, r * BLK : (r + 1) * BLK, :], prev, preferred_element_type=f32)
        v = v + jnp.dot(band_ref[1, r * BLK : (r + 1) * BLK, :], own, preferred_element_type=f32)
        v = v + jnp.dot(band_ref[2, r * BLK : (r + 1) * BLK, :], nxt, preferred_element_type=f32)
        acc[r * BLK : (r + 1) * BLK, :] = v
    acc[nblk * BLK :, :] = jnp.zeros((BLK, acc.shape[1]), f32)

    def slot(k, carry):
        row = row_ref[k]
        piece = arr_ref[src_ref[k]]
        start = pl.multiple_of(row * BLK, BLK)
        acc[pl.ds(start, BLK), :] += jnp.dot(farw_ref[k], piece, preferred_element_type=f32)
        return carry

    lax.fori_loop(0, far_cap, slot, 0)


def hop1_kernel(
    src_ref, row_ref, send_ref, field_ref, lo_ref, hi_ref, arr_ref, band_ref, farw_ref,
    out_ref, out_send_ref, acc,
):
    accumulate(src_ref, row_ref, field_ref, lo_ref, hi_ref, arr_ref, band_ref, farw_ref, acc)
    nrows = field_ref.shape[0]
    out_ref[...] = acc[:nrows, :].astype(bf16)
    for p in range(out_send_ref.shape[0]):
        start = pl.multiple_of(send_ref[p] * BLK, BLK)
        out_send_ref[p] = out_ref[pl.ds(start, BLK), :]


def hop2_kernel(
    src_ref, row_ref, field_ref, lo_ref, hi_ref, arr_ref, band_ref, farw_ref,
    x_ref, h_ref, mix_ref, out_ref, acc,
):
    accumulate(src_ref, row_ref, field_ref, lo_ref, hi_ref, arr_ref, band_ref, farw_ref, acc)
    nrows, width = field_ref.shape
    half = x_ref.shape[1] // 2
    cw = mix_ref.shape[1]
    per = CHUNK // cw
    mix = mix_ref[...]
    m = [bd_inkernel(mix[i * cw : (i + 1) * cw], per) for i in range(3)]
    for j in range(width // CHUNK):
        cols = slice(j * CHUNK, (j + 1) * CHUNK)
        two = acc[:nrows, cols].astype(bf16)
        v = x_ref[:, half + j * CHUNK : half + (j + 1) * CHUNK].astype(f32)
        v = v + jnp.dot(h_ref[:, cols], m[0], preferred_element_type=f32)
        v = v + jnp.dot(field_ref[:, cols], m[1], preferred_element_type=f32)
        v = v + jnp.dot(two, m[2], preferred_element_type=f32)
        out_ref[:, cols] = v.astype(bf16)


def vmem():
    return pl.BlockSpec(memory_space=pltpu.VMEM)


def smem():
    return pl.BlockSpec(memory_space=pltpu.SMEM)


def hop1(src, rows, send_rows, field, lo, hi, arrived, band3, farw3):
    nrows, width = field.shape
    return pl.pallas_call(
        hop1_kernel,
        in_specs=[smem(), smem(), smem()] + [vmem()] * 6,
        out_specs=[vmem(), vmem()],
        out_shape=[
            jax.ShapeDtypeStruct((nrows, width), bf16),
            jax.ShapeDtypeStruct(arrived.shape, bf16),
        ],
        scratch_shapes=[pltpu.VMEM((nrows + BLK, width), f32)],
        compiler_params=pltpu.CompilerParams(vmem_limit_bytes=48 * 1024 * 1024),
        cost_estimate=pl.CostEstimate(
            flops=2 * BLK * BLK * width * (3 * nrows // BLK + farw3.shape[0]),
            transcendentals=0,
            bytes_accessed=2 * width * (nrows * 2 + 2 * arrived.shape[0] * BLK),
        ),
    )(src, rows, send_rows, field, lo, hi, arrived, band3, farw3)


def hop2(src, rows, field, lo, hi, arrived, band3, farw3, features, hidden, mix):
    nrows, width = field.shape
    return pl.pallas_call(
        hop2_kernel,
        in_specs=[smem(), smem()] + [vmem()] * 9,
        out_specs=vmem(),
        out_shape=jax.ShapeDtypeStruct((nrows, width), bf16),
        scratch_shapes=[pltpu.VMEM((nrows + BLK, width), f32)],
        compiler_params=pltpu.CompilerParams(vmem_limit_bytes=48 * 1024 * 1024),
        cost_estimate=pl.CostEstimate(
            flops=2 * BLK * BLK * width * (3 * nrows // BLK + farw3.shape[0])
            + 2 * nrows * width * CHUNK * 3,
            transcendentals=0,
            bytes_accessed=2 * width * (nrows * 6 + arrived.shape[0] * BLK),
        ),
    )(src, rows, field, lo, hi, arrived, band3, farw3, features, hidden, mix)


def halo(field):
    count = lax.axis_size("node")
    forward = [(i, i + 1) for i in range(count - 1)]
    backward = [(t, s) for s, t in forward]
    lo = lax.ppermute(field[field.shape[0] - BLK :], "node", forward)
    hi = lax.ppermute(field[:BLK], "node", backward)
    return lo, hi


def local(
    features,
    filter_gate_weight,
    skip_weight,
    mix_weight,
    band_weight,
    far_weight,
    far_ptr,
    far_col,
    export_block,
):
    node_rows = features.shape[0]
    blocks = node_rows // BLK
    far_cap = far_col.shape[1]

    own_index = lax.axis_index("node")
    own_exports = lax.dynamic_slice_in_dim(export_block, own_index, 1, 0)[0].astype(jnp.int32)
    columns = far_col[0].astype(jnp.int32)
    sources = columns // EXPORT
    pointers = far_ptr[0].astype(jnp.int32)
    slot_ids = jnp.arange(far_cap, dtype=jnp.int32)
    slot_rows = jnp.sum(
        (pointers[1:, None] <= slot_ids[None, :]).astype(jnp.int32), axis=0
    ).astype(jnp.int32)
    info = jnp.concatenate([columns, pointers[-1:]]).astype(f32)
    info_all = lax.all_gather(info, "node", axis=0).astype(jnp.int32)
    cols_all = info_all[:, :far_cap]
    used_all = info_all[:, far_cap]
    hits = (cols_all // EXPORT == own_index) & (slot_ids[None, :] < used_all[:, None])
    requested = jnp.sum(jnp.where(hits, cols_all % EXPORT, 0), axis=1)
    send_rows = own_exports[requested].astype(jnp.int32)

    hidden = front_hidden(features, filter_gate_weight)
    width = hidden.shape[1]
    band3 = band_weight.reshape(node_rows, 3, BLK).transpose(1, 0, 2)
    farw3 = far_weight.reshape(BLK, far_cap, BLK).transpose(1, 0, 2)

    def exchange(send):
        return lax.all_to_all(send, "node", split_axis=0, concat_axis=0, tiled=True)

    arrived1 = exchange(hidden.reshape(blocks, BLK, width)[send_rows])
    lo1, hi1 = halo(hidden)
    skip_out = front_skip(hidden, skip_weight)
    hop_one, send2 = hop1(sources, slot_rows, send_rows, hidden, lo1, hi1, arrived1, band3, farw3)
    arrived2 = exchange(send2)
    lo2, hi2 = halo(hop_one)
    residual = hop2(
        sources, slot_rows, hop_one, lo2, hi2, arrived2, band3, farw3, features, hidden, mix_weight
    )
    return residual, skip_out


def solution(mesh):
    placed = (
        P(("groups", "node"), None),
        P(),
        P(),
        P(),
        P("node", None),
        P(None, "node"),
        P("node", None),
        P("node", None),
        P(),
    )
    return jax.shard_map(
        local,
        mesh=mesh,
        in_specs=placed,
        out_specs=(P(("groups", "node"), None), P(("groups", "node"), None)),
        check_vma=False,
    )
```

```python
import functools

import jax
import jax.numpy as jnp
from jax import lax
from jax.experimental import pallas as pl
from jax.experimental.pallas import tpu as pltpu
from jax.sharding import PartitionSpec as P

BLK = 64
TOUT = 16
DILATION_STEP = 16
EXPORT = 2
CHANNEL_WIDTH = 32
S = 256
TIN = 32
CHUNK = 256
ROW_TILE = 256

f32 = jnp.float32
bf16 = jnp.bfloat16


def bd_inkernel(w, reps):
    r, c = w.shape
    shape_r = (reps * r, r)
    rep_r = jnp.where(
        lax.broadcasted_iota(jnp.int32, shape_r, 0) % r == lax.broadcasted_iota(jnp.int32, shape_r, 1),
        1.0, 0.0,
    ).astype(bf16)
    shape_c = (c, reps * c)
    rep_c = jnp.where(
        lax.broadcasted_iota(jnp.int32, shape_c, 1) % c == lax.broadcasted_iota(jnp.int32, shape_c, 0),
        1.0, 0.0,
    ).astype(bf16)
    rows = jnp.dot(rep_r, w, preferred_element_type=f32).astype(bf16)
    tiled = jnp.dot(rows, rep_c, preferred_element_type=f32)
    shape = tiled.shape
    mask = lax.broadcasted_iota(jnp.int32, shape, 0) // r == lax.broadcasted_iota(jnp.int32, shape, 1) // c
    return jnp.where(mask, tiled, 0.0).astype(bf16)


def hidden_kernel(x_ref, fgw_ref, h_ref, wlo, whi):
    half = x_ref.shape[1] // 2
    cw = fgw_ref.shape[0] // 2
    per = CHUNK // cw

    @pl.when(pl.program_id(0) == 0)
    def _():
        w = fgw_ref[...]
        wlo[:, :CHUNK] = bd_inkernel(w[:cw, :cw], per)
        wlo[:, CHUNK:] = bd_inkernel(w[:cw, cw:], per)
        whi[:, :CHUNK] = bd_inkernel(w[cw:, :cw], per)
        whi[:, CHUNK:] = bd_inkernel(w[cw:, cw:], per)

    for j in range(half // CHUNK):
        x0 = x_ref[:, j * CHUNK : (j + 1) * CHUNK]
        x1 = x_ref[:, half + j * CHUNK : half + (j + 1) * CHUNK]
        pre = jnp.dot(x0, wlo[...], preferred_element_type=f32)
        pre = pre + jnp.dot(x1, whi[...], preferred_element_type=f32)
        h_ref[:, j * CHUNK : (j + 1) * CHUNK] = (
            jnp.tanh(pre[:, :CHUNK]) * jax.nn.sigmoid(pre[:, CHUNK:])
        ).astype(bf16)


def skip_kernel(h_ref, sw_ref, s_ref, ws):
    cw = sw_ref.shape[0]

    @pl.when(pl.program_id(0) == 0)
    def _():
        ws[...] = bd_inkernel(sw_ref[...], CHUNK // cw)

    skip_w = ws.shape[1]
    for j in range(h_ref.shape[1] // CHUNK):
        s_ref[:, j * skip_w : (j + 1) * skip_w] = jnp.dot(
            h_ref[:, j * CHUNK : (j + 1) * CHUNK], ws[...], preferred_element_type=f32
        ).astype(bf16)


def front_hidden(features, fgw):
    rows, cols = features.shape
    chunks = cols // 2 // CHUNK
    tile = min(ROW_TILE, rows)
    return pl.pallas_call(
        hidden_kernel,
        grid=(rows // tile,),
        in_specs=[
            pl.BlockSpec((tile, cols), lambda i: (i, 0)),
            pl.BlockSpec(fgw.shape, lambda i: (0, 0)),
        ],
        out_specs=pl.BlockSpec((tile, chunks * CHUNK), lambda i: (i, 0)),
        out_shape=jax.ShapeDtypeStruct((rows, chunks * CHUNK), bf16),
        scratch_shapes=[pltpu.VMEM((CHUNK, 2 * CHUNK), bf16), pltpu.VMEM((CHUNK, 2 * CHUNK), bf16)],
        compiler_params=pltpu.CompilerParams(vmem_limit_bytes=48 * 1024 * 1024),
        cost_estimate=pl.CostEstimate(
            flops=2 * rows * CHUNK * 4 * CHUNK * chunks,
            transcendentals=rows * CHUNK * chunks * 2,
            bytes_accessed=2 * rows * (cols + CHUNK * chunks),
        ),
    )(features, fgw)


def front_skip(hidden, skip_weight):
    rows, width = hidden.shape
    chunks = width // CHUNK
    cw, s = skip_weight.shape
    per = CHUNK // cw
    skip_cols = s * per * chunks
    tile = min(ROW_TILE, rows)
    return pl.pallas_call(
        skip_kernel,
        grid=(rows // tile,),
        in_specs=[
            pl.BlockSpec((tile, width), lambda i: (i, 0)),
            pl.BlockSpec(skip_weight.shape, lambda i: (0, 0)),
        ],
        out_specs=pl.BlockSpec((tile, skip_cols), lambda i: (i, 0)),
        out_shape=jax.ShapeDtypeStruct((rows, skip_cols), bf16),
        scratch_shapes=[pltpu.VMEM((CHUNK, s * per), bf16)],
        compiler_params=pltpu.CompilerParams(vmem_limit_bytes=48 * 1024 * 1024),
        cost_estimate=pl.CostEstimate(
            flops=2 * rows * CHUNK * s * per * chunks,
            transcendentals=0,
            bytes_accessed=2 * rows * (CHUNK * chunks + skip_cols),
        ),
    )(hidden, skip_weight)


def accumulate(src_ref, row_ref, field, lo_ref, hi_ref, arr_ref, band_ref, farw_ref, acc):
    nblk = field.shape[0] // BLK
    far_cap = farw_ref.shape[0]
    for r in range(nblk):
        prev = lo_ref[...] if r == 0 else field[(r - 1) * BLK : r * BLK, :]
        nxt = hi_ref[...] if r == nblk - 1 else field[(r + 1) * BLK : (r + 2) * BLK, :]
        own = field[r * BLK : (r + 1) * BLK, :]
        v = jnp.dot(band_ref[0, r * BLK : (r + 1) * BLK, :], prev, preferred_element_type=f32)
        v = v + jnp.dot(band_ref[1, r * BLK : (r + 1) * BLK, :], own, preferred_element_type=f32)
        v = v + jnp.dot(band_ref[2, r * BLK : (r + 1) * BLK, :], nxt, preferred_element_type=f32)
        acc[r * BLK : (r + 1) * BLK, :] = v
    acc[nblk * BLK :, :] = jnp.zeros((BLK, acc.shape[1]), f32)

    def slot(k, carry):
        row = row_ref[k]
        piece = arr_ref[src_ref[k]]
        start = pl.multiple_of(row * BLK, BLK)
        acc[pl.ds(start, BLK), :] += jnp.dot(farw_ref[k], piece, preferred_element_type=f32)
        return carry

    lax.fori_loop(0, far_cap, slot, 0)


def hop1_kernel(
    src_ref, row_ref, send_ref, field_ref, lo_ref, hi_ref, arr_ref, band_ref, farw_ref,
    out_ref, out_send_ref, acc,
):
    accumulate(src_ref, row_ref, field_ref, lo_ref, hi_ref, arr_ref, band_ref, farw_ref, acc)
    nrows = field_ref.shape[0]
    out_ref[...] = acc[:nrows, :].astype(bf16)
    for p in range(out_send_ref.shape[0]):
        start = pl.multiple_of(send_ref[p] * BLK, BLK)
        out_send_ref[p] = out_ref[pl.ds(start, BLK), :]


def hop2_kernel(
    src_ref, row_ref, field_ref, lo_ref, hi_ref, arr_ref, band_ref, farw_ref,
    x_ref, h_ref, mix_ref, out_ref, acc,
):
    accumulate(src_ref, row_ref, field_ref, lo_ref, hi_ref, arr_ref, band_ref, farw_ref, acc)
    nrows, width = field_ref.shape
    half = x_ref.shape[1] // 2
    cw = mix_ref.shape[1]
    per = CHUNK // cw
    mix = mix_ref[...]
    m = [bd_inkernel(mix[i * cw : (i + 1) * cw], per) for i in range(3)]
    for j in range(width // CHUNK):
        cols = slice(j * CHUNK, (j + 1) * CHUNK)
        two = acc[:nrows, cols].astype(bf16)
        v = x_ref[:, half + j * CHUNK : half + (j + 1) * CHUNK].astype(f32)
        v = v + jnp.dot(h_ref[:, cols], m[0], preferred_element_type=f32)
        v = v + jnp.dot(field_ref[:, cols], m[1], preferred_element_type=f32)
        v = v + jnp.dot(two, m[2], preferred_element_type=f32)
        out_ref[:, cols] = v.astype(bf16)


def vmem():
    return pl.BlockSpec(memory_space=pltpu.VMEM)


def smem():
    return pl.BlockSpec(memory_space=pltpu.SMEM)


def hop1(src, rows, send_rows, field, lo, hi, arrived, band3, farw3):
    nrows, width = field.shape
    return pl.pallas_call(
        hop1_kernel,
        in_specs=[smem(), smem(), smem()] + [vmem()] * 6,
        out_specs=[vmem(), vmem()],
        out_shape=[
            jax.ShapeDtypeStruct((nrows, width), bf16),
            jax.ShapeDtypeStruct(arrived.shape, bf16),
        ],
        scratch_shapes=[pltpu.VMEM((nrows + BLK, width), f32)],
        compiler_params=pltpu.CompilerParams(vmem_limit_bytes=48 * 1024 * 1024),
        cost_estimate=pl.CostEstimate(
            flops=2 * BLK * BLK * width * (3 * nrows // BLK + farw3.shape[0]),
            transcendentals=0,
            bytes_accessed=2 * width * (nrows * 2 + 2 * arrived.shape[0] * BLK),
        ),
    )(src, rows, send_rows, field, lo, hi, arrived, band3, farw3)


def hop2(src, rows, field, lo, hi, arrived, band3, farw3, features, hidden, mix):
    nrows, width = field.shape
    return pl.pallas_call(
        hop2_kernel,
        in_specs=[smem(), smem()] + [vmem()] * 9,
        out_specs=vmem(),
        out_shape=jax.ShapeDtypeStruct((nrows, width), bf16),
        scratch_shapes=[pltpu.VMEM((nrows + BLK, width), f32)],
        compiler_params=pltpu.CompilerParams(vmem_limit_bytes=48 * 1024 * 1024),
        cost_estimate=pl.CostEstimate(
            flops=2 * BLK * BLK * width * (3 * nrows // BLK + farw3.shape[0])
            + 2 * nrows * width * CHUNK * 3,
            transcendentals=0,
            bytes_accessed=2 * width * (nrows * 6 + arrived.shape[0] * BLK),
        ),
    )(src, rows, field, lo, hi, arrived, band3, farw3, features, hidden, mix)


def halo(field):
    count = lax.axis_size("node")
    forward = [(i, i + 1) for i in range(count - 1)]
    backward = [(t, s) for s, t in forward]
    lo = lax.ppermute(field[field.shape[0] - BLK :], "node", forward)
    hi = lax.ppermute(field[:BLK], "node", backward)
    return lo, hi


def local(
    features,
    filter_gate_weight,
    skip_weight,
    mix_weight,
    band_weight,
    far_weight,
    far_ptr,
    far_col,
    export_block,
):
    node_rows = features.shape[0]
    blocks = node_rows // BLK
    far_cap = far_col.shape[1]

    own_index = lax.axis_index("node")
    own_exports = lax.dynamic_slice_in_dim(export_block, own_index, 1, 0)[0].astype(jnp.int32)
    columns = far_col[0].astype(jnp.int32)
    sources = columns // EXPORT
    pointers = far_ptr[0].astype(jnp.int32)
    slot_ids = jnp.arange(far_cap, dtype=jnp.int32)
    slot_rows = jnp.sum(
        (pointers[1:, None] <= slot_ids[None, :]).astype(jnp.int32), axis=0
    ).astype(jnp.int32)
    slot_export = columns % EXPORT
    in_use = slot_ids < pointers[-1]
    peers = jnp.arange(far_col.shape[1] + 1, dtype=jnp.int32)
    matches = (sources[None, :] == peers[:, None]) & in_use[None, :]
    wanted = jnp.sum(jnp.where(matches, slot_export[None, :], 0), axis=1)
    requested = lax.all_to_all(wanted[:, None], "node", split_axis=0, concat_axis=0, tiled=True)[
        :, 0
    ]
    send_rows = own_exports[requested].astype(jnp.int32)

    hidden = front_hidden(features, filter_gate_weight)
    width = hidden.shape[1]
    band3 = band_weight.reshape(node_rows, 3, BLK).transpose(1, 0, 2)
    farw3 = far_weight.reshape(BLK, far_cap, BLK).transpose(1, 0, 2)

    def exchange(send):
        return lax.all_to_all(send, "node", split_axis=0, concat_axis=0, tiled=True)

    arrived1 = exchange(hidden.reshape(blocks, BLK, width)[send_rows])
    lo1, hi1 = halo(hidden)
    skip_out = front_skip(hidden, skip_weight)
    hop_one, send2 = hop1(sources, slot_rows, send_rows, hidden, lo1, hi1, arrived1, band3, farw3)
    arrived2 = exchange(send2)
    lo2, hi2 = halo(hop_one)
    residual = hop2(
        sources, slot_rows, hop_one, lo2, hi2, arrived2, band3, farw3, features, hidden, mix_weight
    )
    return residual, skip_out


def solution(mesh):
    placed = (
        P(("groups", "node"), None),
        P(),
        P(),
        P(),
        P("node", None),
        P(None, "node"),
        P("node", None),
        P("node", None),
        P(),
    )
    return jax.shard_map(
        local,
        mesh=mesh,
        in_specs=placed,
        out_specs=(P(("groups", "node"), None), P(("groups", "node"), None)),
        check_vma=False,
    )
```

```python
import functools

import jax
import jax.numpy as jnp
from jax import lax
from jax.experimental import pallas as pl
from jax.experimental.pallas import tpu as pltpu
from jax.sharding import PartitionSpec as P

BLK = 64
TOUT = 16
DILATION_STEP = 16
EXPORT = 2
CHANNEL_WIDTH = 32
S = 256
TIN = 32
CHUNK = 256
ROW_TILE = 256

f32 = jnp.float32
bf16 = jnp.bfloat16


def vmem():
    return pl.BlockSpec(memory_space=pltpu.VMEM)


def smem():
    return pl.BlockSpec(memory_space=pltpu.SMEM)


def bd_inkernel(w, reps):
    r, c = w.shape
    shape_r = (reps * r, r)
    rep_r = jnp.where(
        lax.broadcasted_iota(jnp.int32, shape_r, 0) % r == lax.broadcasted_iota(jnp.int32, shape_r, 1),
        1.0, 0.0,
    ).astype(bf16)
    shape_c = (c, reps * c)
    rep_c = jnp.where(
        lax.broadcasted_iota(jnp.int32, shape_c, 1) % c == lax.broadcasted_iota(jnp.int32, shape_c, 0),
        1.0, 0.0,
    ).astype(bf16)
    rows = jnp.dot(rep_r, w, preferred_element_type=f32).astype(bf16)
    tiled = jnp.dot(rows, rep_c, preferred_element_type=f32)
    shape = tiled.shape
    mask = lax.broadcasted_iota(jnp.int32, shape, 0) // r == lax.broadcasted_iota(jnp.int32, shape, 1) // c
    return jnp.where(mask, tiled, 0.0).astype(bf16)


def send_row(req_ref, exp_ref, p):
    own = lax.axis_index("node")
    return exp_ref[own, req_ref[p]]


def write_send(req_ref, exp_ref, field_ref, send_ref):
    def body(p, carry):
        start = pl.multiple_of(send_row(req_ref, exp_ref, p) * BLK, BLK)
        send_ref[p] = field_ref[pl.ds(start, BLK), :]
        return carry

    lax.fori_loop(0, send_ref.shape[0], body, 0)


def hidden_kernel(req_ref, exp_ref, x_ref, fgw_ref, h_ref, send_ref):
    rows, cols = x_ref.shape
    half = cols // 2
    cw = fgw_ref.shape[0] // 2
    per = CHUNK // cw
    w = fgw_ref[...]
    wlo = jnp.concatenate([bd_inkernel(w[:cw, :cw], per), bd_inkernel(w[:cw, cw:], per)], axis=1)
    whi = jnp.concatenate([bd_inkernel(w[cw:, :cw], per), bd_inkernel(w[cw:, cw:], per)], axis=1)
    tile = min(ROW_TILE, rows)
    for t in range(rows // tile):
        rs = slice(t * tile, (t + 1) * tile)
        for j in range(half // CHUNK):
            x0 = x_ref[rs, j * CHUNK : (j + 1) * CHUNK]
            x1 = x_ref[rs, half + j * CHUNK : half + (j + 1) * CHUNK]
            pre = jnp.dot(x0, wlo, preferred_element_type=f32)
            pre = pre + jnp.dot(x1, whi, preferred_element_type=f32)
            h_ref[rs, j * CHUNK : (j + 1) * CHUNK] = (
                jnp.tanh(pre[:, :CHUNK]) * jax.nn.sigmoid(pre[:, CHUNK:])
            ).astype(bf16)
    write_send(req_ref, exp_ref, h_ref, send_ref)


def prep_kernel(col_ref, ptr_ref, out_ref):
    far_cap = col_ref.shape[1]
    used = ptr_ref[0, ptr_ref.shape[1] - 1]

    def clear(p, carry):
        out_ref[p] = 0
        return carry

    lax.fori_loop(0, out_ref.shape[0], clear, 0)

    def body(k, carry):
        col = col_ref[0, k]

        @pl.when(k < used)
        def _():
            out_ref[col // EXPORT] = col % EXPORT

        return carry

    lax.fori_loop(0, far_cap, body, 0)


def prep(far_col, far_ptr):
    return pl.pallas_call(
        prep_kernel,
        in_specs=[smem(), smem()],
        out_specs=smem(),
        out_shape=jax.ShapeDtypeStruct((far_col.shape[1] + 1,), jnp.int32),
    )(far_col, far_ptr)


def skip_kernel(h_ref, sw_ref, s_ref, ws):
    cw = sw_ref.shape[0]

    @pl.when(pl.program_id(0) == 0)
    def _():
        ws[...] = bd_inkernel(sw_ref[...], CHUNK // cw)

    skip_w = ws.shape[1]
    for j in range(h_ref.shape[1] // CHUNK):
        s_ref[:, j * skip_w : (j + 1) * skip_w] = jnp.dot(
            h_ref[:, j * CHUNK : (j + 1) * CHUNK], ws[...], preferred_element_type=f32
        ).astype(bf16)


def front_hidden(requested, export_block, features, fgw):
    rows, cols = features.shape
    half = cols // 2
    peers = requested.shape[0]
    return pl.pallas_call(
        hidden_kernel,
        in_specs=[smem(), smem(), vmem(), vmem()],
        out_specs=[vmem(), vmem()],
        out_shape=[
            jax.ShapeDtypeStruct((rows, half), bf16),
            jax.ShapeDtypeStruct((peers, BLK, half), bf16),
        ],
        compiler_params=pltpu.CompilerParams(vmem_limit_bytes=48 * 1024 * 1024),
        cost_estimate=pl.CostEstimate(
            flops=2 * rows * CHUNK * 4 * CHUNK * (half // CHUNK),
            transcendentals=rows * half * 2,
            bytes_accessed=2 * rows * (cols + 2 * half),
        ),
    )(requested, export_block, features, fgw)


def front_skip(hidden, skip_weight):
    rows, width = hidden.shape
    chunks = width // CHUNK
    cw, s = skip_weight.shape
    per = CHUNK // cw
    skip_cols = s * per * chunks
    tile = min(ROW_TILE, rows)
    return pl.pallas_call(
        skip_kernel,
        grid=(rows // tile,),
        in_specs=[
            pl.BlockSpec((tile, width), lambda i: (i, 0)),
            pl.BlockSpec(skip_weight.shape, lambda i: (0, 0)),
        ],
        out_specs=pl.BlockSpec((tile, skip_cols), lambda i: (i, 0)),
        out_shape=jax.ShapeDtypeStruct((rows, skip_cols), bf16),
        scratch_shapes=[pltpu.VMEM((CHUNK, s * per), bf16)],
        compiler_params=pltpu.CompilerParams(vmem_limit_bytes=48 * 1024 * 1024),
        cost_estimate=pl.CostEstimate(
            flops=2 * rows * CHUNK * s * per * chunks,
            transcendentals=0,
            bytes_accessed=2 * rows * (CHUNK * chunks + skip_cols),
        ),
    )(hidden, skip_weight)


def accumulate(col_ref, ptr_ref, field, lo_ref, hi_ref, arr_ref, band_ref, farw_ref, acc):
    nblk = field.shape[0] // BLK
    far_cap = farw_ref.shape[0]
    for r in range(nblk):
        prev = lo_ref[...] if r == 0 else field[(r - 1) * BLK : r * BLK, :]
        nxt = hi_ref[...] if r == nblk - 1 else field[(r + 1) * BLK : (r + 2) * BLK, :]
        own = field[r * BLK : (r + 1) * BLK, :]
        v = jnp.dot(band_ref[0, r * BLK : (r + 1) * BLK, :], prev, preferred_element_type=f32)
        v = v + jnp.dot(band_ref[1, r * BLK : (r + 1) * BLK, :], own, preferred_element_type=f32)
        v = v + jnp.dot(band_ref[2, r * BLK : (r + 1) * BLK, :], nxt, preferred_element_type=f32)
        acc[r * BLK : (r + 1) * BLK, :] = v
    acc[nblk * BLK :, :] = jnp.zeros((BLK, acc.shape[1]), f32)

    nptr = ptr_ref.shape[1]

    def slot(k, carry):
        row = 0
        for r in range(1, nptr):
            row = row + jnp.where(ptr_ref[0, r] <= k, 1, 0)
        piece = arr_ref[col_ref[0, k] // EXPORT]
        start = pl.multiple_of(row * BLK, BLK)
        acc[pl.ds(start, BLK), :] += jnp.dot(farw_ref[k], piece, preferred_element_type=f32)
        return carry

    lax.fori_loop(0, far_cap, slot, 0)


def hop1_kernel(
    col_ref, ptr_ref, req_ref, exp_ref, field_ref, lo_ref, hi_ref, arr_ref, band_ref, farw_ref,
    out_ref, out_send_ref, acc,
):
    accumulate(col_ref, ptr_ref, field_ref, lo_ref, hi_ref, arr_ref, band_ref, farw_ref, acc)
    nrows = field_ref.shape[0]
    out_ref[...] = acc[:nrows, :].astype(bf16)
    write_send(req_ref, exp_ref, out_ref, out_send_ref)


def hop2_kernel(
    col_ref, ptr_ref, field_ref, lo_ref, hi_ref, arr_ref, band_ref, farw_ref,
    x_ref, h_ref, mix_ref, out_ref, acc,
):
    accumulate(col_ref, ptr_ref, field_ref, lo_ref, hi_ref, arr_ref, band_ref, farw_ref, acc)
    nrows, width = field_ref.shape
    half = x_ref.shape[1] // 2
    cw = mix_ref.shape[1]
    per = CHUNK // cw
    mix = mix_ref[...]
    m = [bd_inkernel(mix[i * cw : (i + 1) * cw], per) for i in range(3)]
    for j in range(width // CHUNK):
        cols = slice(j * CHUNK, (j + 1) * CHUNK)
        two = acc[:nrows, cols].astype(bf16)
        v = x_ref[:, half + j * CHUNK : half + (j + 1) * CHUNK].astype(f32)
        v = v + jnp.dot(h_ref[:, cols], m[0], preferred_element_type=f32)
        v = v + jnp.dot(field_ref[:, cols], m[1], preferred_element_type=f32)
        v = v + jnp.dot(two, m[2], preferred_element_type=f32)
        out_ref[:, cols] = v.astype(bf16)


def hop1(far_col, far_ptr, requested, export_block, field, lo, hi, arrived, band3, farw3):
    nrows, width = field.shape
    return pl.pallas_call(
        hop1_kernel,
        in_specs=[smem(), smem(), smem(), smem()] + [vmem()] * 6,
        out_specs=[vmem(), vmem()],
        out_shape=[
            jax.ShapeDtypeStruct((nrows, width), bf16),
            jax.ShapeDtypeStruct(arrived.shape, bf16),
        ],
        scratch_shapes=[pltpu.VMEM((nrows + BLK, width), f32)],
        compiler_params=pltpu.CompilerParams(vmem_limit_bytes=48 * 1024 * 1024),
        cost_estimate=pl.CostEstimate(
            flops=2 * BLK * BLK * width * (3 * nrows // BLK + farw3.shape[0]),
            transcendentals=0,
            bytes_accessed=2 * width * (nrows * 2 + 2 * arrived.shape[0] * BLK),
        ),
    )(far_col, far_ptr, requested, export_block, field, lo, hi, arrived, band3, farw3)


def hop2(far_col, far_ptr, field, lo, hi, arrived, band3, farw3, features, hidden, mix):
    nrows, width = field.shape
    return pl.pallas_call(
        hop2_kernel,
        in_specs=[smem(), smem()] + [vmem()] * 9,
        out_specs=vmem(),
        out_shape=jax.ShapeDtypeStruct((nrows, width), bf16),
        scratch_shapes=[pltpu.VMEM((nrows + BLK, width), f32)],
        compiler_params=pltpu.CompilerParams(vmem_limit_bytes=48 * 1024 * 1024),
        cost_estimate=pl.CostEstimate(
            flops=2 * BLK * BLK * width * (3 * nrows // BLK + farw3.shape[0])
            + 2 * nrows * width * CHUNK * 3,
            transcendentals=0,
            bytes_accessed=2 * width * (nrows * 6 + arrived.shape[0] * BLK),
        ),
    )(far_col, far_ptr, field, lo, hi, arrived, band3, farw3, features, hidden, mix)


def halo(field):
    count = lax.axis_size("node")
    forward = [(i, i + 1) for i in range(count - 1)]
    backward = [(t, s) for s, t in forward]
    lo = lax.ppermute(field[field.shape[0] - BLK :], "node", forward)
    hi = lax.ppermute(field[:BLK], "node", backward)
    return lo, hi


def local(
    features,
    filter_gate_weight,
    skip_weight,
    mix_weight,
    band_weight,
    far_weight,
    far_ptr,
    far_col,
    export_block,
):
    node_rows = features.shape[0]
    blocks = node_rows // BLK
    far_cap = far_col.shape[1]

    wanted = prep(far_col, far_ptr)
    requested = lax.all_to_all(wanted[:, None], "node", split_axis=0, concat_axis=0, tiled=True)[
        :, 0
    ]
    hidden, send1 = front_hidden(requested, export_block, features, filter_gate_weight)
    width = hidden.shape[1]
    band3 = band_weight.reshape(node_rows, 3, BLK).transpose(1, 0, 2)
    farw3 = far_weight.reshape(BLK, far_cap, BLK).transpose(1, 0, 2)

    def exchange(send):
        return lax.all_to_all(send, "node", split_axis=0, concat_axis=0, tiled=True)

    arrived1 = exchange(send1)
    lo1, hi1 = halo(hidden)
    skip_out = front_skip(hidden, skip_weight)
    hop_one, send2 = hop1(far_col, far_ptr, requested, export_block, hidden, lo1, hi1, arrived1, band3, farw3)
    arrived2 = exchange(send2)
    lo2, hi2 = halo(hop_one)
    residual = hop2(
        far_col, far_ptr, hop_one, lo2, hi2, arrived2, band3, farw3, features, hidden, mix_weight
    )
    return residual, skip_out


def solution(mesh):
    placed = (
        P(("groups", "node"), None),
        P(),
        P(),
        P(),
        P("node", None),
        P(None, "node"),
        P("node", None),
        P("node", None),
        P(),
    )
    return jax.shard_map(
        local,
        mesh=mesh,
        in_specs=placed,
        out_specs=(P(("groups", "node"), None), P(("groups", "node"), None)),
        check_vma=False,
    )
```

```python
import functools

import jax
import jax.numpy as jnp
from jax import lax
from jax.experimental import pallas as pl
from jax.experimental.pallas import tpu as pltpu
from jax.sharding import PartitionSpec as P

BLK = 64
TOUT = 16
DILATION_STEP = 16
EXPORT = 2
CHANNEL_WIDTH = 32
S = 256
TIN = 32
CHUNK = 256
ROW_TILE = 256

f32 = jnp.float32
bf16 = jnp.bfloat16


def vmem():
    return pl.BlockSpec(memory_space=pltpu.VMEM)


def smem():
    return pl.BlockSpec(memory_space=pltpu.SMEM)


def bd_inkernel(w, reps):
    r, c = w.shape
    shape_r = (reps * r, r)
    rep_r = jnp.where(
        lax.broadcasted_iota(jnp.int32, shape_r, 0) % r == lax.broadcasted_iota(jnp.int32, shape_r, 1),
        1.0, 0.0,
    ).astype(bf16)
    shape_c = (c, reps * c)
    rep_c = jnp.where(
        lax.broadcasted_iota(jnp.int32, shape_c, 1) % c == lax.broadcasted_iota(jnp.int32, shape_c, 0),
        1.0, 0.0,
    ).astype(bf16)
    rows = jnp.dot(rep_r, w, preferred_element_type=f32).astype(bf16)
    tiled = jnp.dot(rows, rep_c, preferred_element_type=f32)
    shape = tiled.shape
    mask = lax.broadcasted_iota(jnp.int32, shape, 0) // r == lax.broadcasted_iota(jnp.int32, shape, 1) // c
    return jnp.where(mask, tiled, 0.0).astype(bf16)


def send_row(req_ref, exp_ref, p):
    own = lax.axis_index("node")
    return exp_ref[own, req_ref[p]]


def write_send(req_ref, exp_ref, field_ref, send_ref):
    def body(p, carry):
        start = pl.multiple_of(send_row(req_ref, exp_ref, p) * BLK, BLK)
        send_ref[p] = field_ref[pl.ds(start, BLK), :]
        return carry

    lax.fori_loop(0, send_ref.shape[0], body, 0)


def hidden_kernel(x_ref, fgw_ref, h_ref):
    rows, cols = x_ref.shape
    half = cols // 2
    cw = fgw_ref.shape[0] // 2
    per = CHUNK // cw
    w = fgw_ref[...]
    wlo = jnp.concatenate([bd_inkernel(w[:cw, :cw], per), bd_inkernel(w[:cw, cw:], per)], axis=1)
    whi = jnp.concatenate([bd_inkernel(w[cw:, :cw], per), bd_inkernel(w[cw:, cw:], per)], axis=1)
    tile = min(ROW_TILE, rows)
    for t in range(rows // tile):
        rs = slice(t * tile, (t + 1) * tile)
        for j in range(half // CHUNK):
            x0 = x_ref[rs, j * CHUNK : (j + 1) * CHUNK]
            x1 = x_ref[rs, half + j * CHUNK : half + (j + 1) * CHUNK]
            pre = jnp.dot(x0, wlo, preferred_element_type=f32)
            pre = pre + jnp.dot(x1, whi, preferred_element_type=f32)
            h_ref[rs, j * CHUNK : (j + 1) * CHUNK] = (
                jnp.tanh(pre[:, :CHUNK]) * jax.nn.sigmoid(pre[:, CHUNK:])
            ).astype(bf16)


def pack_kernel(req_ref, exp_ref, field_ref, send_ref):
    write_send(req_ref, exp_ref, field_ref, send_ref)


def pack(requested, export_block, field):
    nrows, width = field.shape
    return pl.pallas_call(
        pack_kernel,
        in_specs=[smem(), smem(), vmem()],
        out_specs=vmem(),
        out_shape=jax.ShapeDtypeStruct((requested.shape[0], BLK, width), bf16),
    )(requested, export_block, field)


def prep_kernel(col_ref, ptr_ref, out_ref):
    far_cap = col_ref.shape[1]
    used = ptr_ref[0, ptr_ref.shape[1] - 1]

    def clear(p, carry):
        out_ref[p] = 0
        return carry

    lax.fori_loop(0, out_ref.shape[0], clear, 0)

    def body(k, carry):
        col = col_ref[0, k]

        @pl.when(k < used)
        def _():
            out_ref[col // EXPORT] = col % EXPORT

        return carry

    lax.fori_loop(0, far_cap, body, 0)


def prep(far_col, far_ptr):
    return pl.pallas_call(
        prep_kernel,
        in_specs=[smem(), smem()],
        out_specs=smem(),
        out_shape=jax.ShapeDtypeStruct((far_col.shape[1] + 1,), jnp.int32),
    )(far_col, far_ptr)


def skip_kernel(h_ref, sw_ref, s_ref, ws):
    cw = sw_ref.shape[0]

    @pl.when(pl.program_id(0) == 0)
    def _():
        ws[...] = bd_inkernel(sw_ref[...], CHUNK // cw)

    skip_w = ws.shape[1]
    for j in range(h_ref.shape[1] // CHUNK):
        s_ref[:, j * skip_w : (j + 1) * skip_w] = jnp.dot(
            h_ref[:, j * CHUNK : (j + 1) * CHUNK], ws[...], preferred_element_type=f32
        ).astype(bf16)


def front_hidden(features, fgw):
    rows, cols = features.shape
    half = cols // 2
    return pl.pallas_call(
        hidden_kernel,
        in_specs=[vmem(), vmem()],
        out_specs=vmem(),
        out_shape=jax.ShapeDtypeStruct((rows, half), bf16),
        compiler_params=pltpu.CompilerParams(vmem_limit_bytes=48 * 1024 * 1024),
        cost_estimate=pl.CostEstimate(
            flops=2 * rows * CHUNK * 4 * CHUNK * (half // CHUNK),
            transcendentals=rows * half * 2,
            bytes_accessed=2 * rows * (cols + half),
        ),
    )(features, fgw)


def front_skip(hidden, skip_weight):
    rows, width = hidden.shape
    chunks = width // CHUNK
    cw, s = skip_weight.shape
    per = CHUNK // cw
    skip_cols = s * per * chunks
    tile = min(ROW_TILE, rows)
    return pl.pallas_call(
        skip_kernel,
        grid=(rows // tile,),
        in_specs=[
            pl.BlockSpec((tile, width), lambda i: (i, 0)),
            pl.BlockSpec(skip_weight.shape, lambda i: (0, 0)),
        ],
        out_specs=pl.BlockSpec((tile, skip_cols), lambda i: (i, 0)),
        out_shape=jax.ShapeDtypeStruct((rows, skip_cols), bf16),
        scratch_shapes=[pltpu.VMEM((CHUNK, s * per), bf16)],
        compiler_params=pltpu.CompilerParams(vmem_limit_bytes=48 * 1024 * 1024),
        cost_estimate=pl.CostEstimate(
            flops=2 * rows * CHUNK * s * per * chunks,
            transcendentals=0,
            bytes_accessed=2 * rows * (CHUNK * chunks + skip_cols),
        ),
    )(hidden, skip_weight)


def band_terms(field_ref, lo_ref, hi_ref, band_ref, acc_ref):
    nblk = field_ref.shape[0] // BLK
    for r in range(nblk):
        prev = lo_ref[...] if r == 0 else field_ref[(r - 1) * BLK : r * BLK, :]
        nxt = hi_ref[...] if r == nblk - 1 else field_ref[(r + 1) * BLK : (r + 2) * BLK, :]
        own = field_ref[r * BLK : (r + 1) * BLK, :]
        v = jnp.dot(band_ref[0, r * BLK : (r + 1) * BLK, :], prev, preferred_element_type=f32)
        v = v + jnp.dot(band_ref[1, r * BLK : (r + 1) * BLK, :], own, preferred_element_type=f32)
        v = v + jnp.dot(band_ref[2, r * BLK : (r + 1) * BLK, :], nxt, preferred_element_type=f32)
        acc_ref[r * BLK : (r + 1) * BLK, :] = v
    acc_ref[nblk * BLK :, :] = jnp.zeros((BLK, acc_ref.shape[1]), f32)


def far_terms(col_ref, ptr_ref, arr_ref, farw_ref, acc):
    far_cap = farw_ref.shape[0]
    nptr = ptr_ref.shape[1]

    def slot(k, carry):
        row = 0
        for r in range(1, nptr):
            row = row + jnp.where(ptr_ref[0, r] <= k, 1, 0)
        piece = arr_ref[col_ref[0, k] // EXPORT]
        start = pl.multiple_of(row * BLK, BLK)
        acc[pl.ds(start, BLK), :] += jnp.dot(farw_ref[k], piece, preferred_element_type=f32)
        return carry

    lax.fori_loop(0, far_cap, slot, 0)


def band1_kernel(field_ref, lo_ref, hi_ref, band_ref, acc_ref):
    band_terms(field_ref, lo_ref, hi_ref, band_ref, acc_ref)


def band2_kernel(field_ref, lo_ref, hi_ref, band_ref, x_ref, h_ref, mix_ref, acc_ref, part_ref):
    band_terms(field_ref, lo_ref, hi_ref, band_ref, acc_ref)
    width = field_ref.shape[1]
    half = x_ref.shape[1] // 2
    cw = mix_ref.shape[1]
    per = CHUNK // cw
    mix = mix_ref[...]
    m0 = bd_inkernel(mix[:cw], per)
    m1 = bd_inkernel(mix[cw : 2 * cw], per)
    for j in range(width // CHUNK):
        cols = slice(j * CHUNK, (j + 1) * CHUNK)
        v = x_ref[:, half + j * CHUNK : half + (j + 1) * CHUNK].astype(f32)
        v = v + jnp.dot(h_ref[:, cols], m0, preferred_element_type=f32)
        v = v + jnp.dot(field_ref[:, cols], m1, preferred_element_type=f32)
        part_ref[:, cols] = v


def far1_kernel(col_ref, ptr_ref, req_ref, exp_ref, acc_in, arr_ref, farw_ref, out_ref, send_ref, acc):
    acc[...] = acc_in[...]
    far_terms(col_ref, ptr_ref, arr_ref, farw_ref, acc)
    nrows = out_ref.shape[0]
    out_ref[...] = acc[:nrows, :].astype(bf16)
    write_send(req_ref, exp_ref, out_ref, send_ref)


def far2_kernel(col_ref, ptr_ref, acc_in, arr_ref, farw_ref, part_ref, mix_ref, out_ref, acc):
    acc[...] = acc_in[...]
    far_terms(col_ref, ptr_ref, arr_ref, farw_ref, acc)
    nrows, width = out_ref.shape
    cw = mix_ref.shape[1]
    m2 = bd_inkernel(mix_ref[2 * cw :], CHUNK // cw)
    for j in range(width // CHUNK):
        cols = slice(j * CHUNK, (j + 1) * CHUNK)
        two = acc[:nrows, cols].astype(bf16)
        v = part_ref[:, cols] + jnp.dot(two, m2, preferred_element_type=f32)
        out_ref[:, cols] = v.astype(bf16)


BIG_VMEM = pltpu.CompilerParams(vmem_limit_bytes=48 * 1024 * 1024)


def band1(field, lo, hi, band3):
    nrows, width = field.shape
    return pl.pallas_call(
        band1_kernel,
        in_specs=[vmem()] * 4,
        out_specs=vmem(),
        out_shape=jax.ShapeDtypeStruct((nrows + BLK, width), f32),
        compiler_params=BIG_VMEM,
        cost_estimate=pl.CostEstimate(
            flops=2 * BLK * width * 3 * nrows, transcendentals=0,
            bytes_accessed=2 * width * nrows * 3,
        ),
    )(field, lo, hi, band3)


def band2(field, lo, hi, band3, features, hidden, mix):
    nrows, width = field.shape
    return pl.pallas_call(
        band2_kernel,
        in_specs=[vmem()] * 7,
        out_specs=[vmem(), vmem()],
        out_shape=[
            jax.ShapeDtypeStruct((nrows + BLK, width), f32),
            jax.ShapeDtypeStruct((nrows, width), f32),
        ],
        compiler_params=BIG_VMEM,
        cost_estimate=pl.CostEstimate(
            flops=2 * BLK * width * 3 * nrows + 2 * nrows * width * CHUNK * 2, transcendentals=0,
            bytes_accessed=2 * width * nrows * 8,
        ),
    )(field, lo, hi, band3, features, hidden, mix)


def far1(far_col, far_ptr, requested, export_block, acc, arrived, farw3):
    nrows = acc.shape[0] - BLK
    width = acc.shape[1]
    return pl.pallas_call(
        far1_kernel,
        in_specs=[smem()] * 4 + [vmem()] * 3,
        out_specs=[vmem(), vmem()],
        out_shape=[
            jax.ShapeDtypeStruct((nrows, width), bf16),
            jax.ShapeDtypeStruct(arrived.shape, bf16),
        ],
        scratch_shapes=[pltpu.VMEM(acc.shape, f32)],
        compiler_params=BIG_VMEM,
        cost_estimate=pl.CostEstimate(
            flops=2 * BLK * BLK * width * farw3.shape[0], transcendentals=0,
            bytes_accessed=2 * width * nrows * 4,
        ),
    )(far_col, far_ptr, requested, export_block, acc, arrived, farw3)


def far2(far_col, far_ptr, acc, arrived, farw3, part, mix):
    nrows, width = part.shape
    return pl.pallas_call(
        far2_kernel,
        in_specs=[smem()] * 2 + [vmem()] * 5,
        out_specs=vmem(),
        out_shape=jax.ShapeDtypeStruct((nrows, width), bf16),
        scratch_shapes=[pltpu.VMEM(acc.shape, f32)],
        compiler_params=BIG_VMEM,
        cost_estimate=pl.CostEstimate(
            flops=2 * BLK * BLK * width * farw3.shape[0] + 2 * nrows * width * CHUNK,
            transcendentals=0,
            bytes_accessed=2 * width * nrows * 6,
        ),
    )(far_col, far_ptr, acc, arrived, farw3, part, mix)


def halo(field):
    count = lax.axis_size("node")
    forward = [(i, i + 1) for i in range(count - 1)]
    backward = [(t, s) for s, t in forward]
    lo = lax.ppermute(field[field.shape[0] - BLK :], "node", forward)
    hi = lax.ppermute(field[:BLK], "node", backward)
    return lo, hi


def local(
    features,
    filter_gate_weight,
    skip_weight,
    mix_weight,
    band_weight,
    far_weight,
    far_ptr,
    far_col,
    export_block,
):
    node_rows = features.shape[0]
    far_cap = far_col.shape[1]

    wanted = prep(far_col, far_ptr)
    requested = lax.all_to_all(wanted[:, None], "node", split_axis=0, concat_axis=0, tiled=True)[
        :, 0
    ]
    hidden = front_hidden(features, filter_gate_weight)
    band3 = band_weight.reshape(node_rows, 3, BLK).transpose(1, 0, 2)
    farw3 = far_weight.reshape(BLK, far_cap, BLK).transpose(1, 0, 2)

    def exchange(send):
        return lax.all_to_all(send, "node", split_axis=0, concat_axis=0, tiled=True)

    arrived1 = exchange(pack(requested, export_block, hidden))
    lo1, hi1 = halo(hidden)
    acc1 = band1(hidden, lo1, hi1, band3)
    skip_out = front_skip(hidden, skip_weight)
    hop_one, send2 = far1(far_col, far_ptr, requested, export_block, acc1, arrived1, farw3)
    arrived2 = exchange(send2)
    lo2, hi2 = halo(hop_one)
    acc2, part = band2(hop_one, lo2, hi2, band3, features, hidden, mix_weight)
    residual = far2(far_col, far_ptr, acc2, arrived2, farw3, part, mix_weight)
    return residual, skip_out


def solution(mesh):
    placed = (
        P(("groups", "node"), None),
        P(),
        P(),
        P(),
        P("node", None),
        P(None, "node"),
        P("node", None),
        P("node", None),
        P(),
    )
    return jax.shard_map(
        local,
        mesh=mesh,
        in_specs=placed,
        out_specs=(P(("groups", "node"), None), P(("groups", "node"), None)),
        check_vma=False,
    )
```

```python
import functools

import jax
import jax.numpy as jnp
from jax import lax
from jax.experimental import pallas as pl
from jax.experimental.pallas import tpu as pltpu
from jax.sharding import PartitionSpec as P

BLK = 64
TOUT = 16
DILATION_STEP = 16
EXPORT = 2
CHANNEL_WIDTH = 32
S = 256
TIN = 32
CHUNK = 256
ROW_TILE = 256

f32 = jnp.float32
bf16 = jnp.bfloat16


def bd_inkernel(w, reps):
    r, c = w.shape
    shape_r = (reps * r, r)
    rep_r = jnp.where(
        lax.broadcasted_iota(jnp.int32, shape_r, 0) % r == lax.broadcasted_iota(jnp.int32, shape_r, 1),
        1.0, 0.0,
    ).astype(bf16)
    shape_c = (c, reps * c)
    rep_c = jnp.where(
        lax.broadcasted_iota(jnp.int32, shape_c, 1) % c == lax.broadcasted_iota(jnp.int32, shape_c, 0),
        1.0, 0.0,
    ).astype(bf16)
    rows = jnp.dot(rep_r, w, preferred_element_type=f32).astype(bf16)
    tiled = jnp.dot(rows, rep_c, preferred_element_type=f32)
    shape = tiled.shape
    mask = lax.broadcasted_iota(jnp.int32, shape, 0) // r == lax.broadcasted_iota(jnp.int32, shape, 1) // c
    return jnp.where(mask, tiled, 0.0).astype(bf16)


def hidden_kernel(x_ref, fgw_ref, h_ref, wlo, whi):
    half = x_ref.shape[1] // 2
    cw = fgw_ref.shape[0] // 2
    per = CHUNK // cw

    @pl.when(pl.program_id(0) == 0)
    def _():
        w = fgw_ref[...]
        wlo[:, :CHUNK] = bd_inkernel(w[:cw, :cw], per)
        wlo[:, CHUNK:] = bd_inkernel(w[:cw, cw:], per)
        whi[:, :CHUNK] = bd_inkernel(w[cw:, :cw], per)
        whi[:, CHUNK:] = bd_inkernel(w[cw:, cw:], per)

    for j in range(half // CHUNK):
        x0 = x_ref[:, j * CHUNK : (j + 1) * CHUNK]
        x1 = x_ref[:, half + j * CHUNK : half + (j + 1) * CHUNK]
        pre = jnp.dot(x0, wlo[...], preferred_element_type=f32)
        pre = pre + jnp.dot(x1, whi[...], preferred_element_type=f32)
        h_ref[:, j * CHUNK : (j + 1) * CHUNK] = (
            jnp.tanh(pre[:, :CHUNK]) * jax.nn.sigmoid(pre[:, CHUNK:])
        ).astype(bf16)


def skip_kernel(h_ref, sw_ref, s_ref, ws):
    cw = sw_ref.shape[0]

    @pl.when(pl.program_id(0) == 0)
    def _():
        ws[...] = bd_inkernel(sw_ref[...], CHUNK // cw)

    skip_w = ws.shape[1]
    for j in range(h_ref.shape[1] // CHUNK):
        s_ref[:, j * skip_w : (j + 1) * skip_w] = jnp.dot(
            h_ref[:, j * CHUNK : (j + 1) * CHUNK], ws[...], preferred_element_type=f32
        ).astype(bf16)


def front_hidden(features, fgw):
    rows, cols = features.shape
    chunks = cols // 2 // CHUNK
    tile = min(ROW_TILE, rows)
    return pl.pallas_call(
        hidden_kernel,
        grid=(rows // tile,),
        in_specs=[
            pl.BlockSpec((tile, cols), lambda i: (i, 0)),
            pl.BlockSpec(fgw.shape, lambda i: (0, 0)),
        ],
        out_specs=pl.BlockSpec((tile, chunks * CHUNK), lambda i: (i, 0)),
        out_shape=jax.ShapeDtypeStruct((rows, chunks * CHUNK), bf16),
        scratch_shapes=[pltpu.VMEM((CHUNK, 2 * CHUNK), bf16), pltpu.VMEM((CHUNK, 2 * CHUNK), bf16)],
        compiler_params=pltpu.CompilerParams(vmem_limit_bytes=48 * 1024 * 1024),
        cost_estimate=pl.CostEstimate(
            flops=2 * rows * CHUNK * 4 * CHUNK * chunks,
            transcendentals=rows * CHUNK * chunks * 2,
            bytes_accessed=2 * rows * (cols + CHUNK * chunks),
        ),
    )(features, fgw)


def front_skip(hidden, skip_weight):
    rows, width = hidden.shape
    chunks = width // CHUNK
    cw, s = skip_weight.shape
    per = CHUNK // cw
    skip_cols = s * per * chunks
    tile = min(ROW_TILE, rows)
    return pl.pallas_call(
        skip_kernel,
        grid=(rows // tile,),
        in_specs=[
            pl.BlockSpec((tile, width), lambda i: (i, 0)),
            pl.BlockSpec(skip_weight.shape, lambda i: (0, 0)),
        ],
        out_specs=pl.BlockSpec((tile, skip_cols), lambda i: (i, 0)),
        out_shape=jax.ShapeDtypeStruct((rows, skip_cols), bf16),
        scratch_shapes=[pltpu.VMEM((CHUNK, s * per), bf16)],
        compiler_params=pltpu.CompilerParams(vmem_limit_bytes=48 * 1024 * 1024),
        cost_estimate=pl.CostEstimate(
            flops=2 * rows * CHUNK * s * per * chunks,
            transcendentals=0,
            bytes_accessed=2 * rows * (CHUNK * chunks + skip_cols),
        ),
    )(hidden, skip_weight)


def fill_pad(field_ref, lo_ref, hi_ref, pad):
    nrows = field_ref.shape[0]
    pad[:BLK, :] = lo_ref[...]
    pad[BLK : BLK + nrows, :] = field_ref[...]
    pad[BLK + nrows :, :] = hi_ref[...]


def band_block(band_ref, pad, t):
    start = pl.multiple_of(t * BLK, BLK)
    return jnp.dot(
        band_ref[pl.ds(start, BLK), :], pad[pl.ds(start, 3 * BLK), :], preferred_element_type=f32
    )


def slot_product(col_ref, farw_ref, arr_ref, k):
    return jnp.dot(farw_ref[k], arr_ref[col_ref[0, k] // EXPORT], preferred_element_type=f32)


def accumulate(col_ref, ptr_ref, field_ref, lo_ref, hi_ref, arr_ref, band_ref, farw_ref, acc, pad):
    nblk = field_ref.shape[0] // BLK
    far_cap = farw_ref.shape[0]
    nptr = ptr_ref.shape[1]
    fill_pad(field_ref, lo_ref, hi_ref, pad)
    for r in range(nblk):
        acc[r * BLK : (r + 1) * BLK, :] = band_block(band_ref, pad, r)
    acc[nblk * BLK :, :] = jnp.zeros((BLK, acc.shape[1]), f32)

    def slot(k, carry):
        row = 0
        for r in range(1, nptr):
            row = row + jnp.where(ptr_ref[0, r] <= k, 1, 0)
        start = pl.multiple_of(row * BLK, BLK)
        acc[pl.ds(start, BLK), :] += slot_product(col_ref, farw_ref, arr_ref, k)
        return carry

    lax.fori_loop(0, far_cap, slot, 0)


def early_kernel(
    col_ref, ptr_ref, req_ref, exp_ref, field_ref, lo_ref, hi_ref, arr_ref, band_ref, farw_ref,
    send_ref, edge_ref, pad, blk,
):
    nblk = field_ref.shape[0] // BLK
    own = lax.axis_index("node")
    fill_pad(field_ref, lo_ref, hi_ref, pad)
    targets = [exp_ref[own, 0], exp_ref[own, 1], 0, nblk - 1]
    for i, t in enumerate(targets):
        v = band_block(band_ref, pad, t)

        def slot(k, acc):
            return acc + slot_product(col_ref, farw_ref, arr_ref, k)

        v = lax.fori_loop(ptr_ref[0, t], ptr_ref[0, t + 1], slot, v)
        blk[i] = v.astype(bf16)

    def body(p, carry):
        send_ref[p] = blk[req_ref[p]]
        return carry

    lax.fori_loop(0, send_ref.shape[0], body, 0)
    edge_ref[0] = blk[2]
    edge_ref[1] = blk[3]


def hop1_kernel(
    col_ref, ptr_ref, field_ref, lo_ref, hi_ref, arr_ref, band_ref, farw_ref, out_ref, acc, pad,
):
    accumulate(col_ref, ptr_ref, field_ref, lo_ref, hi_ref, arr_ref, band_ref, farw_ref, acc, pad)
    nrows = field_ref.shape[0]
    out_ref[...] = acc[:nrows, :].astype(bf16)


def hop2_kernel(
    col_ref, ptr_ref, field_ref, lo_ref, hi_ref, arr_ref, band_ref, farw_ref,
    x_ref, h_ref, mix_ref, out_ref, acc, pad,
):
    accumulate(col_ref, ptr_ref, field_ref, lo_ref, hi_ref, arr_ref, band_ref, farw_ref, acc, pad)
    nrows, width = field_ref.shape
    half = x_ref.shape[1] // 2
    cw = mix_ref.shape[1]
    per = CHUNK // cw
    mix = mix_ref[...]
    m = [bd_inkernel(mix[i * cw : (i + 1) * cw], per) for i in range(3)]
    for j in range(width // CHUNK):
        cols = slice(j * CHUNK, (j + 1) * CHUNK)
        two = acc[:nrows, cols].astype(bf16)
        v = x_ref[:, half + j * CHUNK : half + (j + 1) * CHUNK].astype(f32)
        v = v + jnp.dot(h_ref[:, cols], m[0], preferred_element_type=f32)
        v = v + jnp.dot(field_ref[:, cols], m[1], preferred_element_type=f32)
        v = v + jnp.dot(two, m[2], preferred_element_type=f32)
        out_ref[:, cols] = v.astype(bf16)


def vmem():
    return pl.BlockSpec(memory_space=pltpu.VMEM)


def smem():
    return pl.BlockSpec(memory_space=pltpu.SMEM)


BIG_VMEM = pltpu.CompilerParams(vmem_limit_bytes=48 * 1024 * 1024)


def scratch(field):
    nrows, width = field.shape
    return [pltpu.VMEM((nrows + BLK, width), f32), pltpu.VMEM((nrows + 2 * BLK, width), bf16)]


def early(far_col, far_ptr, requested, export_block, field, lo, hi, arrived, band, farw3):
    nrows, width = field.shape
    return pl.pallas_call(
        early_kernel,
        in_specs=[smem()] * 4 + [vmem()] * 6,
        out_specs=[vmem(), vmem()],
        out_shape=[
            jax.ShapeDtypeStruct(arrived.shape, bf16),
            jax.ShapeDtypeStruct((2, BLK, width), bf16),
        ],
        scratch_shapes=[pltpu.VMEM((nrows + 2 * BLK, width), bf16), pltpu.VMEM((4, BLK, width), bf16)],
        compiler_params=BIG_VMEM,
        cost_estimate=pl.CostEstimate(
            flops=2 * BLK * BLK * width * (12 + farw3.shape[0]),
            transcendentals=0,
            bytes_accessed=2 * width * (nrows + 2 * arrived.shape[0] * BLK),
        ),
    )(far_col, far_ptr, requested, export_block, field, lo, hi, arrived, band, farw3)


def hop1(far_col, far_ptr, field, lo, hi, arrived, band, farw3):
    nrows, width = field.shape
    return pl.pallas_call(
        hop1_kernel,
        in_specs=[smem(), smem()] + [vmem()] * 6,
        out_specs=vmem(),
        out_shape=jax.ShapeDtypeStruct((nrows, width), bf16),
        scratch_shapes=scratch(field),
        compiler_params=BIG_VMEM,
        cost_estimate=pl.CostEstimate(
            flops=2 * BLK * BLK * width * (3 * nrows // BLK + farw3.shape[0]),
            transcendentals=0,
            bytes_accessed=2 * width * (nrows * 2 + arrived.shape[0] * BLK),
        ),
    )(far_col, far_ptr, field, lo, hi, arrived, band, farw3)


def hop2(far_col, far_ptr, field, lo, hi, arrived, band, farw3, features, hidden, mix):
    nrows, width = field.shape
    return pl.pallas_call(
        hop2_kernel,
        in_specs=[smem(), smem()] + [vmem()] * 9,
        out_specs=vmem(),
        out_shape=jax.ShapeDtypeStruct((nrows, width), bf16),
        scratch_shapes=scratch(field),
        compiler_params=BIG_VMEM,
        cost_estimate=pl.CostEstimate(
            flops=2 * BLK * BLK * width * (3 * nrows // BLK + farw3.shape[0])
            + 2 * nrows * width * CHUNK * 3,
            transcendentals=0,
            bytes_accessed=2 * width * (nrows * 6 + arrived.shape[0] * BLK),
        ),
    )(far_col, far_ptr, field, lo, hi, arrived, band, farw3, features, hidden, mix)


def halo(first, last):
    count = lax.axis_size("node")
    forward = [(i, i + 1) for i in range(count - 1)]
    backward = [(t, s) for s, t in forward]
    lo = lax.ppermute(last, "node", forward)
    hi = lax.ppermute(first, "node", backward)
    return lo, hi


def local(
    features,
    filter_gate_weight,
    skip_weight,
    mix_weight,
    band_weight,
    far_weight,
    far_ptr,
    far_col,
    export_block,
):
    node_rows = features.shape[0]
    blocks = node_rows // BLK
    far_cap = far_col.shape[1]

    own_index = lax.axis_index("node")
    own_exports = lax.dynamic_slice_in_dim(export_block, own_index, 1, 0)[0].astype(jnp.int32)
    columns = far_col[0].astype(jnp.int32)
    sources = columns // EXPORT
    pointers = far_ptr[0].astype(jnp.int32)
    slot_ids = jnp.arange(far_cap, dtype=jnp.int32)
    slot_rows = jnp.sum(
        (pointers[1:, None] <= slot_ids[None, :]).astype(jnp.int32), axis=0
    ).astype(jnp.int32)
    slot_export = columns % EXPORT
    in_use = slot_ids < pointers[-1]
    peers = jnp.arange(far_col.shape[1] + 1, dtype=jnp.int32)
    matches = (sources[None, :] == peers[:, None]) & in_use[None, :]
    wanted = jnp.sum(jnp.where(matches, slot_export[None, :], 0), axis=1)
    requested = lax.all_to_all(wanted[:, None], "node", split_axis=0, concat_axis=0, tiled=True)[
        :, 0
    ]
    send_rows = own_exports[requested].astype(jnp.int32)

    hidden = front_hidden(features, filter_gate_weight)
    blocks = node_rows // BLK
    width = hidden.shape[1]
    farw3 = far_weight.reshape(BLK, far_cap, BLK).transpose(1, 0, 2)

    def exchange(send):
        return lax.all_to_all(send, "node", split_axis=0, concat_axis=0, tiled=True)

    arrived1 = exchange(hidden.reshape(blocks, BLK, width)[send_rows])
    lo1, hi1 = halo(hidden[:BLK], hidden[node_rows - BLK :])
    skip_out = front_skip(hidden, skip_weight)
    send2, edge = early(
        far_col, far_ptr, requested, export_block, hidden, lo1, hi1, arrived1, band_weight, farw3
    )
    arrived2 = exchange(send2)
    lo2, hi2 = halo(edge[0], edge[1])
    hop_one = hop1(far_col, far_ptr, hidden, lo1, hi1, arrived1, band_weight, farw3)
    residual = hop2(
        far_col, far_ptr, hop_one, lo2, hi2, arrived2, band_weight, farw3, features, hidden, mix_weight
    )
    return residual, skip_out


def solution(mesh):
    placed = (
        P(("groups", "node"), None),
        P(),
        P(),
        P(),
        P("node", None),
        P(None, "node"),
        P("node", None),
        P("node", None),
        P(),
    )
    return jax.shard_map(
        local,
        mesh=mesh,
        in_specs=placed,
        out_specs=(P(("groups", "node"), None), P(("groups", "node"), None)),
        check_vma=False,
    )
```

```python
import functools

import jax
import jax.numpy as jnp
from jax import lax
from jax.experimental import pallas as pl
from jax.experimental.pallas import tpu as pltpu
from jax.sharding import PartitionSpec as P

BLK = 64
TOUT = 16
DILATION_STEP = 16
EXPORT = 2
CHANNEL_WIDTH = 32
S = 256
TIN = 32
CHUNK = 256
ROW_TILE = 256

f32 = jnp.float32
bf16 = jnp.bfloat16


def bd_inkernel(w, reps):
    r, c = w.shape
    shape_r = (reps * r, r)
    rep_r = jnp.where(
        lax.broadcasted_iota(jnp.int32, shape_r, 0) % r == lax.broadcasted_iota(jnp.int32, shape_r, 1),
        1.0, 0.0,
    ).astype(bf16)
    shape_c = (c, reps * c)
    rep_c = jnp.where(
        lax.broadcasted_iota(jnp.int32, shape_c, 1) % c == lax.broadcasted_iota(jnp.int32, shape_c, 0),
        1.0, 0.0,
    ).astype(bf16)
    rows = jnp.dot(rep_r, w, preferred_element_type=f32).astype(bf16)
    tiled = jnp.dot(rows, rep_c, preferred_element_type=f32)
    shape = tiled.shape
    mask = lax.broadcasted_iota(jnp.int32, shape, 0) // r == lax.broadcasted_iota(jnp.int32, shape, 1) // c
    return jnp.where(mask, tiled, 0.0).astype(bf16)


def hidden_kernel(x_ref, fgw_ref, h_ref, wlo, whi):
    half = x_ref.shape[1] // 2
    cw = fgw_ref.shape[0] // 2
    per = CHUNK // cw

    @pl.when(pl.program_id(0) == 0)
    def _():
        w = fgw_ref[...]
        wlo[:, :CHUNK] = bd_inkernel(w[:cw, :cw], per)
        wlo[:, CHUNK:] = bd_inkernel(w[:cw, cw:], per)
        whi[:, :CHUNK] = bd_inkernel(w[cw:, :cw], per)
        whi[:, CHUNK:] = bd_inkernel(w[cw:, cw:], per)

    for j in range(half // CHUNK):
        x0 = x_ref[:, j * CHUNK : (j + 1) * CHUNK]
        x1 = x_ref[:, half + j * CHUNK : half + (j + 1) * CHUNK]
        pre = jnp.dot(x0, wlo[...], preferred_element_type=f32)
        pre = pre + jnp.dot(x1, whi[...], preferred_element_type=f32)
        h_ref[:, j * CHUNK : (j + 1) * CHUNK] = (
            jnp.tanh(pre[:, :CHUNK]) * jax.nn.sigmoid(pre[:, CHUNK:])
        ).astype(bf16)


def skip_kernel(h_ref, sw_ref, s_ref, ws):
    cw = sw_ref.shape[0]

    @pl.when(pl.program_id(0) == 0)
    def _():
        ws[...] = bd_inkernel(sw_ref[...], CHUNK // cw)

    skip_w = ws.shape[1]
    for j in range(h_ref.shape[1] // CHUNK):
        s_ref[:, j * skip_w : (j + 1) * skip_w] = jnp.dot(
            h_ref[:, j * CHUNK : (j + 1) * CHUNK], ws[...], preferred_element_type=f32
        ).astype(bf16)


def front_hidden(features, fgw):
    rows, cols = features.shape
    chunks = cols // 2 // CHUNK
    tile = min(ROW_TILE, rows)
    return pl.pallas_call(
        hidden_kernel,
        grid=(rows // tile,),
        in_specs=[
            pl.BlockSpec((tile, cols), lambda i: (i, 0)),
            pl.BlockSpec(fgw.shape, lambda i: (0, 0)),
        ],
        out_specs=pl.BlockSpec((tile, chunks * CHUNK), lambda i: (i, 0)),
        out_shape=jax.ShapeDtypeStruct((rows, chunks * CHUNK), bf16),
        scratch_shapes=[pltpu.VMEM((CHUNK, 2 * CHUNK), bf16), pltpu.VMEM((CHUNK, 2 * CHUNK), bf16)],
        compiler_params=pltpu.CompilerParams(vmem_limit_bytes=48 * 1024 * 1024),
        cost_estimate=pl.CostEstimate(
            flops=2 * rows * CHUNK * 4 * CHUNK * chunks,
            transcendentals=rows * CHUNK * chunks * 2,
            bytes_accessed=2 * rows * (cols + CHUNK * chunks),
        ),
    )(features, fgw)


def front_skip(hidden, skip_weight):
    rows, width = hidden.shape
    chunks = width // CHUNK
    cw, s = skip_weight.shape
    per = CHUNK // cw
    skip_cols = s * per * chunks
    tile = min(ROW_TILE, rows)
    return pl.pallas_call(
        skip_kernel,
        grid=(rows // tile,),
        in_specs=[
            pl.BlockSpec((tile, width), lambda i: (i, 0)),
            pl.BlockSpec(skip_weight.shape, lambda i: (0, 0)),
        ],
        out_specs=pl.BlockSpec((tile, skip_cols), lambda i: (i, 0)),
        out_shape=jax.ShapeDtypeStruct((rows, skip_cols), bf16),
        scratch_shapes=[pltpu.VMEM((CHUNK, s * per), bf16)],
        compiler_params=pltpu.CompilerParams(vmem_limit_bytes=48 * 1024 * 1024),
        cost_estimate=pl.CostEstimate(
            flops=2 * rows * CHUNK * s * per * chunks,
            transcendentals=0,
            bytes_accessed=2 * rows * (CHUNK * chunks + skip_cols),
        ),
    )(hidden, skip_weight)


def fill_pad(field_ref, lo_ref, hi_ref, pad):
    nrows = field_ref.shape[0]
    pad[:BLK, :] = lo_ref[...]
    pad[BLK : BLK + nrows, :] = field_ref[...]
    pad[BLK + nrows :, :] = hi_ref[...]


def band_block(band_ref, pad, t):
    start = pl.multiple_of(t * BLK, BLK)
    return jnp.dot(
        band_ref[pl.ds(start, BLK), :], pad[pl.ds(start, 3 * BLK), :], preferred_element_type=f32
    )


def slot_product(col_ref, farw_ref, arr_ref, k):
    return jnp.dot(farw_ref[k], arr_ref[col_ref[0, k] // EXPORT], preferred_element_type=f32)


def accumulate(col_ref, ptr_ref, field_ref, lo_ref, hi_ref, arr_ref, band_ref, farw_ref, acc, pad):
    nblk = field_ref.shape[0] // BLK
    far_cap = farw_ref.shape[0]
    nptr = ptr_ref.shape[1]
    fill_pad(field_ref, lo_ref, hi_ref, pad)
    for r in range(nblk):
        acc[r * BLK : (r + 1) * BLK, :] = band_block(band_ref, pad, r)
    acc[nblk * BLK :, :] = jnp.zeros((BLK, acc.shape[1]), f32)

    def slot(k, carry):
        row = 0
        for r in range(1, nptr):
            row = row + jnp.where(ptr_ref[0, r] <= k, 1, 0)
        start = pl.multiple_of(row * BLK, BLK)
        acc[pl.ds(start, BLK), :] += slot_product(col_ref, farw_ref, arr_ref, k)
        return carry

    lax.fori_loop(0, far_cap, slot, 0)


def early_kernel(
    col_ref, ptr_ref, req_ref, exp_ref, field_ref, lo_ref, hi_ref, arr_ref, band_ref, farw_ref,
    send_ref, edge_ref, pad, blk,
):
    nblk = field_ref.shape[0] // BLK
    own = lax.axis_index("node")
    fill_pad(field_ref, lo_ref, hi_ref, pad)
    targets = [exp_ref[own, 0], exp_ref[own, 1], 0, nblk - 1]
    for i, t in enumerate(targets):
        v = band_block(band_ref, pad, t)

        def slot(k, acc):
            return acc + slot_product(col_ref, farw_ref, arr_ref, k)

        v = lax.fori_loop(ptr_ref[0, t], ptr_ref[0, t + 1], slot, v)
        blk[i] = v.astype(bf16)

    def body(p, carry):
        send_ref[p] = blk[req_ref[p]]
        return carry

    lax.fori_loop(0, send_ref.shape[0], body, 0)
    edge_ref[0] = blk[2]
    edge_ref[1] = blk[3]


def hop1_kernel(
    col_ref, ptr_ref, field_ref, lo_ref, hi_ref, arr_ref, band_ref, farw_ref, out_ref, acc, pad,
):
    accumulate(col_ref, ptr_ref, field_ref, lo_ref, hi_ref, arr_ref, band_ref, farw_ref, acc, pad)
    nrows = field_ref.shape[0]
    out_ref[...] = acc[:nrows, :].astype(bf16)


def hop2_kernel(
    col_ref, ptr_ref, field_ref, lo_ref, hi_ref, arr_ref, band_ref, farw_ref,
    x_hbm, h_hbm, mix_ref, out_ref, acc, pad, xs, hs, sems,
):
    nrows, width = field_ref.shape
    half = x_hbm.shape[1] // 2
    x_copy = pltpu.make_async_copy(x_hbm.at[:, pl.ds(half, width)], xs, sems.at[0])
    h_copy = pltpu.make_async_copy(h_hbm, hs, sems.at[1])
    x_copy.start()
    h_copy.start()
    accumulate(col_ref, ptr_ref, field_ref, lo_ref, hi_ref, arr_ref, band_ref, farw_ref, acc, pad)
    cw = mix_ref.shape[1]
    per = CHUNK // cw
    mix = mix_ref[...]
    m = [bd_inkernel(mix[i * cw : (i + 1) * cw], per) for i in range(3)]
    x_copy.wait()
    h_copy.wait()
    for j in range(width // CHUNK):
        cols = slice(j * CHUNK, (j + 1) * CHUNK)
        two = acc[:nrows, cols].astype(bf16)
        v = xs[:, cols].astype(f32)
        v = v + jnp.dot(hs[:, cols], m[0], preferred_element_type=f32)
        v = v + jnp.dot(field_ref[:, cols], m[1], preferred_element_type=f32)
        v = v + jnp.dot(two, m[2], preferred_element_type=f32)
        out_ref[:, cols] = v.astype(bf16)


def vmem():
    return pl.BlockSpec(memory_space=pltpu.VMEM)


def smem():
    return pl.BlockSpec(memory_space=pltpu.SMEM)


def hbm():
    return pl.BlockSpec(memory_space=pltpu.HBM)


BIG_VMEM = pltpu.CompilerParams(vmem_limit_bytes=48 * 1024 * 1024)


def scratch(field):
    nrows, width = field.shape
    return [pltpu.VMEM((nrows + BLK, width), f32), pltpu.VMEM((nrows + 2 * BLK, width), bf16)]


def early(far_col, far_ptr, requested, export_block, field, lo, hi, arrived, band, farw3):
    nrows, width = field.shape
    return pl.pallas_call(
        early_kernel,
        in_specs=[smem()] * 4 + [vmem()] * 6,
        out_specs=[vmem(), vmem()],
        out_shape=[
            jax.ShapeDtypeStruct(arrived.shape, bf16),
            jax.ShapeDtypeStruct((2, BLK, width), bf16),
        ],
        scratch_shapes=[pltpu.VMEM((nrows + 2 * BLK, width), bf16), pltpu.VMEM((4, BLK, width), bf16)],
        compiler_params=BIG_VMEM,
        cost_estimate=pl.CostEstimate(
            flops=2 * BLK * BLK * width * (12 + farw3.shape[0]),
            transcendentals=0,
            bytes_accessed=2 * width * (nrows + 2 * arrived.shape[0] * BLK),
        ),
    )(far_col, far_ptr, requested, export_block, field, lo, hi, arrived, band, farw3)


def hop1(far_col, far_ptr, field, lo, hi, arrived, band, farw3):
    nrows, width = field.shape
    return pl.pallas_call(
        hop1_kernel,
        in_specs=[smem(), smem()] + [vmem()] * 6,
        out_specs=vmem(),
        out_shape=jax.ShapeDtypeStruct((nrows, width), bf16),
        scratch_shapes=scratch(field),
        compiler_params=BIG_VMEM,
        cost_estimate=pl.CostEstimate(
            flops=2 * BLK * BLK * width * (3 * nrows // BLK + farw3.shape[0]),
            transcendentals=0,
            bytes_accessed=2 * width * (nrows * 2 + arrived.shape[0] * BLK),
        ),
    )(far_col, far_ptr, field, lo, hi, arrived, band, farw3)


def hop2(far_col, far_ptr, field, lo, hi, arrived, band, farw3, features, hidden, mix):
    nrows, width = field.shape
    return pl.pallas_call(
        hop2_kernel,
        in_specs=[smem(), smem()] + [vmem()] * 6 + [hbm(), hbm(), vmem()],
        out_specs=vmem(),
        out_shape=jax.ShapeDtypeStruct((nrows, width), bf16),
        scratch_shapes=scratch(field)
        + [
            pltpu.VMEM((nrows, width), bf16),
            pltpu.VMEM((nrows, width), bf16),
            pltpu.SemaphoreType.DMA((2,)),
        ],
        compiler_params=pltpu.CompilerParams(),
        cost_estimate=pl.CostEstimate(
            flops=2 * BLK * BLK * width * (3 * nrows // BLK + farw3.shape[0])
            + 2 * nrows * width * CHUNK * 3,
            transcendentals=0,
            bytes_accessed=2 * width * (nrows * 6 + arrived.shape[0] * BLK),
        ),
    )(far_col, far_ptr, field, lo, hi, arrived, band, farw3, features, hidden, mix)


def halo(first, last):
    count = lax.axis_size("node")
    forward = [(i, i + 1) for i in range(count - 1)]
    backward = [(t, s) for s, t in forward]
    lo = lax.ppermute(last, "node", forward)
    hi = lax.ppermute(first, "node", backward)
    return lo, hi


def local(
    features,
    filter_gate_weight,
    skip_weight,
    mix_weight,
    band_weight,
    far_weight,
    far_ptr,
    far_col,
    export_block,
):
    node_rows = features.shape[0]
    blocks = node_rows // BLK
    far_cap = far_col.shape[1]

    own_index = lax.axis_index("node")
    own_exports = lax.dynamic_slice_in_dim(export_block, own_index, 1, 0)[0].astype(jnp.int32)
    columns = far_col[0].astype(jnp.int32)
    sources = columns // EXPORT
    pointers = far_ptr[0].astype(jnp.int32)
    slot_ids = jnp.arange(far_cap, dtype=jnp.int32)
    slot_rows = jnp.sum(
        (pointers[1:, None] <= slot_ids[None, :]).astype(jnp.int32), axis=0
    ).astype(jnp.int32)
    slot_export = columns % EXPORT
    in_use = slot_ids < pointers[-1]
    peers = jnp.arange(far_col.shape[1] + 1, dtype=jnp.int32)
    matches = (sources[None, :] == peers[:, None]) & in_use[None, :]
    wanted = jnp.sum(jnp.where(matches, slot_export[None, :], 0), axis=1)
    requested = lax.all_to_all(wanted[:, None], "node", split_axis=0, concat_axis=0, tiled=True)[
        :, 0
    ]
    send_rows = own_exports[requested].astype(jnp.int32)

    hidden = front_hidden(features, filter_gate_weight)
    blocks = node_rows // BLK
    width = hidden.shape[1]
    farw3 = far_weight.reshape(BLK, far_cap, BLK).transpose(1, 0, 2)

    def exchange(send):
        return lax.all_to_all(send, "node", split_axis=0, concat_axis=0, tiled=True)

    arrived1 = exchange(hidden.reshape(blocks, BLK, width)[send_rows])
    lo1, hi1 = halo(hidden[:BLK], hidden[node_rows - BLK :])
    skip_out = front_skip(hidden, skip_weight)
    send2, edge = early(
        far_col, far_ptr, requested, export_block, hidden, lo1, hi1, arrived1, band_weight, farw3
    )
    arrived2 = exchange(send2)
    lo2, hi2 = halo(edge[0], edge[1])
    hop_one = hop1(far_col, far_ptr, hidden, lo1, hi1, arrived1, band_weight, farw3)
    residual = hop2(
        far_col, far_ptr, hop_one, lo2, hi2, arrived2, band_weight, farw3, features, hidden, mix_weight
    )
    return residual, skip_out


def solution(mesh):
    placed = (
        P(("groups", "node"), None),
        P(),
        P(),
        P(),
        P("node", None),
        P(None, "node"),
        P("node", None),
        P("node", None),
        P(),
    )
    return jax.shard_map(
        local,
        mesh=mesh,
        in_specs=placed,
        out_specs=(P(("groups", "node"), None), P(("groups", "node"), None)),
        check_vma=False,
    )
```

```python
import functools

import jax
import jax.numpy as jnp
from jax import lax
from jax.experimental import pallas as pl
from jax.experimental.pallas import tpu as pltpu
from jax.sharding import PartitionSpec as P

BLK = 64
TOUT = 16
DILATION_STEP = 16
EXPORT = 2
CHANNEL_WIDTH = 32
S = 256
TIN = 32
CHUNK = 256
ROW_TILE = 256

f32 = jnp.float32
bf16 = jnp.bfloat16


def bd_inkernel(w, reps):
    r, c = w.shape
    shape_r = (reps * r, r)
    rep_r = jnp.where(
        lax.broadcasted_iota(jnp.int32, shape_r, 0) % r == lax.broadcasted_iota(jnp.int32, shape_r, 1),
        1.0, 0.0,
    ).astype(bf16)
    shape_c = (c, reps * c)
    rep_c = jnp.where(
        lax.broadcasted_iota(jnp.int32, shape_c, 1) % c == lax.broadcasted_iota(jnp.int32, shape_c, 0),
        1.0, 0.0,
    ).astype(bf16)
    rows = jnp.dot(rep_r, w, preferred_element_type=f32).astype(bf16)
    tiled = jnp.dot(rows, rep_c, preferred_element_type=f32)
    shape = tiled.shape
    mask = lax.broadcasted_iota(jnp.int32, shape, 0) // r == lax.broadcasted_iota(jnp.int32, shape, 1) // c
    return jnp.where(mask, tiled, 0.0).astype(bf16)


def hidden_kernel(x_ref, fgw_ref, h_ref, wlo, whi):
    half = x_ref.shape[1] // 2
    cw = fgw_ref.shape[0] // 2
    per = CHUNK // cw

    @pl.when(pl.program_id(0) == 0)
    def _():
        w = fgw_ref[...]
        wlo[:, :CHUNK] = bd_inkernel(w[:cw, :cw], per)
        wlo[:, CHUNK:] = bd_inkernel(w[:cw, cw:], per)
        whi[:, :CHUNK] = bd_inkernel(w[cw:, :cw], per)
        whi[:, CHUNK:] = bd_inkernel(w[cw:, cw:], per)

    for j in range(half // CHUNK):
        x0 = x_ref[:, j * CHUNK : (j + 1) * CHUNK]
        x1 = x_ref[:, half + j * CHUNK : half + (j + 1) * CHUNK]
        pre = jnp.dot(x0, wlo[...], preferred_element_type=f32)
        pre = pre + jnp.dot(x1, whi[...], preferred_element_type=f32)
        h_ref[:, j * CHUNK : (j + 1) * CHUNK] = (
            jnp.tanh(pre[:, :CHUNK]) * jax.nn.sigmoid(pre[:, CHUNK:])
        ).astype(bf16)


def skip_kernel(h_ref, sw_ref, s_ref, ws):
    cw = sw_ref.shape[0]

    @pl.when(pl.program_id(0) == 0)
    def _():
        ws[...] = bd_inkernel(sw_ref[...], CHUNK // cw)

    skip_w = ws.shape[1]
    for j in range(h_ref.shape[1] // CHUNK):
        s_ref[:, j * skip_w : (j + 1) * skip_w] = jnp.dot(
            h_ref[:, j * CHUNK : (j + 1) * CHUNK], ws[...], preferred_element_type=f32
        ).astype(bf16)


def front_hidden(features, fgw):
    rows, cols = features.shape
    chunks = cols // 2 // CHUNK
    tile = min(ROW_TILE, rows)
    return pl.pallas_call(
        hidden_kernel,
        grid=(rows // tile,),
        in_specs=[
            pl.BlockSpec((tile, cols), lambda i: (i, 0)),
            pl.BlockSpec(fgw.shape, lambda i: (0, 0)),
        ],
        out_specs=pl.BlockSpec((tile, chunks * CHUNK), lambda i: (i, 0)),
        out_shape=jax.ShapeDtypeStruct((rows, chunks * CHUNK), bf16),
        scratch_shapes=[pltpu.VMEM((CHUNK, 2 * CHUNK), bf16), pltpu.VMEM((CHUNK, 2 * CHUNK), bf16)],
        compiler_params=pltpu.CompilerParams(vmem_limit_bytes=48 * 1024 * 1024),
        cost_estimate=pl.CostEstimate(
            flops=2 * rows * CHUNK * 4 * CHUNK * chunks,
            transcendentals=rows * CHUNK * chunks * 2,
            bytes_accessed=2 * rows * (cols + CHUNK * chunks),
        ),
    )(features, fgw)


def front_skip(hidden, skip_weight):
    rows, width = hidden.shape
    chunks = width // CHUNK
    cw, s = skip_weight.shape
    per = CHUNK // cw
    skip_cols = s * per * chunks
    tile = min(ROW_TILE, rows)
    return pl.pallas_call(
        skip_kernel,
        grid=(rows // tile,),
        in_specs=[
            pl.BlockSpec((tile, width), lambda i: (i, 0)),
            pl.BlockSpec(skip_weight.shape, lambda i: (0, 0)),
        ],
        out_specs=pl.BlockSpec((tile, skip_cols), lambda i: (i, 0)),
        out_shape=jax.ShapeDtypeStruct((rows, skip_cols), bf16),
        scratch_shapes=[pltpu.VMEM((CHUNK, s * per), bf16)],
        compiler_params=pltpu.CompilerParams(vmem_limit_bytes=48 * 1024 * 1024),
        cost_estimate=pl.CostEstimate(
            flops=2 * rows * CHUNK * s * per * chunks,
            transcendentals=0,
            bytes_accessed=2 * rows * (CHUNK * chunks + skip_cols),
        ),
    )(hidden, skip_weight)


def fill_pad(field_ref, lo_ref, hi_ref, pad):
    nrows = field_ref.shape[0]
    pad[:BLK, :] = lo_ref[...]
    pad[BLK : BLK + nrows, :] = field_ref[...]
    pad[BLK + nrows :, :] = hi_ref[...]


def band_block(band_ref, pad, t):
    start = pl.multiple_of(t * BLK, BLK)
    return jnp.dot(
        band_ref[pl.ds(start, BLK), :], pad[pl.ds(start, 3 * BLK), :], preferred_element_type=f32
    )


def slot_product(col_ref, farw_ref, arr_ref, k):
    return jnp.dot(farw_ref[k], arr_ref[col_ref[0, k] // EXPORT], preferred_element_type=f32)


def accumulate(col_ref, ptr_ref, field_ref, lo_ref, hi_ref, arr_ref, band_ref, farw_ref, acc, pad):
    nblk = field_ref.shape[0] // BLK
    far_cap = farw_ref.shape[0]
    nptr = ptr_ref.shape[1]
    fill_pad(field_ref, lo_ref, hi_ref, pad)
    for r in range(nblk):
        acc[r * BLK : (r + 1) * BLK, :] = band_block(band_ref, pad, r)
    acc[nblk * BLK :, :] = jnp.zeros((BLK, acc.shape[1]), f32)

    def slot(k, carry):
        row = 0
        for r in range(1, nptr):
            row = row + jnp.where(ptr_ref[0, r] <= k, 1, 0)
        start = pl.multiple_of(row * BLK, BLK)
        acc[pl.ds(start, BLK), :] += slot_product(col_ref, farw_ref, arr_ref, k)
        return carry

    lax.fori_loop(0, far_cap, slot, 0)


def early_kernel(
    col_ref, ptr_ref, req_ref, exp_ref, field_ref, lo_ref, hi_ref, arr_ref, band_ref, farw_ref,
    send_ref, edge_ref, pad, blk,
):
    nblk = field_ref.shape[0] // BLK
    own = lax.axis_index("node")
    fill_pad(field_ref, lo_ref, hi_ref, pad)
    targets = [exp_ref[own, 0], exp_ref[own, 1], 0, nblk - 1]
    for i, t in enumerate(targets):
        v = band_block(band_ref, pad, t)

        def slot(k, acc):
            return acc + slot_product(col_ref, farw_ref, arr_ref, k)

        v = lax.fori_loop(ptr_ref[0, t], ptr_ref[0, t + 1], slot, v)
        blk[i] = v.astype(bf16)

    def body(p, carry):
        send_ref[p] = blk[req_ref[p]]
        return carry

    lax.fori_loop(0, send_ref.shape[0], body, 0)
    edge_ref[0] = blk[2]
    edge_ref[1] = blk[3]


def hop1_kernel(
    col_ref, ptr_ref, field_ref, lo_ref, hi_ref, arr_ref, band_ref, farw_ref, x_hbm, mix_ref,
    out_ref, part_ref, acc, pad, xs, sems,
):
    nrows, width = field_ref.shape
    half = x_hbm.shape[1] // 2
    x_copy = pltpu.make_async_copy(x_hbm.at[:, pl.ds(half, width)], xs, sems.at[0])
    x_copy.start()
    accumulate(col_ref, ptr_ref, field_ref, lo_ref, hi_ref, arr_ref, band_ref, farw_ref, acc, pad)
    out_ref[...] = acc[:nrows, :].astype(bf16)
    cw = mix_ref.shape[1]
    per = CHUNK // cw
    mix = mix_ref[...]
    m0 = bd_inkernel(mix[:cw], per)
    m1 = bd_inkernel(mix[cw : 2 * cw], per)
    x_copy.wait()
    for j in range(width // CHUNK):
        cols = slice(j * CHUNK, (j + 1) * CHUNK)
        v = xs[:, cols].astype(f32)
        v = v + jnp.dot(field_ref[:, cols], m0, preferred_element_type=f32)
        v = v + jnp.dot(out_ref[:, cols], m1, preferred_element_type=f32)
        part_ref[:, cols] = v


def hop2_kernel(
    col_ref, ptr_ref, field_ref, lo_ref, hi_ref, arr_ref, band_ref, farw_ref,
    part_hbm, mix_ref, out_ref, acc, pad, ps, sems,
):
    nrows, width = field_ref.shape
    p_copy = pltpu.make_async_copy(part_hbm, ps, sems.at[0])
    p_copy.start()
    accumulate(col_ref, ptr_ref, field_ref, lo_ref, hi_ref, arr_ref, band_ref, farw_ref, acc, pad)
    cw = mix_ref.shape[1]
    m2 = bd_inkernel(mix_ref[2 * cw :], CHUNK // cw)
    p_copy.wait()
    for j in range(width // CHUNK):
        cols = slice(j * CHUNK, (j + 1) * CHUNK)
        two = acc[:nrows, cols].astype(bf16)
        v = ps[:, cols] + jnp.dot(two, m2, preferred_element_type=f32)
        out_ref[:, cols] = v.astype(bf16)


def vmem():
    return pl.BlockSpec(memory_space=pltpu.VMEM)


def smem():
    return pl.BlockSpec(memory_space=pltpu.SMEM)


def hbm():
    return pl.BlockSpec(memory_space=pltpu.HBM)


BIG_VMEM = pltpu.CompilerParams(vmem_limit_bytes=48 * 1024 * 1024)


def scratch(field):
    nrows, width = field.shape
    return [pltpu.VMEM((nrows + BLK, width), f32), pltpu.VMEM((nrows + 2 * BLK, width), bf16)]


def early(far_col, far_ptr, requested, export_block, field, lo, hi, arrived, band, farw3):
    nrows, width = field.shape
    return pl.pallas_call(
        early_kernel,
        in_specs=[smem()] * 4 + [vmem()] * 6,
        out_specs=[vmem(), vmem()],
        out_shape=[
            jax.ShapeDtypeStruct(arrived.shape, bf16),
            jax.ShapeDtypeStruct((2, BLK, width), bf16),
        ],
        scratch_shapes=[pltpu.VMEM((nrows + 2 * BLK, width), bf16), pltpu.VMEM((4, BLK, width), bf16)],
        compiler_params=BIG_VMEM,
        cost_estimate=pl.CostEstimate(
            flops=2 * BLK * BLK * width * (12 + farw3.shape[0]),
            transcendentals=0,
            bytes_accessed=2 * width * (nrows + 2 * arrived.shape[0] * BLK),
        ),
    )(far_col, far_ptr, requested, export_block, field, lo, hi, arrived, band, farw3)


def hop1(far_col, far_ptr, field, lo, hi, arrived, band, farw3, features, mix):
    nrows, width = field.shape
    return pl.pallas_call(
        hop1_kernel,
        in_specs=[smem(), smem()] + [vmem()] * 6 + [hbm(), vmem()],
        out_specs=[vmem(), vmem()],
        out_shape=[
            jax.ShapeDtypeStruct((nrows, width), bf16),
            jax.ShapeDtypeStruct((nrows, width), f32),
        ],
        scratch_shapes=scratch(field)
        + [pltpu.VMEM((nrows, width), bf16), pltpu.SemaphoreType.DMA((1,))],
        compiler_params=pltpu.CompilerParams(),
        cost_estimate=pl.CostEstimate(
            flops=2 * BLK * BLK * width * (3 * nrows // BLK + farw3.shape[0])
            + 2 * nrows * width * CHUNK * 2,
            transcendentals=0,
            bytes_accessed=2 * width * (nrows * 7 + arrived.shape[0] * BLK),
        ),
    )(far_col, far_ptr, field, lo, hi, arrived, band, farw3, features, mix)


def hop2(far_col, far_ptr, field, lo, hi, arrived, band, farw3, part, mix):
    nrows, width = field.shape
    return pl.pallas_call(
        hop2_kernel,
        in_specs=[smem(), smem()] + [vmem()] * 6 + [hbm(), vmem()],
        out_specs=vmem(),
        out_shape=jax.ShapeDtypeStruct((nrows, width), bf16),
        scratch_shapes=scratch(field)
        + [pltpu.VMEM((nrows, width), f32), pltpu.SemaphoreType.DMA((1,))],
        compiler_params=pltpu.CompilerParams(),
        cost_estimate=pl.CostEstimate(
            flops=2 * BLK * BLK * width * (3 * nrows // BLK + farw3.shape[0])
            + 2 * nrows * width * CHUNK,
            transcendentals=0,
            bytes_accessed=2 * width * (nrows * 5 + arrived.shape[0] * BLK),
        ),
    )(far_col, far_ptr, field, lo, hi, arrived, band, farw3, part, mix)


def halo(first, last):
    count = lax.axis_size("node")
    forward = [(i, i + 1) for i in range(count - 1)]
    backward = [(t, s) for s, t in forward]
    lo = lax.ppermute(last, "node", forward)
    hi = lax.ppermute(first, "node", backward)
    return lo, hi


def local(
    features,
    filter_gate_weight,
    skip_weight,
    mix_weight,
    band_weight,
    far_weight,
    far_ptr,
    far_col,
    export_block,
):
    node_rows = features.shape[0]
    blocks = node_rows // BLK
    far_cap = far_col.shape[1]

    own_index = lax.axis_index("node")
    own_exports = lax.dynamic_slice_in_dim(export_block, own_index, 1, 0)[0].astype(jnp.int32)
    peer_count = far_cap + 1
    info = jnp.concatenate([far_col[0], far_ptr[0, -1:]]).astype(jnp.int32)
    info_all = lax.all_to_all(
        jnp.broadcast_to(info[None, :], (peer_count, far_cap + 1)),
        "node", split_axis=0, concat_axis=0, tiled=True,
    )
    slot_ids = jnp.arange(far_cap, dtype=jnp.int32)
    cols_all = info_all[:, :far_cap]
    hits = (cols_all // EXPORT == own_index) & (slot_ids[None, :] < info_all[:, far_cap:])
    requested = jnp.sum(jnp.where(hits, cols_all % EXPORT, 0), axis=1).astype(jnp.int32)
    send_rows = own_exports[requested].astype(jnp.int32)
    hidden = front_hidden(features, filter_gate_weight)
    blocks = node_rows // BLK
    width = hidden.shape[1]
    farw3 = far_weight.reshape(BLK, far_cap, BLK).transpose(1, 0, 2)

    def exchange(send):
        return lax.all_to_all(send, "node", split_axis=0, concat_axis=0, tiled=True)

    arrived1 = exchange(hidden.reshape(blocks, BLK, width)[send_rows])
    lo1, hi1 = halo(hidden[:BLK], hidden[node_rows - BLK :])
    skip_out = front_skip(hidden, skip_weight)
    send2, edge = early(
        far_col, far_ptr, requested, export_block, hidden, lo1, hi1, arrived1, band_weight, farw3
    )
    arrived2 = exchange(send2)
    lo2, hi2 = halo(edge[0], edge[1])
    hop_one, part = hop1(
        far_col, far_ptr, hidden, lo1, hi1, arrived1, band_weight, farw3, features, mix_weight
    )
    residual = hop2(far_col, far_ptr, hop_one, lo2, hi2, arrived2, band_weight, farw3, part, mix_weight)
    return residual, skip_out


def solution(mesh):
    placed = (
        P(("groups", "node"), None),
        P(),
        P(),
        P(),
        P("node", None),
        P(None, "node"),
        P("node", None),
        P("node", None),
        P(),
    )
    return jax.shard_map(
        local,
        mesh=mesh,
        in_specs=placed,
        out_specs=(P(("groups", "node"), None), P(("groups", "node"), None)),
        check_vma=False,
    )
```

```python
import functools

import jax
import jax.numpy as jnp
from jax import lax
from jax.experimental import pallas as pl
from jax.experimental.pallas import tpu as pltpu
from jax.sharding import PartitionSpec as P

BLK = 64
TOUT = 16
DILATION_STEP = 16
EXPORT = 2
CHANNEL_WIDTH = 32
S = 256
TIN = 32
CHUNK = 256
ROW_TILE = 256

f32 = jnp.float32
bf16 = jnp.bfloat16


def bd_inkernel(w, reps):
    r, c = w.shape
    shape_r = (reps * r, r)
    rep_r = jnp.where(
        lax.broadcasted_iota(jnp.int32, shape_r, 0) % r == lax.broadcasted_iota(jnp.int32, shape_r, 1),
        1.0, 0.0,
    ).astype(bf16)
    shape_c = (c, reps * c)
    rep_c = jnp.where(
        lax.broadcasted_iota(jnp.int32, shape_c, 1) % c == lax.broadcasted_iota(jnp.int32, shape_c, 0),
        1.0, 0.0,
    ).astype(bf16)
    rows = jnp.dot(rep_r, w, preferred_element_type=f32).astype(bf16)
    tiled = jnp.dot(rows, rep_c, preferred_element_type=f32)
    shape = tiled.shape
    mask = lax.broadcasted_iota(jnp.int32, shape, 0) // r == lax.broadcasted_iota(jnp.int32, shape, 1) // c
    return jnp.where(mask, tiled, 0.0).astype(bf16)


def hidden_kernel(x_ref, fgw_ref, h_ref, wlo, whi):
    half = x_ref.shape[1] // 2
    cw = fgw_ref.shape[0] // 2
    per = CHUNK // cw

    @pl.when(pl.program_id(0) == 0)
    def _():
        w = fgw_ref[...]
        wlo[:, :CHUNK] = bd_inkernel(w[:cw, :cw], per)
        wlo[:, CHUNK:] = bd_inkernel(w[:cw, cw:], per)
        whi[:, :CHUNK] = bd_inkernel(w[cw:, :cw], per)
        whi[:, CHUNK:] = bd_inkernel(w[cw:, cw:], per)

    for j in range(half // CHUNK):
        x0 = x_ref[:, j * CHUNK : (j + 1) * CHUNK]
        x1 = x_ref[:, half + j * CHUNK : half + (j + 1) * CHUNK]
        pre = jnp.dot(x0, wlo[...], preferred_element_type=f32)
        pre = pre + jnp.dot(x1, whi[...], preferred_element_type=f32)
        h_ref[:, j * CHUNK : (j + 1) * CHUNK] = (
            jnp.tanh(pre[:, :CHUNK]) * jax.nn.sigmoid(pre[:, CHUNK:])
        ).astype(bf16)


def skip_kernel(h_ref, sw_ref, s_ref, ws):
    cw = sw_ref.shape[0]

    @pl.when(pl.program_id(0) == 0)
    def _():
        ws[...] = bd_inkernel(sw_ref[...], CHUNK // cw)

    skip_w = ws.shape[1]
    for j in range(h_ref.shape[1] // CHUNK):
        s_ref[:, j * skip_w : (j + 1) * skip_w] = jnp.dot(
            h_ref[:, j * CHUNK : (j + 1) * CHUNK], ws[...], preferred_element_type=f32
        ).astype(bf16)


def front_hidden(features, fgw):
    rows, cols = features.shape
    chunks = cols // 2 // CHUNK
    tile = min(ROW_TILE, rows)
    return pl.pallas_call(
        hidden_kernel,
        grid=(rows // tile,),
        in_specs=[
            pl.BlockSpec((tile, cols), lambda i: (i, 0)),
            pl.BlockSpec(fgw.shape, lambda i: (0, 0)),
        ],
        out_specs=pl.BlockSpec((tile, chunks * CHUNK), lambda i: (i, 0)),
        out_shape=jax.ShapeDtypeStruct((rows, chunks * CHUNK), bf16),
        scratch_shapes=[pltpu.VMEM((CHUNK, 2 * CHUNK), bf16), pltpu.VMEM((CHUNK, 2 * CHUNK), bf16)],
        compiler_params=pltpu.CompilerParams(vmem_limit_bytes=48 * 1024 * 1024),
        cost_estimate=pl.CostEstimate(
            flops=2 * rows * CHUNK * 4 * CHUNK * chunks,
            transcendentals=rows * CHUNK * chunks * 2,
            bytes_accessed=2 * rows * (cols + CHUNK * chunks),
        ),
    )(features, fgw)


def front_skip(hidden, skip_weight):
    rows, width = hidden.shape
    chunks = width // CHUNK
    cw, s = skip_weight.shape
    per = CHUNK // cw
    skip_cols = s * per * chunks
    tile = min(ROW_TILE, rows)
    return pl.pallas_call(
        skip_kernel,
        grid=(rows // tile,),
        in_specs=[
            pl.BlockSpec((tile, width), lambda i: (i, 0)),
            pl.BlockSpec(skip_weight.shape, lambda i: (0, 0)),
        ],
        out_specs=pl.BlockSpec((tile, skip_cols), lambda i: (i, 0)),
        out_shape=jax.ShapeDtypeStruct((rows, skip_cols), bf16),
        scratch_shapes=[pltpu.VMEM((CHUNK, s * per), bf16)],
        compiler_params=pltpu.CompilerParams(vmem_limit_bytes=48 * 1024 * 1024),
        cost_estimate=pl.CostEstimate(
            flops=2 * rows * CHUNK * s * per * chunks,
            transcendentals=0,
            bytes_accessed=2 * rows * (CHUNK * chunks + skip_cols),
        ),
    )(hidden, skip_weight)


def fill_pad(field_ref, lo_ref, hi_ref, pad):
    nrows = field_ref.shape[0]
    pad[:BLK, :] = lo_ref[...]
    pad[BLK : BLK + nrows, :] = field_ref[...]
    pad[BLK + nrows :, :] = hi_ref[...]


def band_block(band_ref, pad, t):
    start = pl.multiple_of(t * BLK, BLK)
    return jnp.dot(
        band_ref[pl.ds(start, BLK), :], pad[pl.ds(start, 3 * BLK), :], preferred_element_type=f32
    )


def slot_product(col_ref, farw_ref, arr_ref, k):
    return jnp.dot(farw_ref[k], arr_ref[col_ref[0, k] // EXPORT], preferred_element_type=f32)


def accumulate(col_ref, ptr_ref, field_ref, lo_ref, hi_ref, arr_ref, band_ref, farw_ref, acc, pad):
    nblk = field_ref.shape[0] // BLK
    far_cap = farw_ref.shape[0]
    nptr = ptr_ref.shape[1]
    fill_pad(field_ref, lo_ref, hi_ref, pad)
    for r in range(nblk):
        acc[r * BLK : (r + 1) * BLK, :] = band_block(band_ref, pad, r)
    acc[nblk * BLK :, :] = jnp.zeros((BLK, acc.shape[1]), f32)

    def slot(k, carry):
        row = 0
        for r in range(1, nptr):
            row = row + jnp.where(ptr_ref[0, r] <= k, 1, 0)
        start = pl.multiple_of(row * BLK, BLK)
        acc[pl.ds(start, BLK), :] += slot_product(col_ref, farw_ref, arr_ref, k)
        return carry

    lax.fori_loop(0, far_cap, slot, 0)


def early_kernel(
    col_ref, ptr_ref, req_ref, exp_ref, field_ref, lo_ref, hi_ref, arr_ref, band_ref, farw_ref,
    send_ref, edge_ref, blk,
):
    nblk = field_ref.shape[0] // BLK
    own = lax.axis_index("node")
    targets = [exp_ref[own, 0], exp_ref[own, 1], 0, nblk - 1]
    for i, t in enumerate(targets):
        pieces = []
        for s in range(3):
            b = jnp.clip(t - 1 + s, 0, nblk - 1)
            v = field_ref[pl.ds(pl.multiple_of(b * BLK, BLK), BLK), :]
            if s == 0:
                v = jnp.where(t == 0, lo_ref[...], v)
            if s == 2:
                v = jnp.where(t == nblk - 1, hi_ref[...], v)
            pieces.append(v)
        win = jnp.concatenate(pieces, axis=0)
        start = pl.multiple_of(t * BLK, BLK)
        v = jnp.dot(band_ref[pl.ds(start, BLK), :], win, preferred_element_type=f32)

        def slot(k, acc):
            return acc + slot_product(col_ref, farw_ref, arr_ref, k)

        v = lax.fori_loop(ptr_ref[0, t], ptr_ref[0, t + 1], slot, v)
        blk[i] = v.astype(bf16)

    def body(p, carry):
        send_ref[p] = blk[req_ref[p]]
        return carry

    lax.fori_loop(0, send_ref.shape[0], body, 0)
    edge_ref[0] = blk[2]
    edge_ref[1] = blk[3]


def hop1_kernel(
    col_ref, ptr_ref, field_ref, lo_ref, hi_ref, arr_ref, band_ref, farw_ref, x_hbm, mix_ref,
    lo2_ref, hi2_ref, out_ref, part_ref, acc2_ref, acc, pad, xs, sems,
):
    nrows, width = field_ref.shape
    nblk = nrows // BLK
    half = x_hbm.shape[1] // 2
    x_copy = pltpu.make_async_copy(x_hbm.at[:, pl.ds(half, width)], xs, sems.at[0])
    x_copy.start()
    accumulate(col_ref, ptr_ref, field_ref, lo_ref, hi_ref, arr_ref, band_ref, farw_ref, acc, pad)
    out_ref[...] = acc[:nrows, :].astype(bf16)
    fill_pad(out_ref, lo2_ref, hi2_ref, pad)
    for r in range(nblk):
        acc2_ref[r * BLK : (r + 1) * BLK, :] = band_block(band_ref, pad, r)
    acc2_ref[nblk * BLK :, :] = jnp.zeros((BLK, width), f32)
    cw = mix_ref.shape[1]
    per = CHUNK // cw
    mix = mix_ref[...]
    m0 = bd_inkernel(mix[:cw], per)
    m1 = bd_inkernel(mix[cw : 2 * cw], per)
    x_copy.wait()
    for j in range(width // CHUNK):
        cols = slice(j * CHUNK, (j + 1) * CHUNK)
        v = xs[:, cols].astype(f32)
        v = v + jnp.dot(field_ref[:, cols], m0, preferred_element_type=f32)
        v = v + jnp.dot(out_ref[:, cols], m1, preferred_element_type=f32)
        part_ref[:, cols] = v


def hop2_kernel(col_ref, ptr_ref, arr_ref, farw_ref, acc2_hbm, part_hbm, mix_ref, out_ref, far, a2, ps, sems):
    nrows, width = out_ref.shape
    a_copy = pltpu.make_async_copy(acc2_hbm, a2, sems.at[0])
    p_copy = pltpu.make_async_copy(part_hbm, ps, sems.at[1])
    a_copy.start()
    p_copy.start()
    far[...] = jnp.zeros(far.shape, f32)
    far_cap = farw_ref.shape[0]
    nptr = ptr_ref.shape[1]

    def slot(k, carry):
        row = 0
        for r in range(1, nptr):
            row = row + jnp.where(ptr_ref[0, r] <= k, 1, 0)
        start = pl.multiple_of(row * BLK, BLK)
        far[pl.ds(start, BLK), :] += slot_product(col_ref, farw_ref, arr_ref, k)
        return carry

    lax.fori_loop(0, far_cap, slot, 0)
    cw = mix_ref.shape[1]
    m2 = bd_inkernel(mix_ref[2 * cw :], CHUNK // cw)
    a_copy.wait()
    p_copy.wait()
    for j in range(width // CHUNK):
        cols = slice(j * CHUNK, (j + 1) * CHUNK)
        two = (a2[:nrows, cols] + far[:nrows, cols]).astype(bf16)
        v = ps[:, cols] + jnp.dot(two, m2, preferred_element_type=f32)
        out_ref[:, cols] = v.astype(bf16)


def vmem():
    return pl.BlockSpec(memory_space=pltpu.VMEM)


def smem():
    return pl.BlockSpec(memory_space=pltpu.SMEM)


def hbm():
    return pl.BlockSpec(memory_space=pltpu.HBM)


BIG_VMEM = pltpu.CompilerParams(vmem_limit_bytes=48 * 1024 * 1024)


def scratch(field):
    nrows, width = field.shape
    return [pltpu.VMEM((nrows + BLK, width), f32), pltpu.VMEM((nrows + 2 * BLK, width), bf16)]


def early(far_col, far_ptr, requested, export_block, field, lo, hi, arrived, band, farw3):
    nrows, width = field.shape
    return pl.pallas_call(
        early_kernel,
        in_specs=[smem()] * 4 + [vmem()] * 6,
        out_specs=[vmem(), vmem()],
        out_shape=[
            jax.ShapeDtypeStruct(arrived.shape, bf16),
            jax.ShapeDtypeStruct((2, BLK, width), bf16),
        ],
        scratch_shapes=[pltpu.VMEM((4, BLK, width), bf16)],
        compiler_params=BIG_VMEM,
        cost_estimate=pl.CostEstimate(
            flops=2 * BLK * BLK * width * (12 + farw3.shape[0]),
            transcendentals=0,
            bytes_accessed=2 * width * (nrows + 2 * arrived.shape[0] * BLK),
        ),
    )(far_col, far_ptr, requested, export_block, field, lo, hi, arrived, band, farw3)


def hop1(far_col, far_ptr, field, lo, hi, arrived, band, farw3, features, mix, lo2, hi2):
    nrows, width = field.shape
    return pl.pallas_call(
        hop1_kernel,
        in_specs=[smem(), smem()] + [vmem()] * 6 + [hbm(), vmem(), vmem(), vmem()],
        out_specs=[vmem(), vmem(), vmem()],
        out_shape=[
            jax.ShapeDtypeStruct((nrows, width), bf16),
            jax.ShapeDtypeStruct((nrows, width), f32),
            jax.ShapeDtypeStruct((nrows + BLK, width), f32),
        ],
        scratch_shapes=scratch(field)
        + [pltpu.VMEM((nrows, width), bf16), pltpu.SemaphoreType.DMA((1,))],
        compiler_params=pltpu.CompilerParams(),
        cost_estimate=pl.CostEstimate(
            flops=2 * BLK * BLK * width * (6 * nrows // BLK + farw3.shape[0])
            + 2 * nrows * width * CHUNK * 2,
            transcendentals=0,
            bytes_accessed=2 * width * (nrows * 9 + arrived.shape[0] * BLK),
        ),
    )(far_col, far_ptr, field, lo, hi, arrived, band, farw3, features, mix, lo2, hi2)


def hop2(far_col, far_ptr, arrived, farw3, acc2, part, mix):
    nrows, width = part.shape
    return pl.pallas_call(
        hop2_kernel,
        in_specs=[smem(), smem(), vmem(), vmem(), hbm(), hbm(), vmem()],
        out_specs=vmem(),
        out_shape=jax.ShapeDtypeStruct((nrows, width), bf16),
        scratch_shapes=[
            pltpu.VMEM((nrows + BLK, width), f32),
            pltpu.VMEM((nrows + BLK, width), f32),
            pltpu.VMEM((nrows, width), f32),
            pltpu.SemaphoreType.DMA((2,)),
        ],
        compiler_params=pltpu.CompilerParams(),
        cost_estimate=pl.CostEstimate(
            flops=2 * BLK * BLK * width * farw3.shape[0] + 2 * nrows * width * CHUNK,
            transcendentals=0,
            bytes_accessed=4 * width * nrows * 3,
        ),
    )(far_col, far_ptr, arrived, farw3, acc2, part, mix)


def halo(first, last):
    count = lax.axis_size("node")
    forward = [(i, i + 1) for i in range(count - 1)]
    backward = [(t, s) for s, t in forward]
    lo = lax.ppermute(last, "node", forward)
    hi = lax.ppermute(first, "node", backward)
    return lo, hi


def local(
    features,
    filter_gate_weight,
    skip_weight,
    mix_weight,
    band_weight,
    far_weight,
    far_ptr,
    far_col,
    export_block,
):
    node_rows = features.shape[0]
    blocks = node_rows // BLK
    far_cap = far_col.shape[1]

    own_index = lax.axis_index("node")
    own_exports = lax.dynamic_slice_in_dim(export_block, own_index, 1, 0)[0].astype(jnp.int32)
    peer_count = far_cap + 1
    info = jnp.concatenate([far_col[0], far_ptr[0, -1:]]).astype(jnp.int32)
    info_all = lax.all_to_all(
        jnp.broadcast_to(info[None, :], (peer_count, far_cap + 1)),
        "node", split_axis=0, concat_axis=0, tiled=True,
    )
    slot_ids = jnp.arange(far_cap, dtype=jnp.int32)
    cols_all = info_all[:, :far_cap]
    hits = (cols_all // EXPORT == own_index) & (slot_ids[None, :] < info_all[:, far_cap:])
    requested = jnp.sum(jnp.where(hits, cols_all % EXPORT, 0), axis=1).astype(jnp.int32)
    send_rows = own_exports[requested].astype(jnp.int32)
    hidden = front_hidden(features, filter_gate_weight)
    blocks = node_rows // BLK
    width = hidden.shape[1]
    farw3 = far_weight.reshape(BLK, far_cap, BLK).transpose(1, 0, 2)

    def exchange(send):
        return lax.all_to_all(send, "node", split_axis=0, concat_axis=0, tiled=True)

    arrived1 = exchange(hidden.reshape(blocks, BLK, width)[send_rows])
    lo1, hi1 = halo(hidden[:BLK], hidden[node_rows - BLK :])
    skip_out = front_skip(hidden, skip_weight)
    send2, edge = early(
        far_col, far_ptr, requested, export_block, hidden, lo1, hi1, arrived1, band_weight, farw3
    )
    arrived2 = exchange(send2)
    lo2, hi2 = halo(edge[0], edge[1])
    hop_one, part, acc2 = hop1(
        far_col, far_ptr, hidden, lo1, hi1, arrived1, band_weight, farw3, features, mix_weight,
        lo2, hi2,
    )
    residual = hop2(far_col, far_ptr, arrived2, farw3, acc2, part, mix_weight)
    return residual, skip_out


def solution(mesh):
    placed = (
        P(("groups", "node"), None),
        P(),
        P(),
        P(),
        P("node", None),
        P(None, "node"),
        P("node", None),
        P("node", None),
        P(),
    )
    return jax.shard_map(
        local,
        mesh=mesh,
        in_specs=placed,
        out_specs=(P(("groups", "node"), None), P(("groups", "node"), None)),
        check_vma=False,
    )
```

```python
import functools

import jax
import jax.numpy as jnp
from jax import lax
from jax.experimental import pallas as pl
from jax.experimental.pallas import tpu as pltpu
from jax.sharding import PartitionSpec as P

BLK = 64
TOUT = 16
DILATION_STEP = 16
EXPORT = 2
CHANNEL_WIDTH = 32
S = 256
TIN = 32
CHUNK = 256
ROW_TILE = 256

f32 = jnp.float32
bf16 = jnp.bfloat16


def bd_inkernel(w, reps):
    r, c = w.shape
    shape_r = (reps * r, r)
    rep_r = jnp.where(
        lax.broadcasted_iota(jnp.int32, shape_r, 0) % r == lax.broadcasted_iota(jnp.int32, shape_r, 1),
        1.0, 0.0,
    ).astype(bf16)
    shape_c = (c, reps * c)
    rep_c = jnp.where(
        lax.broadcasted_iota(jnp.int32, shape_c, 1) % c == lax.broadcasted_iota(jnp.int32, shape_c, 0),
        1.0, 0.0,
    ).astype(bf16)
    rows = jnp.dot(rep_r, w, preferred_element_type=f32).astype(bf16)
    tiled = jnp.dot(rows, rep_c, preferred_element_type=f32)
    shape = tiled.shape
    mask = lax.broadcasted_iota(jnp.int32, shape, 0) // r == lax.broadcasted_iota(jnp.int32, shape, 1) // c
    return jnp.where(mask, tiled, 0.0).astype(bf16)


def hidden_kernel(x_ref, fgw_ref, h_ref, wlo, whi):
    half = x_ref.shape[1] // 2
    cw = fgw_ref.shape[0] // 2
    per = CHUNK // cw

    @pl.when(pl.program_id(0) == 0)
    def _():
        w = fgw_ref[...]
        wlo[:, :CHUNK] = bd_inkernel(w[:cw, :cw], per)
        wlo[:, CHUNK:] = bd_inkernel(w[:cw, cw:], per)
        whi[:, :CHUNK] = bd_inkernel(w[cw:, :cw], per)
        whi[:, CHUNK:] = bd_inkernel(w[cw:, cw:], per)

    for j in range(half // CHUNK):
        x0 = x_ref[:, j * CHUNK : (j + 1) * CHUNK]
        x1 = x_ref[:, half + j * CHUNK : half + (j + 1) * CHUNK]
        pre = jnp.dot(x0, wlo[...], preferred_element_type=f32)
        pre = pre + jnp.dot(x1, whi[...], preferred_element_type=f32)
        h_ref[:, j * CHUNK : (j + 1) * CHUNK] = (
            jnp.tanh(pre[:, :CHUNK]) * jax.nn.sigmoid(pre[:, CHUNK:])
        ).astype(bf16)


def skip_kernel(h_ref, sw_ref, s_ref, ws):
    cw = sw_ref.shape[0]

    @pl.when(pl.program_id(0) == 0)
    def _():
        ws[...] = bd_inkernel(sw_ref[...], CHUNK // cw)

    skip_w = ws.shape[1]
    for j in range(h_ref.shape[1] // CHUNK):
        s_ref[:, j * skip_w : (j + 1) * skip_w] = jnp.dot(
            h_ref[:, j * CHUNK : (j + 1) * CHUNK], ws[...], preferred_element_type=f32
        ).astype(bf16)


def front_hidden(features, fgw):
    rows, cols = features.shape
    chunks = cols // 2 // CHUNK
    tile = min(ROW_TILE, rows)
    return pl.pallas_call(
        hidden_kernel,
        grid=(rows // tile,),
        in_specs=[
            pl.BlockSpec((tile, cols), lambda i: (i, 0)),
            pl.BlockSpec(fgw.shape, lambda i: (0, 0)),
        ],
        out_specs=pl.BlockSpec((tile, chunks * CHUNK), lambda i: (i, 0)),
        out_shape=jax.ShapeDtypeStruct((rows, chunks * CHUNK), bf16),
        scratch_shapes=[pltpu.VMEM((CHUNK, 2 * CHUNK), bf16), pltpu.VMEM((CHUNK, 2 * CHUNK), bf16)],
        compiler_params=pltpu.CompilerParams(vmem_limit_bytes=48 * 1024 * 1024),
        cost_estimate=pl.CostEstimate(
            flops=2 * rows * CHUNK * 4 * CHUNK * chunks,
            transcendentals=rows * CHUNK * chunks * 2,
            bytes_accessed=2 * rows * (cols + CHUNK * chunks),
        ),
    )(features, fgw)


def front_skip(hidden, skip_weight):
    rows, width = hidden.shape
    chunks = width // CHUNK
    cw, s = skip_weight.shape
    per = CHUNK // cw
    skip_cols = s * per * chunks
    tile = min(ROW_TILE, rows)
    return pl.pallas_call(
        skip_kernel,
        grid=(rows // tile,),
        in_specs=[
            pl.BlockSpec((tile, width), lambda i: (i, 0)),
            pl.BlockSpec(skip_weight.shape, lambda i: (0, 0)),
        ],
        out_specs=pl.BlockSpec((tile, skip_cols), lambda i: (i, 0)),
        out_shape=jax.ShapeDtypeStruct((rows, skip_cols), bf16),
        scratch_shapes=[pltpu.VMEM((CHUNK, s * per), bf16)],
        compiler_params=pltpu.CompilerParams(vmem_limit_bytes=48 * 1024 * 1024),
        cost_estimate=pl.CostEstimate(
            flops=2 * rows * CHUNK * s * per * chunks,
            transcendentals=0,
            bytes_accessed=2 * rows * (CHUNK * chunks + skip_cols),
        ),
    )(hidden, skip_weight)


def fill_pad(field_ref, lo_ref, hi_ref, pad):
    nrows = field_ref.shape[0]
    pad[:BLK, :] = lo_ref[...]
    pad[BLK : BLK + nrows, :] = field_ref[...]
    pad[BLK + nrows :, :] = hi_ref[...]


def band_block(band_ref, pad, t):
    start = pl.multiple_of(t * BLK, BLK)
    return jnp.dot(
        band_ref[pl.ds(start, BLK), :], pad[pl.ds(start, 3 * BLK), :], preferred_element_type=f32
    )


def slot_product(col_ref, farw_ref, arr_ref, k):
    return jnp.dot(farw_ref[k], arr_ref[col_ref[0, k] // EXPORT], preferred_element_type=f32)


def accumulate(col_ref, ptr_ref, field_ref, lo_ref, hi_ref, arr_ref, band_ref, farw_ref, acc, pad):
    nblk = field_ref.shape[0] // BLK
    far_cap = farw_ref.shape[0]
    nptr = ptr_ref.shape[1]
    fill_pad(field_ref, lo_ref, hi_ref, pad)
    for r in range(nblk):
        acc[r * BLK : (r + 1) * BLK, :] = band_block(band_ref, pad, r)
    acc[nblk * BLK :, :] = jnp.zeros((BLK, acc.shape[1]), f32)

    def slot(k, carry):
        row = 0
        for r in range(1, nptr):
            row = row + jnp.where(ptr_ref[0, r] <= k, 1, 0)
        start = pl.multiple_of(row * BLK, BLK)
        acc[pl.ds(start, BLK), :] += slot_product(col_ref, farw_ref, arr_ref, k)
        return carry

    lax.fori_loop(0, far_cap, slot, 0)


def early_kernel(
    col_ref, ptr_ref, req_ref, exp_ref, field_ref, lo_ref, hi_ref, arr_ref, band_ref, farw_ref,
    send_ref, edge_ref, pad, blk,
):
    nblk = field_ref.shape[0] // BLK
    own = lax.axis_index("node")
    fill_pad(field_ref, lo_ref, hi_ref, pad)
    targets = [exp_ref[own, 0], exp_ref[own, 1], 0, nblk - 1]
    for i, t in enumerate(targets):
        v = band_block(band_ref, pad, t)

        def slot(k, acc):
            return acc + slot_product(col_ref, farw_ref, arr_ref, k)

        v = lax.fori_loop(ptr_ref[0, t], ptr_ref[0, t + 1], slot, v)
        blk[i] = v.astype(bf16)

    def body(p, carry):
        send_ref[p] = blk[req_ref[p]]
        return carry

    lax.fori_loop(0, send_ref.shape[0], body, 0)
    edge_ref[0] = blk[2]
    edge_ref[1] = blk[3]


def hop1_kernel(
    col_ref, ptr_ref, field_ref, lo_ref, hi_ref, arr_ref, band_ref, farw_ref, x_hbm, mix_ref,
    out_ref, part_ref, acc2_ref, acc, pad, xs, sems,
):
    nrows, width = field_ref.shape
    nblk = nrows // BLK
    half = x_hbm.shape[1] // 2
    x_copy = pltpu.make_async_copy(x_hbm.at[:, pl.ds(half, width)], xs, sems.at[0])
    x_copy.start()
    accumulate(col_ref, ptr_ref, field_ref, lo_ref, hi_ref, arr_ref, band_ref, farw_ref, acc, pad)
    out_ref[...] = acc[:nrows, :].astype(bf16)
    zero = jnp.zeros((BLK, width), bf16)
    fill_pad(out_ref, zero, zero, pad)
    for r in range(nblk):
        acc2_ref[r * BLK : (r + 1) * BLK, :] = band_block(band_ref, pad, r)
    cw = mix_ref.shape[1]
    per = CHUNK // cw
    mix = mix_ref[...]
    m0 = bd_inkernel(mix[:cw], per)
    m1 = bd_inkernel(mix[cw : 2 * cw], per)
    x_copy.wait()
    for j in range(width // CHUNK):
        cols = slice(j * CHUNK, (j + 1) * CHUNK)
        v = xs[:, cols].astype(f32)
        v = v + jnp.dot(field_ref[:, cols], m0, preferred_element_type=f32)
        v = v + jnp.dot(out_ref[:, cols], m1, preferred_element_type=f32)
        part_ref[:, cols] = v


def hop2_kernel(
    col_ref, ptr_ref, lo_ref, hi_ref, arr_ref, band_ref, farw_ref, acc2_hbm, part_hbm, mix_ref,
    out_ref, far, a2, ps, sems,
):
    nrows, width = out_ref.shape
    nblk = nrows // BLK
    chunks = width // CHUNK
    copies = []
    for j in range(chunks):
        cols = pl.ds(j * CHUNK, CHUNK)
        ca = pltpu.make_async_copy(acc2_hbm.at[:, cols], a2.at[:, cols], sems.at[2 * j])
        cp = pltpu.make_async_copy(part_hbm.at[:, cols], ps.at[:, cols], sems.at[2 * j + 1])
        ca.start()
        cp.start()
        copies.append((ca, cp))
    far[...] = jnp.zeros(far.shape, f32)
    far[:BLK, :] = jnp.dot(band_ref[:BLK, :BLK], lo_ref[...], preferred_element_type=f32)
    last = (nblk - 1) * BLK
    far[last : last + BLK, :] = jnp.dot(
        band_ref[last : last + BLK, 2 * BLK :], hi_ref[...], preferred_element_type=f32
    )
    far_cap = farw_ref.shape[0]
    nptr = ptr_ref.shape[1]

    def slot(k, carry):
        row = 0
        for r in range(1, nptr):
            row = row + jnp.where(ptr_ref[0, r] <= k, 1, 0)
        start = pl.multiple_of(row * BLK, BLK)
        far[pl.ds(start, BLK), :] += slot_product(col_ref, farw_ref, arr_ref, k)
        return carry

    lax.fori_loop(0, far_cap, slot, 0)
    cw = mix_ref.shape[1]
    m2 = bd_inkernel(mix_ref[2 * cw :], CHUNK // cw)
    for j in range(chunks):
        ca, cp = copies[j]
        ca.wait()
        cp.wait()
        cols = slice(j * CHUNK, (j + 1) * CHUNK)
        two = (a2[:, cols] + far[:nrows, cols]).astype(bf16)
        v = ps[:, cols] + jnp.dot(two, m2, preferred_element_type=f32)
        out_ref[:, cols] = v.astype(bf16)


def vmem():
    return pl.BlockSpec(memory_space=pltpu.VMEM)


def smem():
    return pl.BlockSpec(memory_space=pltpu.SMEM)


def hbm():
    return pl.BlockSpec(memory_space=pltpu.HBM)


BIG_VMEM = pltpu.CompilerParams(vmem_limit_bytes=48 * 1024 * 1024)


def scratch(field):
    nrows, width = field.shape
    return [pltpu.VMEM((nrows + BLK, width), f32), pltpu.VMEM((nrows + 2 * BLK, width), bf16)]


def early(far_col, far_ptr, requested, export_block, field, lo, hi, arrived, band, farw3):
    nrows, width = field.shape
    return pl.pallas_call(
        early_kernel,
        in_specs=[smem()] * 4 + [vmem()] * 6,
        out_specs=[vmem(), vmem()],
        out_shape=[
            jax.ShapeDtypeStruct(arrived.shape, bf16),
            jax.ShapeDtypeStruct((2, BLK, width), bf16),
        ],
        scratch_shapes=[pltpu.VMEM((nrows + 2 * BLK, width), bf16), pltpu.VMEM((4, BLK, width), bf16)],
        compiler_params=BIG_VMEM,
        cost_estimate=pl.CostEstimate(
            flops=2 * BLK * BLK * width * (12 + farw3.shape[0]),
            transcendentals=0,
            bytes_accessed=2 * width * (nrows + 2 * arrived.shape[0] * BLK),
        ),
    )(far_col, far_ptr, requested, export_block, field, lo, hi, arrived, band, farw3)


def hop1(far_col, far_ptr, field, lo, hi, arrived, band, farw3, features, mix):
    nrows, width = field.shape
    return pl.pallas_call(
        hop1_kernel,
        in_specs=[smem(), smem()] + [vmem()] * 6 + [hbm(), vmem()],
        out_specs=[vmem(), vmem(), vmem()],
        out_shape=[
            jax.ShapeDtypeStruct((nrows, width), bf16),
            jax.ShapeDtypeStruct((nrows, width), f32),
            jax.ShapeDtypeStruct((nrows, width), f32),
        ],
        scratch_shapes=scratch(field)
        + [pltpu.VMEM((nrows, width), bf16), pltpu.SemaphoreType.DMA((1,))],
        compiler_params=pltpu.CompilerParams(),
        cost_estimate=pl.CostEstimate(
            flops=2 * BLK * BLK * width * (6 * nrows // BLK + farw3.shape[0])
            + 2 * nrows * width * CHUNK * 2,
            transcendentals=0,
            bytes_accessed=2 * width * (nrows * 9 + arrived.shape[0] * BLK),
        ),
    )(far_col, far_ptr, field, lo, hi, arrived, band, farw3, features, mix)


def hop2(far_col, far_ptr, lo, hi, arrived, band, farw3, acc2, part, mix):
    nrows, width = part.shape
    return pl.pallas_call(
        hop2_kernel,
        in_specs=[smem(), smem()] + [vmem()] * 5 + [hbm(), hbm(), vmem()],
        out_specs=vmem(),
        out_shape=jax.ShapeDtypeStruct((nrows, width), bf16),
        scratch_shapes=[
            pltpu.VMEM((nrows + BLK, width), f32),
            pltpu.VMEM((nrows, width), f32),
            pltpu.VMEM((nrows, width), f32),
            pltpu.SemaphoreType.DMA((2 * (width // CHUNK),)),
        ],
        compiler_params=pltpu.CompilerParams(),
        cost_estimate=pl.CostEstimate(
            flops=2 * BLK * BLK * width * (farw3.shape[0] + 2) + 2 * nrows * width * CHUNK,
            transcendentals=0,
            bytes_accessed=4 * width * nrows * 3,
        ),
    )(far_col, far_ptr, lo, hi, arrived, band, farw3, acc2, part, mix)


def halo(first, last):
    count = lax.axis_size("node")
    forward = [(i, i + 1) for i in range(count - 1)]
    backward = [(t, s) for s, t in forward]
    lo = lax.ppermute(last, "node", forward)
    hi = lax.ppermute(first, "node", backward)
    return lo, hi


def local(
    features,
    filter_gate_weight,
    skip_weight,
    mix_weight,
    band_weight,
    far_weight,
    far_ptr,
    far_col,
    export_block,
):
    node_rows = features.shape[0]
    blocks = node_rows // BLK
    far_cap = far_col.shape[1]

    own_index = lax.axis_index("node")
    own_exports = lax.dynamic_slice_in_dim(export_block, own_index, 1, 0)[0].astype(jnp.int32)
    peer_count = far_cap + 1
    info = jnp.concatenate([far_col[0], jnp.max(far_ptr[0], keepdims=True)]).astype(jnp.int32)
    info_all = lax.all_to_all(
        jnp.broadcast_to(info[None, :], (peer_count, far_cap + 1)),
        "node", split_axis=0, concat_axis=0, tiled=True,
    )
    slot_ids = jnp.arange(far_cap, dtype=jnp.int32)
    cols_all = info_all[:, :far_cap]
    hits = (cols_all // EXPORT == own_index) & (slot_ids[None, :] < info_all[:, far_cap:])
    requested = jnp.sum(jnp.where(hits, cols_all % EXPORT, 0), axis=1).astype(jnp.int32)
    send_rows = own_exports[requested].astype(jnp.int32)
    hidden = front_hidden(features, filter_gate_weight)
    blocks = node_rows // BLK
    width = hidden.shape[1]
    farw3 = far_weight.reshape(BLK, far_cap, BLK).transpose(1, 0, 2)

    def exchange(send):
        return lax.all_to_all(send, "node", split_axis=0, concat_axis=0, tiled=True)

    arrived1 = exchange(hidden.reshape(blocks, BLK, width)[send_rows])
    lo1, hi1 = halo(hidden[:BLK], hidden[node_rows - BLK :])
    skip_out = front_skip(hidden, skip_weight)
    send2, edge = early(
        far_col, far_ptr, requested, export_block, hidden, lo1, hi1, arrived1, band_weight, farw3
    )
    arrived2 = exchange(send2)
    lo2, hi2 = halo(edge[0], edge[1])
    hop_one, part, acc2 = hop1(
        far_col, far_ptr, hidden, lo1, hi1, arrived1, band_weight, farw3, features, mix_weight
    )
    residual = hop2(
        far_col, far_ptr, lo2, hi2, arrived2, band_weight, farw3, acc2, part, mix_weight
    )
    return residual, skip_out


def solution(mesh):
    placed = (
        P(("groups", "node"), None),
        P(),
        P(),
        P(),
        P("node", None),
        P(None, "node"),
        P("node", None),
        P("node", None),
        P(),
    )
    return jax.shard_map(
        local,
        mesh=mesh,
        in_specs=placed,
        out_specs=(P(("groups", "node"), None), P(("groups", "node"), None)),
        check_vma=False,
    )
```

```python
import functools

import jax
import jax.numpy as jnp
from jax import lax
from jax.experimental import pallas as pl
from jax.experimental.pallas import tpu as pltpu
from jax.sharding import PartitionSpec as P

BLK = 64
TOUT = 16
DILATION_STEP = 16
EXPORT = 2
CHANNEL_WIDTH = 32
S = 256
TIN = 32
CHUNK = 256
ROW_TILE = 256

f32 = jnp.float32
bf16 = jnp.bfloat16


def bd_inkernel(w, reps):
    r, c = w.shape
    shape_r = (reps * r, r)
    rep_r = jnp.where(
        lax.broadcasted_iota(jnp.int32, shape_r, 0) % r == lax.broadcasted_iota(jnp.int32, shape_r, 1),
        1.0, 0.0,
    ).astype(bf16)
    shape_c = (c, reps * c)
    rep_c = jnp.where(
        lax.broadcasted_iota(jnp.int32, shape_c, 1) % c == lax.broadcasted_iota(jnp.int32, shape_c, 0),
        1.0, 0.0,
    ).astype(bf16)
    rows = jnp.dot(rep_r, w, preferred_element_type=f32).astype(bf16)
    tiled = jnp.dot(rows, rep_c, preferred_element_type=f32)
    shape = tiled.shape
    mask = lax.broadcasted_iota(jnp.int32, shape, 0) // r == lax.broadcasted_iota(jnp.int32, shape, 1) // c
    return jnp.where(mask, tiled, 0.0).astype(bf16)


def hidden_kernel(x_ref, fgw_ref, h_ref, wlo, whi):
    half = x_ref.shape[1] // 2
    cw = fgw_ref.shape[0] // 2
    per = CHUNK // cw

    @pl.when(pl.program_id(0) == 0)
    def _():
        w = fgw_ref[...]
        wlo[:, :CHUNK] = bd_inkernel(w[:cw, :cw], per)
        wlo[:, CHUNK:] = bd_inkernel(w[:cw, cw:], per)
        whi[:, :CHUNK] = bd_inkernel(w[cw:, :cw], per)
        whi[:, CHUNK:] = bd_inkernel(w[cw:, cw:], per)

    for j in range(half // CHUNK):
        x0 = x_ref[:, j * CHUNK : (j + 1) * CHUNK]
        x1 = x_ref[:, half + j * CHUNK : half + (j + 1) * CHUNK]
        pre = jnp.dot(x0, wlo[...], preferred_element_type=f32)
        pre = pre + jnp.dot(x1, whi[...], preferred_element_type=f32)
        h_ref[:, j * CHUNK : (j + 1) * CHUNK] = (
            jnp.tanh(pre[:, :CHUNK]) * jax.nn.sigmoid(pre[:, CHUNK:])
        ).astype(bf16)


def prep_kernel(col_ref, ptr_ref, out_ref):
    far_cap = col_ref.shape[1]
    peers = out_ref.shape[0]
    used = jnp.max(ptr_ref[...], axis=1, keepdims=True)
    out_ref[:, :far_cap] = jnp.broadcast_to(col_ref[...], (peers, far_cap))
    out_ref[:, far_cap:] = jnp.broadcast_to(used, (peers, 1))


def prep(far_col, far_ptr):
    far_cap = far_col.shape[1]
    return pl.pallas_call(
        prep_kernel,
        in_specs=[vmem(), vmem()],
        out_specs=vmem(),
        out_shape=jax.ShapeDtypeStruct((far_cap + 1, far_cap + 1), jnp.int32),
    )(far_col, far_ptr)


def pack_kernel(info_ref, exp_ref, h_hbm, send_hbm, req_ref, sems):
    peers = send_hbm.shape[0]
    far_cap = info_ref.shape[1] - 1
    own = lax.axis_index("node")

    def peer(p, carry):
        used = info_ref[p, far_cap]

        def scan(k, acc):
            col = info_ref[p, k]
            hit = jnp.logical_and(col // EXPORT == own, k < used)
            return acc + jnp.where(hit, col % EXPORT, 0)

        req = lax.fori_loop(0, far_cap, scan, 0)
        req_ref[p] = req
        row = exp_ref[own, req]
        start = pl.multiple_of(row * BLK, BLK)
        pltpu.make_async_copy(h_hbm.at[pl.ds(start, BLK)], send_hbm.at[p], sems.at[p]).start()
        return carry

    lax.fori_loop(0, peers, peer, 0)

    def finish(p, carry):
        start = pl.multiple_of(exp_ref[own, req_ref[p]] * BLK, BLK)
        pltpu.make_async_copy(h_hbm.at[pl.ds(start, BLK)], send_hbm.at[p], sems.at[p]).wait()
        return carry

    lax.fori_loop(0, peers, finish, 0)


def pack(info_all, export_block, hidden):
    nrows, width = hidden.shape
    peers = info_all.shape[0]
    return pl.pallas_call(
        pack_kernel,
        in_specs=[smem(), smem(), hbm()],
        out_specs=[hbm(), smem()],
        out_shape=[
            jax.ShapeDtypeStruct((peers, BLK, width), bf16),
            jax.ShapeDtypeStruct((peers,), jnp.int32),
        ],
        scratch_shapes=[pltpu.SemaphoreType.DMA((peers,))],
    )(info_all, export_block, hidden)


def skip_kernel(h_ref, sw_ref, s_ref, ws):
    cw = sw_ref.shape[0]

    @pl.when(pl.program_id(0) == 0)
    def _():
        ws[...] = bd_inkernel(sw_ref[...], CHUNK // cw)

    skip_w = ws.shape[1]
    for j in range(h_ref.shape[1] // CHUNK):
        s_ref[:, j * skip_w : (j + 1) * skip_w] = jnp.dot(
            h_ref[:, j * CHUNK : (j + 1) * CHUNK], ws[...], preferred_element_type=f32
        ).astype(bf16)


def front_hidden(features, fgw):
    rows, cols = features.shape
    half = cols // 2
    tile = min(ROW_TILE, rows)
    return pl.pallas_call(
        hidden_kernel,
        grid=(rows // tile,),
        in_specs=[
            pl.BlockSpec((tile, cols), lambda i: (i, 0)),
            pl.BlockSpec(fgw.shape, lambda i: (0, 0)),
        ],
        out_specs=pl.BlockSpec((tile, half), lambda i: (i, 0)),
        out_shape=jax.ShapeDtypeStruct((rows, half), bf16),
        scratch_shapes=[pltpu.VMEM((CHUNK, 2 * CHUNK), bf16), pltpu.VMEM((CHUNK, 2 * CHUNK), bf16)],
        cost_estimate=pl.CostEstimate(
            flops=2 * rows * CHUNK * 4 * CHUNK * (half // CHUNK),
            transcendentals=rows * half * 2,
            bytes_accessed=2 * rows * (cols + half),
        ),
    )(features, fgw)


def front_skip(hidden, skip_weight):
    rows, width = hidden.shape
    chunks = width // CHUNK
    cw, s = skip_weight.shape
    per = CHUNK // cw
    skip_cols = s * per * chunks
    tile = min(ROW_TILE, rows)
    return pl.pallas_call(
        skip_kernel,
        grid=(rows // tile,),
        in_specs=[
            pl.BlockSpec((tile, width), lambda i: (i, 0)),
            pl.BlockSpec(skip_weight.shape, lambda i: (0, 0)),
        ],
        out_specs=pl.BlockSpec((tile, skip_cols), lambda i: (i, 0)),
        out_shape=jax.ShapeDtypeStruct((rows, skip_cols), bf16),
        scratch_shapes=[pltpu.VMEM((CHUNK, s * per), bf16)],
        compiler_params=pltpu.CompilerParams(vmem_limit_bytes=48 * 1024 * 1024),
        cost_estimate=pl.CostEstimate(
            flops=2 * rows * CHUNK * s * per * chunks,
            transcendentals=0,
            bytes_accessed=2 * rows * (CHUNK * chunks + skip_cols),
        ),
    )(hidden, skip_weight)


def fill_pad(field_ref, lo_ref, hi_ref, pad):
    nrows = field_ref.shape[0]
    pad[:BLK, :] = lo_ref[...]
    pad[BLK : BLK + nrows, :] = field_ref[...]
    pad[BLK + nrows :, :] = hi_ref[...]


def band_block(band_ref, pad, t):
    start = pl.multiple_of(t * BLK, BLK)
    return jnp.dot(
        band_ref[pl.ds(start, BLK), :], pad[pl.ds(start, 3 * BLK), :], preferred_element_type=f32
    )


def slot_product(col_ref, farw_ref, arr_ref, k):
    return jnp.dot(farw_ref[k], arr_ref[col_ref[0, k] // EXPORT], preferred_element_type=f32)


def accumulate(col_ref, ptr_ref, field_ref, lo_ref, hi_ref, arr_ref, band_ref, farw_ref, acc, pad):
    nblk = field_ref.shape[0] // BLK
    far_cap = farw_ref.shape[0]
    nptr = ptr_ref.shape[1]
    fill_pad(field_ref, lo_ref, hi_ref, pad)
    for r in range(nblk):
        acc[r * BLK : (r + 1) * BLK, :] = band_block(band_ref, pad, r)
    acc[nblk * BLK :, :] = jnp.zeros((BLK, acc.shape[1]), f32)

    def slot(k, carry):
        row = 0
        for r in range(1, nptr):
            row = row + jnp.where(ptr_ref[0, r] <= k, 1, 0)
        start = pl.multiple_of(row * BLK, BLK)
        acc[pl.ds(start, BLK), :] += slot_product(col_ref, farw_ref, arr_ref, k)
        return carry

    lax.fori_loop(0, far_cap, slot, 0)


def early_kernel(
    col_ref, ptr_ref, req_ref, exp_ref, field_ref, lo_ref, hi_ref, arr_ref, band_ref, farw_ref,
    send_ref, edge_ref, pad, blk,
):
    nblk = field_ref.shape[0] // BLK
    own = lax.axis_index("node")
    fill_pad(field_ref, lo_ref, hi_ref, pad)
    targets = [exp_ref[own, 0], exp_ref[own, 1], 0, nblk - 1]
    for i, t in enumerate(targets):
        v = band_block(band_ref, pad, t)

        def slot(k, acc):
            return acc + slot_product(col_ref, farw_ref, arr_ref, k)

        v = lax.fori_loop(ptr_ref[0, t], ptr_ref[0, t + 1], slot, v)
        blk[i] = v.astype(bf16)

    def body(p, carry):
        send_ref[p] = blk[req_ref[p]]
        return carry

    lax.fori_loop(0, send_ref.shape[0], body, 0)
    edge_ref[0] = blk[2]
    edge_ref[1] = blk[3]


def hop1_kernel(
    col_ref, ptr_ref, field_ref, lo_ref, hi_ref, arr_ref, band_ref, farw_ref, x_hbm, mix_ref,
    out_ref, part_ref, acc2_ref, acc, pad, xs, sems,
):
    nrows, width = field_ref.shape
    nblk = nrows // BLK
    half = x_hbm.shape[1] // 2
    x_copy = pltpu.make_async_copy(x_hbm.at[:, pl.ds(half, width)], xs, sems.at[0])
    x_copy.start()
    accumulate(col_ref, ptr_ref, field_ref, lo_ref, hi_ref, arr_ref, band_ref, farw_ref, acc, pad)
    out_ref[...] = acc[:nrows, :].astype(bf16)
    zero = jnp.zeros((BLK, width), bf16)
    fill_pad(out_ref, zero, zero, pad)
    for r in range(nblk):
        acc2_ref[r * BLK : (r + 1) * BLK, :] = band_block(band_ref, pad, r)
    cw = mix_ref.shape[1]
    per = CHUNK // cw
    mix = mix_ref[...]
    m0 = bd_inkernel(mix[:cw], per)
    m1 = bd_inkernel(mix[cw : 2 * cw], per)
    x_copy.wait()
    for j in range(width // CHUNK):
        cols = slice(j * CHUNK, (j + 1) * CHUNK)
        v = xs[:, cols].astype(f32)
        v = v + jnp.dot(field_ref[:, cols], m0, preferred_element_type=f32)
        v = v + jnp.dot(out_ref[:, cols], m1, preferred_element_type=f32)
        part_ref[:, cols] = v


def hop2_kernel(
    col_ref, ptr_ref, lo_ref, hi_ref, arr_ref, band_ref, farw_ref, acc2_hbm, part_hbm, mix_ref,
    out_ref, far, a2, ps, sems,
):
    nrows, width = out_ref.shape
    nblk = nrows // BLK
    chunks = width // CHUNK
    copies = []
    for j in range(chunks):
        cols = pl.ds(j * CHUNK, CHUNK)
        ca = pltpu.make_async_copy(acc2_hbm.at[:, cols], a2.at[:, cols], sems.at[2 * j])
        cp = pltpu.make_async_copy(part_hbm.at[:, cols], ps.at[:, cols], sems.at[2 * j + 1])
        ca.start()
        cp.start()
        copies.append((ca, cp))
    far[...] = jnp.zeros(far.shape, f32)
    far[:BLK, :] = jnp.dot(band_ref[:BLK, :BLK], lo_ref[...], preferred_element_type=f32)
    last = (nblk - 1) * BLK
    far[last : last + BLK, :] = jnp.dot(
        band_ref[last : last + BLK, 2 * BLK :], hi_ref[...], preferred_element_type=f32
    )
    far_cap = farw_ref.shape[0]
    nptr = ptr_ref.shape[1]

    def slot(k, carry):
        row = 0
        for r in range(1, nptr):
            row = row + jnp.where(ptr_ref[0, r] <= k, 1, 0)
        start = pl.multiple_of(row * BLK, BLK)
        far[pl.ds(start, BLK), :] += slot_product(col_ref, farw_ref, arr_ref, k)
        return carry

    lax.fori_loop(0, far_cap, slot, 0)
    cw = mix_ref.shape[1]
    m2 = bd_inkernel(mix_ref[2 * cw :], CHUNK // cw)
    for j in range(chunks):
        ca, cp = copies[j]
        ca.wait()
        cp.wait()
        cols = slice(j * CHUNK, (j + 1) * CHUNK)
        two = (a2[:, cols] + far[:nrows, cols]).astype(bf16)
        v = ps[:, cols] + jnp.dot(two, m2, preferred_element_type=f32)
        out_ref[:, cols] = v.astype(bf16)


def vmem():
    return pl.BlockSpec(memory_space=pltpu.VMEM)


def smem():
    return pl.BlockSpec(memory_space=pltpu.SMEM)


def hbm():
    return pl.BlockSpec(memory_space=pltpu.HBM)


BIG_VMEM = pltpu.CompilerParams(vmem_limit_bytes=48 * 1024 * 1024)


def scratch(field):
    nrows, width = field.shape
    return [pltpu.VMEM((nrows + BLK, width), f32), pltpu.VMEM((nrows + 2 * BLK, width), bf16)]


def early(far_col, far_ptr, requested, export_block, field, lo, hi, arrived, band, farw3):
    nrows, width = field.shape
    return pl.pallas_call(
        early_kernel,
        in_specs=[smem()] * 4 + [vmem()] * 6,
        out_specs=[vmem(), vmem()],
        out_shape=[
            jax.ShapeDtypeStruct(arrived.shape, bf16),
            jax.ShapeDtypeStruct((2, BLK, width), bf16),
        ],
        scratch_shapes=[pltpu.VMEM((nrows + 2 * BLK, width), bf16), pltpu.VMEM((4, BLK, width), bf16)],
        compiler_params=BIG_VMEM,
        cost_estimate=pl.CostEstimate(
            flops=2 * BLK * BLK * width * (12 + farw3.shape[0]),
            transcendentals=0,
            bytes_accessed=2 * width * (nrows + 2 * arrived.shape[0] * BLK),
        ),
    )(far_col, far_ptr, requested, export_block, field, lo, hi, arrived, band, farw3)


def hop1(far_col, far_ptr, field, lo, hi, arrived, band, farw3, features, mix):
    nrows, width = field.shape
    return pl.pallas_call(
        hop1_kernel,
        in_specs=[smem(), smem()] + [vmem()] * 6 + [hbm(), vmem()],
        out_specs=[vmem(), vmem(), vmem()],
        out_shape=[
            jax.ShapeDtypeStruct((nrows, width), bf16),
            jax.ShapeDtypeStruct((nrows, width), f32),
            jax.ShapeDtypeStruct((nrows, width), f32),
        ],
        scratch_shapes=scratch(field)
        + [pltpu.VMEM((nrows, width), bf16), pltpu.SemaphoreType.DMA((1,))],
        compiler_params=pltpu.CompilerParams(),
        cost_estimate=pl.CostEstimate(
            flops=2 * BLK * BLK * width * (6 * nrows // BLK + farw3.shape[0])
            + 2 * nrows * width * CHUNK * 2,
            transcendentals=0,
            bytes_accessed=2 * width * (nrows * 9 + arrived.shape[0] * BLK),
        ),
    )(far_col, far_ptr, field, lo, hi, arrived, band, farw3, features, mix)


def hop2(far_col, far_ptr, lo, hi, arrived, band, farw3, acc2, part, mix):
    nrows, width = part.shape
    return pl.pallas_call(
        hop2_kernel,
        in_specs=[smem(), smem()] + [vmem()] * 5 + [hbm(), hbm(), vmem()],
        out_specs=vmem(),
        out_shape=jax.ShapeDtypeStruct((nrows, width), bf16),
        scratch_shapes=[
            pltpu.VMEM((nrows + BLK, width), f32),
            pltpu.VMEM((nrows, width), f32),
            pltpu.VMEM((nrows, width), f32),
            pltpu.SemaphoreType.DMA((2 * (width // CHUNK),)),
        ],
        compiler_params=pltpu.CompilerParams(),
        cost_estimate=pl.CostEstimate(
            flops=2 * BLK * BLK * width * (farw3.shape[0] + 2) + 2 * nrows * width * CHUNK,
            transcendentals=0,
            bytes_accessed=4 * width * nrows * 3,
        ),
    )(far_col, far_ptr, lo, hi, arrived, band, farw3, acc2, part, mix)


def halo(first, last):
    count = lax.axis_size("node")
    forward = [(i, i + 1) for i in range(count - 1)]
    backward = [(t, s) for s, t in forward]
    lo = lax.ppermute(last, "node", forward)
    hi = lax.ppermute(first, "node", backward)
    return lo, hi


def local(
    features,
    filter_gate_weight,
    skip_weight,
    mix_weight,
    band_weight,
    far_weight,
    far_ptr,
    far_col,
    export_block,
):
    node_rows = features.shape[0]
    blocks = node_rows // BLK
    far_cap = far_col.shape[1]

    info_all = lax.all_to_all(prep(far_col, far_ptr), "node", split_axis=0, concat_axis=0, tiled=True)
    hidden = front_hidden(features, filter_gate_weight)
    send1, requested = pack(info_all, export_block, hidden)
    blocks = node_rows // BLK
    width = hidden.shape[1]
    farw3 = far_weight.reshape(BLK, far_cap, BLK).transpose(1, 0, 2)

    def exchange(send):
        return lax.all_to_all(send, "node", split_axis=0, concat_axis=0, tiled=True)

    arrived1 = exchange(send1)
    lo1, hi1 = halo(hidden[:BLK], hidden[node_rows - BLK :])
    skip_out = front_skip(hidden, skip_weight)
    send2, edge = early(
        far_col, far_ptr, requested, export_block, hidden, lo1, hi1, arrived1, band_weight, farw3
    )
    arrived2 = exchange(send2)
    lo2, hi2 = halo(edge[0], edge[1])
    hop_one, part, acc2 = hop1(
        far_col, far_ptr, hidden, lo1, hi1, arrived1, band_weight, farw3, features, mix_weight
    )
    residual = hop2(
        far_col, far_ptr, lo2, hi2, arrived2, band_weight, farw3, acc2, part, mix_weight
    )
    return residual, skip_out


def solution(mesh):
    placed = (
        P(("groups", "node"), None),
        P(),
        P(),
        P(),
        P("node", None),
        P(None, "node"),
        P("node", None),
        P("node", None),
        P(),
    )
    return jax.shard_map(
        local,
        mesh=mesh,
        in_specs=placed,
        out_specs=(P(("groups", "node"), None), P(("groups", "node"), None)),
        check_vma=False,
    )
```

```python
import functools

import jax
import jax.numpy as jnp
from jax import lax
from jax.experimental import pallas as pl
from jax.experimental.pallas import tpu as pltpu
from jax.sharding import PartitionSpec as P

BLK = 64
TOUT = 16
DILATION_STEP = 16
EXPORT = 2
CHANNEL_WIDTH = 32
S = 256
TIN = 32
CHUNK = 256
ROW_TILE = 256

f32 = jnp.float32
bf16 = jnp.bfloat16


def bd_inkernel(w, reps):
    r, c = w.shape
    shape_r = (reps * r, r)
    rep_r = jnp.where(
        lax.broadcasted_iota(jnp.int32, shape_r, 0) % r == lax.broadcasted_iota(jnp.int32, shape_r, 1),
        1.0, 0.0,
    ).astype(bf16)
    shape_c = (c, reps * c)
    rep_c = jnp.where(
        lax.broadcasted_iota(jnp.int32, shape_c, 1) % c == lax.broadcasted_iota(jnp.int32, shape_c, 0),
        1.0, 0.0,
    ).astype(bf16)
    rows = jnp.dot(rep_r, w, preferred_element_type=f32).astype(bf16)
    tiled = jnp.dot(rows, rep_c, preferred_element_type=f32)
    shape = tiled.shape
    mask = lax.broadcasted_iota(jnp.int32, shape, 0) // r == lax.broadcasted_iota(jnp.int32, shape, 1) // c
    return jnp.where(mask, tiled, 0.0).astype(bf16)


def hidden_kernel(x_ref, fgw_ref, h_ref, wlo, whi):
    half = x_ref.shape[1] // 2
    cw = fgw_ref.shape[0] // 2
    per = CHUNK // cw

    @pl.when(pl.program_id(0) == 0)
    def _():
        w = fgw_ref[...]
        wlo[:, :CHUNK] = bd_inkernel(w[:cw, :cw], per)
        wlo[:, CHUNK:] = bd_inkernel(w[:cw, cw:], per)
        whi[:, :CHUNK] = bd_inkernel(w[cw:, :cw], per)
        whi[:, CHUNK:] = bd_inkernel(w[cw:, cw:], per)

    for j in range(half // CHUNK):
        x0 = x_ref[:, j * CHUNK : (j + 1) * CHUNK]
        x1 = x_ref[:, half + j * CHUNK : half + (j + 1) * CHUNK]
        pre = jnp.dot(x0, wlo[...], preferred_element_type=f32)
        pre = pre + jnp.dot(x1, whi[...], preferred_element_type=f32)
        h_ref[:, j * CHUNK : (j + 1) * CHUNK] = (
            jnp.tanh(pre[:, :CHUNK]) * jax.nn.sigmoid(pre[:, CHUNK:])
        ).astype(bf16)


def prep_kernel(col_ref, ptr_ref, out_ref):
    far_cap = col_ref.shape[1]
    peers = out_ref.shape[0]
    used = jnp.max(ptr_ref[...], axis=1, keepdims=True)
    out_ref[:, :far_cap] = jnp.broadcast_to(col_ref[...], (peers, far_cap))
    out_ref[:, far_cap:] = jnp.broadcast_to(used, (peers, 1))


def prep(far_col, far_ptr):
    far_cap = far_col.shape[1]
    return pl.pallas_call(
        prep_kernel,
        in_specs=[vmem(), vmem()],
        out_specs=vmem(),
        out_shape=jax.ShapeDtypeStruct((far_cap + 1, far_cap + 1), jnp.int32),
    )(far_col, far_ptr)


def skip_kernel(h_ref, sw_ref, s_ref, ws):
    cw = sw_ref.shape[0]

    @pl.when(pl.program_id(0) == 0)
    def _():
        ws[...] = bd_inkernel(sw_ref[...], CHUNK // cw)

    skip_w = ws.shape[1]
    for j in range(h_ref.shape[1] // CHUNK):
        s_ref[:, j * skip_w : (j + 1) * skip_w] = jnp.dot(
            h_ref[:, j * CHUNK : (j + 1) * CHUNK], ws[...], preferred_element_type=f32
        ).astype(bf16)


def front_hidden(features, fgw):
    rows, cols = features.shape
    chunks = cols // 2 // CHUNK
    tile = min(ROW_TILE, rows)
    return pl.pallas_call(
        hidden_kernel,
        grid=(rows // tile,),
        in_specs=[
            pl.BlockSpec((tile, cols), lambda i: (i, 0)),
            pl.BlockSpec(fgw.shape, lambda i: (0, 0)),
        ],
        out_specs=pl.BlockSpec((tile, chunks * CHUNK), lambda i: (i, 0)),
        out_shape=jax.ShapeDtypeStruct((rows, chunks * CHUNK), bf16),
        scratch_shapes=[pltpu.VMEM((CHUNK, 2 * CHUNK), bf16), pltpu.VMEM((CHUNK, 2 * CHUNK), bf16)],
        compiler_params=pltpu.CompilerParams(vmem_limit_bytes=48 * 1024 * 1024),
        cost_estimate=pl.CostEstimate(
            flops=2 * rows * CHUNK * 4 * CHUNK * chunks,
            transcendentals=rows * CHUNK * chunks * 2,
            bytes_accessed=2 * rows * (cols + CHUNK * chunks),
        ),
    )(features, fgw)


def front_skip(hidden, skip_weight):
    rows, width = hidden.shape
    chunks = width // CHUNK
    cw, s = skip_weight.shape
    per = CHUNK // cw
    skip_cols = s * per * chunks
    tile = min(ROW_TILE, rows)
    return pl.pallas_call(
        skip_kernel,
        grid=(rows // tile,),
        in_specs=[
            pl.BlockSpec((tile, width), lambda i: (i, 0)),
            pl.BlockSpec(skip_weight.shape, lambda i: (0, 0)),
        ],
        out_specs=pl.BlockSpec((tile, skip_cols), lambda i: (i, 0)),
        out_shape=jax.ShapeDtypeStruct((rows, skip_cols), bf16),
        scratch_shapes=[pltpu.VMEM((CHUNK, s * per), bf16)],
        compiler_params=pltpu.CompilerParams(vmem_limit_bytes=48 * 1024 * 1024),
        cost_estimate=pl.CostEstimate(
            flops=2 * rows * CHUNK * s * per * chunks,
            transcendentals=0,
            bytes_accessed=2 * rows * (CHUNK * chunks + skip_cols),
        ),
    )(hidden, skip_weight)


def fill_pad(field_ref, lo_ref, hi_ref, pad):
    nrows = field_ref.shape[0]
    pad[:BLK, :] = lo_ref[...]
    pad[BLK : BLK + nrows, :] = field_ref[...]
    pad[BLK + nrows :, :] = hi_ref[...]


def band_block(band_ref, pad, t):
    start = pl.multiple_of(t * BLK, BLK)
    return jnp.dot(
        band_ref[pl.ds(start, BLK), :], pad[pl.ds(start, 3 * BLK), :], preferred_element_type=f32
    )


def slot_product(col_ref, farw_ref, arr_ref, k):
    return jnp.dot(farw_ref[k], arr_ref[col_ref[0, k] // EXPORT], preferred_element_type=f32)


def accumulate(col_ref, ptr_ref, field_ref, lo_ref, hi_ref, arr_ref, band_ref, farw_ref, acc, pad):
    nblk = field_ref.shape[0] // BLK
    far_cap = farw_ref.shape[0]
    nptr = ptr_ref.shape[1]
    fill_pad(field_ref, lo_ref, hi_ref, pad)
    for r in range(nblk):
        acc[r * BLK : (r + 1) * BLK, :] = band_block(band_ref, pad, r)
    acc[nblk * BLK :, :] = jnp.zeros((BLK, acc.shape[1]), f32)

    def slot(k, carry):
        row = 0
        for r in range(1, nptr):
            row = row + jnp.where(ptr_ref[0, r] <= k, 1, 0)
        start = pl.multiple_of(row * BLK, BLK)
        acc[pl.ds(start, BLK), :] += slot_product(col_ref, farw_ref, arr_ref, k)
        return carry

    lax.fori_loop(0, far_cap, slot, 0)


def early_kernel(
    col_ref, ptr_ref, req_ref, exp_ref, field_ref, lo_ref, hi_ref, arr_ref, band_ref, farw_ref,
    send_ref, edge_ref, pad, blk,
):
    nblk = field_ref.shape[0] // BLK
    own = lax.axis_index("node")
    fill_pad(field_ref, lo_ref, hi_ref, pad)
    targets = [exp_ref[own, 0], exp_ref[own, 1], 0, nblk - 1]
    for i, t in enumerate(targets):
        v = band_block(band_ref, pad, t)

        def slot(k, acc):
            return acc + slot_product(col_ref, farw_ref, arr_ref, k)

        v = lax.fori_loop(ptr_ref[0, t], ptr_ref[0, t + 1], slot, v)
        blk[i] = v.astype(bf16)

    def body(p, carry):
        send_ref[p] = blk[req_ref[p]]
        return carry

    lax.fori_loop(0, send_ref.shape[0], body, 0)
    edge_ref[0] = blk[2]
    edge_ref[1] = blk[3]


def hop1_kernel(
    col_ref, ptr_ref, field_ref, lo_ref, hi_ref, arr_ref, band_ref, farw_ref, x_hbm, mix_ref,
    out_ref, part_ref, acc2_ref, acc, pad, xs, sems,
):
    nrows, width = field_ref.shape
    nblk = nrows // BLK
    half = x_hbm.shape[1] // 2
    x_copy = pltpu.make_async_copy(x_hbm.at[:, pl.ds(half, width)], xs, sems.at[0])
    x_copy.start()
    accumulate(col_ref, ptr_ref, field_ref, lo_ref, hi_ref, arr_ref, band_ref, farw_ref, acc, pad)
    out_ref[...] = acc[:nrows, :].astype(bf16)
    zero = jnp.zeros((BLK, width), bf16)
    fill_pad(out_ref, zero, zero, pad)
    for r in range(nblk):
        acc2_ref[r * BLK : (r + 1) * BLK, :] = band_block(band_ref, pad, r)
    cw = mix_ref.shape[1]
    per = CHUNK // cw
    mix = mix_ref[...]
    m0 = bd_inkernel(mix[:cw], per)
    m1 = bd_inkernel(mix[cw : 2 * cw], per)
    x_copy.wait()
    for j in range(width // CHUNK):
        cols = slice(j * CHUNK, (j + 1) * CHUNK)
        v = xs[:, cols].astype(f32)
        v = v + jnp.dot(field_ref[:, cols], m0, preferred_element_type=f32)
        v = v + jnp.dot(out_ref[:, cols], m1, preferred_element_type=f32)
        part_ref[:, cols] = v


def hop2_kernel(
    col_ref, ptr_ref, lo_ref, hi_ref, arr_ref, band_ref, farw_ref, acc2_hbm, part_hbm, mix_ref,
    out_ref, far, a2, ps, sems,
):
    nrows, width = out_ref.shape
    nblk = nrows // BLK
    chunks = width // CHUNK
    copies = []
    for j in range(chunks):
        cols = pl.ds(j * CHUNK, CHUNK)
        ca = pltpu.make_async_copy(acc2_hbm.at[:, cols], a2.at[:, cols], sems.at[2 * j])
        cp = pltpu.make_async_copy(part_hbm.at[:, cols], ps.at[:, cols], sems.at[2 * j + 1])
        ca.start()
        cp.start()
        copies.append((ca, cp))
    far[...] = jnp.zeros(far.shape, f32)
    far[:BLK, :] = jnp.dot(band_ref[:BLK, :BLK], lo_ref[...], preferred_element_type=f32)
    last = (nblk - 1) * BLK
    far[last : last + BLK, :] = jnp.dot(
        band_ref[last : last + BLK, 2 * BLK :], hi_ref[...], preferred_element_type=f32
    )
    far_cap = farw_ref.shape[0]
    nptr = ptr_ref.shape[1]

    def slot(k, carry):
        row = 0
        for r in range(1, nptr):
            row = row + jnp.where(ptr_ref[0, r] <= k, 1, 0)
        start = pl.multiple_of(row * BLK, BLK)
        far[pl.ds(start, BLK), :] += slot_product(col_ref, farw_ref, arr_ref, k)
        return carry

    lax.fori_loop(0, far_cap, slot, 0)
    cw = mix_ref.shape[1]
    m2 = bd_inkernel(mix_ref[2 * cw :], CHUNK // cw)
    for j in range(chunks):
        ca, cp = copies[j]
        ca.wait()
        cp.wait()
        cols = slice(j * CHUNK, (j + 1) * CHUNK)
        two = (a2[:, cols] + far[:nrows, cols]).astype(bf16)
        v = ps[:, cols] + jnp.dot(two, m2, preferred_element_type=f32)
        out_ref[:, cols] = v.astype(bf16)


def vmem():
    return pl.BlockSpec(memory_space=pltpu.VMEM)


def smem():
    return pl.BlockSpec(memory_space=pltpu.SMEM)


def hbm():
    return pl.BlockSpec(memory_space=pltpu.HBM)


BIG_VMEM = pltpu.CompilerParams(vmem_limit_bytes=48 * 1024 * 1024)


def scratch(field):
    nrows, width = field.shape
    return [pltpu.VMEM((nrows + BLK, width), f32), pltpu.VMEM((nrows + 2 * BLK, width), bf16)]


def early(far_col, far_ptr, requested, export_block, field, lo, hi, arrived, band, farw3):
    nrows, width = field.shape
    return pl.pallas_call(
        early_kernel,
        in_specs=[smem()] * 4 + [vmem()] * 6,
        out_specs=[vmem(), vmem()],
        out_shape=[
            jax.ShapeDtypeStruct(arrived.shape, bf16),
            jax.ShapeDtypeStruct((2, BLK, width), bf16),
        ],
        scratch_shapes=[pltpu.VMEM((nrows + 2 * BLK, width), bf16), pltpu.VMEM((4, BLK, width), bf16)],
        compiler_params=BIG_VMEM,
        cost_estimate=pl.CostEstimate(
            flops=2 * BLK * BLK * width * (12 + farw3.shape[0]),
            transcendentals=0,
            bytes_accessed=2 * width * (nrows + 2 * arrived.shape[0] * BLK),
        ),
    )(far_col, far_ptr, requested, export_block, field, lo, hi, arrived, band, farw3)


def hop1(far_col, far_ptr, field, lo, hi, arrived, band, farw3, features, mix):
    nrows, width = field.shape
    return pl.pallas_call(
        hop1_kernel,
        in_specs=[smem(), smem()] + [vmem()] * 6 + [hbm(), vmem()],
        out_specs=[vmem(), vmem(), vmem()],
        out_shape=[
            jax.ShapeDtypeStruct((nrows, width), bf16),
            jax.ShapeDtypeStruct((nrows, width), f32),
            jax.ShapeDtypeStruct((nrows, width), f32),
        ],
        scratch_shapes=scratch(field)
        + [pltpu.VMEM((nrows, width), bf16), pltpu.SemaphoreType.DMA((1,))],
        compiler_params=pltpu.CompilerParams(),
        cost_estimate=pl.CostEstimate(
            flops=2 * BLK * BLK * width * (6 * nrows // BLK + farw3.shape[0])
            + 2 * nrows * width * CHUNK * 2,
            transcendentals=0,
            bytes_accessed=2 * width * (nrows * 9 + arrived.shape[0] * BLK),
        ),
    )(far_col, far_ptr, field, lo, hi, arrived, band, farw3, features, mix)


def hop2(far_col, far_ptr, lo, hi, arrived, band, farw3, acc2, part, mix):
    nrows, width = part.shape
    return pl.pallas_call(
        hop2_kernel,
        in_specs=[smem(), smem()] + [vmem()] * 5 + [hbm(), hbm(), vmem()],
        out_specs=vmem(),
        out_shape=jax.ShapeDtypeStruct((nrows, width), bf16),
        scratch_shapes=[
            pltpu.VMEM((nrows + BLK, width), f32),
            pltpu.VMEM((nrows, width), f32),
            pltpu.VMEM((nrows, width), f32),
            pltpu.SemaphoreType.DMA((2 * (width // CHUNK),)),
        ],
        compiler_params=pltpu.CompilerParams(),
        cost_estimate=pl.CostEstimate(
            flops=2 * BLK * BLK * width * (farw3.shape[0] + 2) + 2 * nrows * width * CHUNK,
            transcendentals=0,
            bytes_accessed=4 * width * nrows * 3,
        ),
    )(far_col, far_ptr, lo, hi, arrived, band, farw3, acc2, part, mix)


def halo(first, last):
    count = lax.axis_size("node")
    forward = [(i, i + 1) for i in range(count - 1)]
    backward = [(t, s) for s, t in forward]
    lo = lax.ppermute(last, "node", forward)
    hi = lax.ppermute(first, "node", backward)
    return lo, hi


def local(
    features,
    filter_gate_weight,
    skip_weight,
    mix_weight,
    band_weight,
    far_weight,
    far_ptr,
    far_col,
    export_block,
):
    node_rows = features.shape[0]
    blocks = node_rows // BLK
    far_cap = far_col.shape[1]

    own_index = lax.axis_index("node")
    own_exports = lax.dynamic_slice_in_dim(export_block, own_index, 1, 0)[0].astype(jnp.int32)
    peer_count = far_cap + 1
    info_all = lax.all_to_all(prep(far_col, far_ptr), "node", split_axis=0, concat_axis=0, tiled=True)
    slot_ids = jnp.arange(far_cap, dtype=jnp.int32)
    cols_all = info_all[:, :far_cap]
    hits = (cols_all // EXPORT == own_index) & (slot_ids[None, :] < info_all[:, far_cap:])
    requested = jnp.sum(jnp.where(hits, cols_all % EXPORT, 0), axis=1).astype(jnp.int32)
    send_rows = own_exports[requested].astype(jnp.int32)
    hidden = front_hidden(features, filter_gate_weight)
    blocks = node_rows // BLK
    width = hidden.shape[1]
    farw3 = far_weight.reshape(BLK, far_cap, BLK).transpose(1, 0, 2)

    def exchange(send):
        return lax.all_to_all(send, "node", split_axis=0, concat_axis=0, tiled=True)

    arrived1 = exchange(hidden.reshape(blocks, BLK, width)[send_rows])
    lo1, hi1 = halo(hidden[:BLK], hidden[node_rows - BLK :])
    skip_out = front_skip(hidden, skip_weight)
    send2, edge = early(
        far_col, far_ptr, requested, export_block, hidden, lo1, hi1, arrived1, band_weight, farw3
    )
    arrived2 = exchange(send2)
    lo2, hi2 = halo(edge[0], edge[1])
    hop_one, part, acc2 = hop1(
        far_col, far_ptr, hidden, lo1, hi1, arrived1, band_weight, farw3, features, mix_weight
    )
    residual = hop2(
        far_col, far_ptr, lo2, hi2, arrived2, band_weight, farw3, acc2, part, mix_weight
    )
    return residual, skip_out


def solution(mesh):
    placed = (
        P(("groups", "node"), None),
        P(),
        P(),
        P(),
        P("node", None),
        P(None, "node"),
        P("node", None),
        P("node", None),
        P(),
    )
    return jax.shard_map(
        local,
        mesh=mesh,
        in_specs=placed,
        out_specs=(P(("groups", "node"), None), P(("groups", "node"), None)),
        check_vma=False,
    )
```

```python
import functools

import jax
import jax.numpy as jnp
from jax import lax
from jax.experimental import pallas as pl
from jax.experimental.pallas import tpu as pltpu
from jax.sharding import PartitionSpec as P

BLK = 64
TOUT = 16
DILATION_STEP = 16
EXPORT = 2
CHANNEL_WIDTH = 32
S = 256
TIN = 32
CHUNK = 256
ROW_TILE = 256

f32 = jnp.float32
bf16 = jnp.bfloat16


def bd_inkernel(w, reps):
    r, c = w.shape
    shape_r = (reps * r, r)
    rep_r = jnp.where(
        lax.broadcasted_iota(jnp.int32, shape_r, 0) % r == lax.broadcasted_iota(jnp.int32, shape_r, 1),
        1.0, 0.0,
    ).astype(bf16)
    shape_c = (c, reps * c)
    rep_c = jnp.where(
        lax.broadcasted_iota(jnp.int32, shape_c, 1) % c == lax.broadcasted_iota(jnp.int32, shape_c, 0),
        1.0, 0.0,
    ).astype(bf16)
    rows = jnp.dot(rep_r, w, preferred_element_type=f32).astype(bf16)
    tiled = jnp.dot(rows, rep_c, preferred_element_type=f32)
    shape = tiled.shape
    mask = lax.broadcasted_iota(jnp.int32, shape, 0) // r == lax.broadcasted_iota(jnp.int32, shape, 1) // c
    return jnp.where(mask, tiled, 0.0).astype(bf16)


def hidden_kernel(exp_ref, x_ref, fgw_ref, h_ref, ex_ref):
    rows, cols = x_ref.shape
    half = cols // 2
    cw = fgw_ref.shape[0] // 2
    per = CHUNK // cw
    w = fgw_ref[...]
    wlo = jnp.concatenate([bd_inkernel(w[:cw, :cw], per), bd_inkernel(w[:cw, cw:], per)], axis=1)
    whi = jnp.concatenate([bd_inkernel(w[cw:, :cw], per), bd_inkernel(w[cw:, cw:], per)], axis=1)
    tile = min(ROW_TILE, rows)
    for t in range(rows // tile):
        rs = slice(t * tile, (t + 1) * tile)
        for j in range(half // CHUNK):
            x0 = x_ref[rs, j * CHUNK : (j + 1) * CHUNK]
            x1 = x_ref[rs, half + j * CHUNK : half + (j + 1) * CHUNK]
            pre = jnp.dot(x0, wlo, preferred_element_type=f32)
            pre = pre + jnp.dot(x1, whi, preferred_element_type=f32)
            h_ref[rs, j * CHUNK : (j + 1) * CHUNK] = (
                jnp.tanh(pre[:, :CHUNK]) * jax.nn.sigmoid(pre[:, CHUNK:])
            ).astype(bf16)
    own = lax.axis_index("node")
    for e in range(ex_ref.shape[0]):
        ex_ref[e] = h_ref[pl.ds(pl.multiple_of(exp_ref[own, e] * BLK, BLK), BLK), :]


def prep_kernel(col_ref, ptr_ref, out_ref):
    far_cap = col_ref.shape[1]
    peers = out_ref.shape[0]
    used = jnp.max(ptr_ref[...], axis=1, keepdims=True)
    out_ref[:, :far_cap] = jnp.broadcast_to(col_ref[...], (peers, far_cap))
    out_ref[:, far_cap:] = jnp.broadcast_to(used, (peers, 1))


def prep(far_col, far_ptr):
    far_cap = far_col.shape[1]
    return pl.pallas_call(
        prep_kernel,
        in_specs=[vmem(), vmem()],
        out_specs=vmem(),
        out_shape=jax.ShapeDtypeStruct((far_cap + 1, far_cap + 1), jnp.int32),
    )(far_col, far_ptr)


def skip_kernel(h_ref, sw_ref, s_ref, ws):
    cw = sw_ref.shape[0]

    @pl.when(pl.program_id(0) == 0)
    def _():
        ws[...] = bd_inkernel(sw_ref[...], CHUNK // cw)

    skip_w = ws.shape[1]
    for j in range(h_ref.shape[1] // CHUNK):
        s_ref[:, j * skip_w : (j + 1) * skip_w] = jnp.dot(
            h_ref[:, j * CHUNK : (j + 1) * CHUNK], ws[...], preferred_element_type=f32
        ).astype(bf16)


def front_hidden(export_block, features, fgw):
    rows, cols = features.shape
    half = cols // 2
    return pl.pallas_call(
        hidden_kernel,
        in_specs=[smem(), vmem(), vmem()],
        out_specs=[vmem(), vmem()],
        out_shape=[
            jax.ShapeDtypeStruct((rows, half), bf16),
            jax.ShapeDtypeStruct((export_block.shape[1], BLK, half), bf16),
        ],
        compiler_params=pltpu.CompilerParams(vmem_limit_bytes=48 * 1024 * 1024),
        cost_estimate=pl.CostEstimate(
            flops=2 * rows * CHUNK * 4 * CHUNK * (half // CHUNK),
            transcendentals=rows * half * 2,
            bytes_accessed=2 * rows * (cols + half),
        ),
    )(export_block, features, fgw)


def front_skip(hidden, skip_weight):
    rows, width = hidden.shape
    chunks = width // CHUNK
    cw, s = skip_weight.shape
    per = CHUNK // cw
    skip_cols = s * per * chunks
    tile = min(ROW_TILE, rows)
    return pl.pallas_call(
        skip_kernel,
        grid=(rows // tile,),
        in_specs=[
            pl.BlockSpec((tile, width), lambda i: (i, 0)),
            pl.BlockSpec(skip_weight.shape, lambda i: (0, 0)),
        ],
        out_specs=pl.BlockSpec((tile, skip_cols), lambda i: (i, 0)),
        out_shape=jax.ShapeDtypeStruct((rows, skip_cols), bf16),
        scratch_shapes=[pltpu.VMEM((CHUNK, s * per), bf16)],
        compiler_params=pltpu.CompilerParams(vmem_limit_bytes=48 * 1024 * 1024),
        cost_estimate=pl.CostEstimate(
            flops=2 * rows * CHUNK * s * per * chunks,
            transcendentals=0,
            bytes_accessed=2 * rows * (CHUNK * chunks + skip_cols),
        ),
    )(hidden, skip_weight)


def fill_pad(field_ref, lo_ref, hi_ref, pad):
    nrows = field_ref.shape[0]
    pad[:BLK, :] = lo_ref[...]
    pad[BLK : BLK + nrows, :] = field_ref[...]
    pad[BLK + nrows :, :] = hi_ref[...]


def band_block(band_ref, pad, t):
    start = pl.multiple_of(t * BLK, BLK)
    return jnp.dot(
        band_ref[pl.ds(start, BLK), :], pad[pl.ds(start, 3 * BLK), :], preferred_element_type=f32
    )


def slot_product(col_ref, farw_ref, arr_ref, k):
    return jnp.dot(farw_ref[k], arr_ref[col_ref[0, k] // EXPORT], preferred_element_type=f32)


def accumulate(col_ref, ptr_ref, field_ref, lo_ref, hi_ref, arr_ref, band_ref, farw_ref, acc, pad):
    nblk = field_ref.shape[0] // BLK
    far_cap = farw_ref.shape[0]
    nptr = ptr_ref.shape[1]
    fill_pad(field_ref, lo_ref, hi_ref, pad)
    for r in range(nblk):
        acc[r * BLK : (r + 1) * BLK, :] = band_block(band_ref, pad, r)
    acc[nblk * BLK :, :] = jnp.zeros((BLK, acc.shape[1]), f32)

    def slot(k, carry):
        row = 0
        for r in range(1, nptr):
            row = row + jnp.where(ptr_ref[0, r] <= k, 1, 0)
        start = pl.multiple_of(row * BLK, BLK)
        acc[pl.ds(start, BLK), :] += slot_product(col_ref, farw_ref, arr_ref, k)
        return carry

    lax.fori_loop(0, far_cap, slot, 0)


def early_kernel(
    col_ref, ptr_ref, req_ref, exp_ref, field_ref, lo_ref, hi_ref, arr_ref, band_ref, farw_ref,
    send_ref, edge_ref, pad, blk,
):
    nblk = field_ref.shape[0] // BLK
    own = lax.axis_index("node")
    fill_pad(field_ref, lo_ref, hi_ref, pad)
    targets = [exp_ref[own, 0], exp_ref[own, 1], 0, nblk - 1]
    for i, t in enumerate(targets):
        v = band_block(band_ref, pad, t)

        def slot(k, acc):
            return acc + slot_product(col_ref, farw_ref, arr_ref, k)

        v = lax.fori_loop(ptr_ref[0, t], ptr_ref[0, t + 1], slot, v)
        blk[i] = v.astype(bf16)

    def body(p, carry):
        send_ref[p] = blk[req_ref[p]]
        return carry

    lax.fori_loop(0, send_ref.shape[0], body, 0)
    edge_ref[0] = blk[2]
    edge_ref[1] = blk[3]


def hop1_kernel(
    col_ref, ptr_ref, field_ref, lo_ref, hi_ref, arr_ref, band_ref, farw_ref, x_hbm, mix_ref,
    out_ref, part_ref, acc2_ref, acc, pad, xs, sems,
):
    nrows, width = field_ref.shape
    nblk = nrows // BLK
    half = x_hbm.shape[1] // 2
    x_copy = pltpu.make_async_copy(x_hbm.at[:, pl.ds(half, width)], xs, sems.at[0])
    x_copy.start()
    accumulate(col_ref, ptr_ref, field_ref, lo_ref, hi_ref, arr_ref, band_ref, farw_ref, acc, pad)
    out_ref[...] = acc[:nrows, :].astype(bf16)
    zero = jnp.zeros((BLK, width), bf16)
    fill_pad(out_ref, zero, zero, pad)
    for r in range(nblk):
        acc2_ref[r * BLK : (r + 1) * BLK, :] = band_block(band_ref, pad, r)
    cw = mix_ref.shape[1]
    per = CHUNK // cw
    mix = mix_ref[...]
    m0 = bd_inkernel(mix[:cw], per)
    m1 = bd_inkernel(mix[cw : 2 * cw], per)
    x_copy.wait()
    for j in range(width // CHUNK):
        cols = slice(j * CHUNK, (j + 1) * CHUNK)
        v = xs[:, cols].astype(f32)
        v = v + jnp.dot(field_ref[:, cols], m0, preferred_element_type=f32)
        v = v + jnp.dot(out_ref[:, cols], m1, preferred_element_type=f32)
        part_ref[:, cols] = v


def hop2_kernel(
    col_ref, ptr_ref, lo_ref, hi_ref, arr_ref, band_ref, farw_ref, acc2_hbm, part_hbm, mix_ref,
    out_ref, far, a2, ps, sems,
):
    nrows, width = out_ref.shape
    nblk = nrows // BLK
    chunks = width // CHUNK
    copies = []
    for j in range(chunks):
        cols = pl.ds(j * CHUNK, CHUNK)
        ca = pltpu.make_async_copy(acc2_hbm.at[:, cols], a2.at[:, cols], sems.at[2 * j])
        cp = pltpu.make_async_copy(part_hbm.at[:, cols], ps.at[:, cols], sems.at[2 * j + 1])
        ca.start()
        cp.start()
        copies.append((ca, cp))
    far[...] = jnp.zeros(far.shape, f32)
    far[:BLK, :] = jnp.dot(band_ref[:BLK, :BLK], lo_ref[...], preferred_element_type=f32)
    last = (nblk - 1) * BLK
    far[last : last + BLK, :] = jnp.dot(
        band_ref[last : last + BLK, 2 * BLK :], hi_ref[...], preferred_element_type=f32
    )
    far_cap = farw_ref.shape[0]
    nptr = ptr_ref.shape[1]

    def slot(k, carry):
        row = 0
        for r in range(1, nptr):
            row = row + jnp.where(ptr_ref[0, r] <= k, 1, 0)
        start = pl.multiple_of(row * BLK, BLK)
        far[pl.ds(start, BLK), :] += slot_product(col_ref, farw_ref, arr_ref, k)
        return carry

    lax.fori_loop(0, far_cap, slot, 0)
    cw = mix_ref.shape[1]
    m2 = bd_inkernel(mix_ref[2 * cw :], CHUNK // cw)
    for j in range(chunks):
        ca, cp = copies[j]
        ca.wait()
        cp.wait()
        cols = slice(j * CHUNK, (j + 1) * CHUNK)
        two = (a2[:, cols] + far[:nrows, cols]).astype(bf16)
        v = ps[:, cols] + jnp.dot(two, m2, preferred_element_type=f32)
        out_ref[:, cols] = v.astype(bf16)


def vmem():
    return pl.BlockSpec(memory_space=pltpu.VMEM)


def smem():
    return pl.BlockSpec(memory_space=pltpu.SMEM)


def hbm():
    return pl.BlockSpec(memory_space=pltpu.HBM)


BIG_VMEM = pltpu.CompilerParams(vmem_limit_bytes=48 * 1024 * 1024)


def scratch(field):
    nrows, width = field.shape
    return [pltpu.VMEM((nrows + BLK, width), f32), pltpu.VMEM((nrows + 2 * BLK, width), bf16)]


def early(far_col, far_ptr, requested, export_block, field, lo, hi, arrived, band, farw3):
    nrows, width = field.shape
    return pl.pallas_call(
        early_kernel,
        in_specs=[smem()] * 4 + [vmem()] * 6,
        out_specs=[vmem(), vmem()],
        out_shape=[
            jax.ShapeDtypeStruct(arrived.shape, bf16),
            jax.ShapeDtypeStruct((2, BLK, width), bf16),
        ],
        scratch_shapes=[pltpu.VMEM((nrows + 2 * BLK, width), bf16), pltpu.VMEM((4, BLK, width), bf16)],
        compiler_params=BIG_VMEM,
        cost_estimate=pl.CostEstimate(
            flops=2 * BLK * BLK * width * (12 + farw3.shape[0]),
            transcendentals=0,
            bytes_accessed=2 * width * (nrows + 2 * arrived.shape[0] * BLK),
        ),
    )(far_col, far_ptr, requested, export_block, field, lo, hi, arrived, band, farw3)


def hop1(far_col, far_ptr, field, lo, hi, arrived, band, farw3, features, mix):
    nrows, width = field.shape
    return pl.pallas_call(
        hop1_kernel,
        in_specs=[smem(), smem()] + [vmem()] * 6 + [hbm(), vmem()],
        out_specs=[vmem(), vmem(), vmem()],
        out_shape=[
            jax.ShapeDtypeStruct((nrows, width), bf16),
            jax.ShapeDtypeStruct((nrows, width), f32),
            jax.ShapeDtypeStruct((nrows, width), f32),
        ],
        scratch_shapes=scratch(field)
        + [pltpu.VMEM((nrows, width), bf16), pltpu.SemaphoreType.DMA((1,))],
        compiler_params=pltpu.CompilerParams(),
        cost_estimate=pl.CostEstimate(
            flops=2 * BLK * BLK * width * (6 * nrows // BLK + farw3.shape[0])
            + 2 * nrows * width * CHUNK * 2,
            transcendentals=0,
            bytes_accessed=2 * width * (nrows * 9 + arrived.shape[0] * BLK),
        ),
    )(far_col, far_ptr, field, lo, hi, arrived, band, farw3, features, mix)


def hop2(far_col, far_ptr, lo, hi, arrived, band, farw3, acc2, part, mix):
    nrows, width = part.shape
    return pl.pallas_call(
        hop2_kernel,
        in_specs=[smem(), smem()] + [vmem()] * 5 + [hbm(), hbm(), vmem()],
        out_specs=vmem(),
        out_shape=jax.ShapeDtypeStruct((nrows, width), bf16),
        scratch_shapes=[
            pltpu.VMEM((nrows + BLK, width), f32),
            pltpu.VMEM((nrows, width), f32),
            pltpu.VMEM((nrows, width), f32),
            pltpu.SemaphoreType.DMA((2 * (width // CHUNK),)),
        ],
        compiler_params=pltpu.CompilerParams(),
        cost_estimate=pl.CostEstimate(
            flops=2 * BLK * BLK * width * (farw3.shape[0] + 2) + 2 * nrows * width * CHUNK,
            transcendentals=0,
            bytes_accessed=4 * width * nrows * 3,
        ),
    )(far_col, far_ptr, lo, hi, arrived, band, farw3, acc2, part, mix)


def halo(first, last):
    count = lax.axis_size("node")
    forward = [(i, i + 1) for i in range(count - 1)]
    backward = [(t, s) for s, t in forward]
    lo = lax.ppermute(last, "node", forward)
    hi = lax.ppermute(first, "node", backward)
    return lo, hi


def local(
    features,
    filter_gate_weight,
    skip_weight,
    mix_weight,
    band_weight,
    far_weight,
    far_ptr,
    far_col,
    export_block,
):
    node_rows = features.shape[0]
    blocks = node_rows // BLK
    far_cap = far_col.shape[1]

    own_index = lax.axis_index("node")
    own_exports = lax.dynamic_slice_in_dim(export_block, own_index, 1, 0)[0].astype(jnp.int32)
    peer_count = far_cap + 1
    info_all = lax.all_to_all(prep(far_col, far_ptr), "node", split_axis=0, concat_axis=0, tiled=True)
    slot_ids = jnp.arange(far_cap, dtype=jnp.int32)
    cols_all = info_all[:, :far_cap]
    hits = (cols_all // EXPORT == own_index) & (slot_ids[None, :] < info_all[:, far_cap:])
    requested = jnp.sum(jnp.where(hits, cols_all % EXPORT, 0), axis=1).astype(jnp.int32)
    hidden, ex2 = front_hidden(export_block, features, filter_gate_weight)
    blocks = node_rows // BLK
    width = hidden.shape[1]
    farw3 = far_weight.reshape(BLK, far_cap, BLK).transpose(1, 0, 2)

    def exchange(send):
        return lax.all_to_all(send, "node", split_axis=0, concat_axis=0, tiled=True)

    arrived1 = exchange(jnp.where((requested == 0)[:, None, None], ex2[0][None], ex2[1][None]))
    lo1, hi1 = halo(hidden[:BLK], hidden[node_rows - BLK :])
    skip_out = front_skip(hidden, skip_weight)
    send2, edge = early(
        far_col, far_ptr, requested, export_block, hidden, lo1, hi1, arrived1, band_weight, farw3
    )
    arrived2 = exchange(send2)
    lo2, hi2 = halo(edge[0], edge[1])
    hop_one, part, acc2 = hop1(
        far_col, far_ptr, hidden, lo1, hi1, arrived1, band_weight, farw3, features, mix_weight
    )
    residual = hop2(
        far_col, far_ptr, lo2, hi2, arrived2, band_weight, farw3, acc2, part, mix_weight
    )
    return residual, skip_out


def solution(mesh):
    placed = (
        P(("groups", "node"), None),
        P(),
        P(),
        P(),
        P("node", None),
        P(None, "node"),
        P("node", None),
        P("node", None),
        P(),
    )
    return jax.shard_map(
        local,
        mesh=mesh,
        in_specs=placed,
        out_specs=(P(("groups", "node"), None), P(("groups", "node"), None)),
        check_vma=False,
    )
```

```python
import functools

import jax
import jax.numpy as jnp
from jax import lax
from jax.experimental import pallas as pl
from jax.experimental.pallas import tpu as pltpu
from jax.sharding import PartitionSpec as P

BLK = 64
TOUT = 16
DILATION_STEP = 16
EXPORT = 2
CHANNEL_WIDTH = 32
S = 256
TIN = 32
CHUNK = 256
ROW_TILE = 256

f32 = jnp.float32
bf16 = jnp.bfloat16


def bd_inkernel(w, reps):
    r, c = w.shape
    shape_r = (reps * r, r)
    rep_r = jnp.where(
        lax.broadcasted_iota(jnp.int32, shape_r, 0) % r == lax.broadcasted_iota(jnp.int32, shape_r, 1),
        1.0, 0.0,
    ).astype(bf16)
    shape_c = (c, reps * c)
    rep_c = jnp.where(
        lax.broadcasted_iota(jnp.int32, shape_c, 1) % c == lax.broadcasted_iota(jnp.int32, shape_c, 0),
        1.0, 0.0,
    ).astype(bf16)
    rows = jnp.dot(rep_r, w, preferred_element_type=f32).astype(bf16)
    tiled = jnp.dot(rows, rep_c, preferred_element_type=f32)
    shape = tiled.shape
    mask = lax.broadcasted_iota(jnp.int32, shape, 0) // r == lax.broadcasted_iota(jnp.int32, shape, 1) // c
    return jnp.where(mask, tiled, 0.0).astype(bf16)


def hidden_kernel(exp_ref, x_ref, fgw_ref, h_ref, ex_ref):
    rows, cols = x_ref.shape
    half = cols // 2
    cw = fgw_ref.shape[0] // 2
    per = CHUNK // cw
    w = fgw_ref[...]
    wlo = jnp.concatenate([bd_inkernel(w[:cw, :cw], per), bd_inkernel(w[:cw, cw:], per)], axis=1)
    whi = jnp.concatenate([bd_inkernel(w[cw:, :cw], per), bd_inkernel(w[cw:, cw:], per)], axis=1)
    tile = min(ROW_TILE, rows)
    for t in range(rows // tile):
        rs = slice(t * tile, (t + 1) * tile)
        for j in range(half // CHUNK):
            x0 = x_ref[rs, j * CHUNK : (j + 1) * CHUNK]
            x1 = x_ref[rs, half + j * CHUNK : half + (j + 1) * CHUNK]
            pre = jnp.dot(x0, wlo, preferred_element_type=f32)
            pre = pre + jnp.dot(x1, whi, preferred_element_type=f32)
            h_ref[rs, j * CHUNK : (j + 1) * CHUNK] = (
                jnp.tanh(pre[:, :CHUNK]) * jax.nn.sigmoid(pre[:, CHUNK:])
            ).astype(bf16)
    own = lax.axis_index("node")
    for e in range(ex_ref.shape[0]):
        ex_ref[e] = h_ref[pl.ds(pl.multiple_of(exp_ref[own, e] * BLK, BLK), BLK), :]


def prep_kernel(col_ref, ptr_ref, out_ref):
    far_cap = col_ref.shape[1]
    peers = out_ref.shape[0]
    used = jnp.max(ptr_ref[...], axis=1, keepdims=True)
    out_ref[:, :far_cap] = jnp.broadcast_to(col_ref[...], (peers, far_cap))
    out_ref[:, far_cap:] = jnp.broadcast_to(used, (peers, 1))


def prep(far_col, far_ptr):
    far_cap = far_col.shape[1]
    return pl.pallas_call(
        prep_kernel,
        in_specs=[vmem(), vmem()],
        out_specs=vmem(),
        out_shape=jax.ShapeDtypeStruct((far_cap + 1, far_cap + 1), jnp.int32),
    )(far_col, far_ptr)


def skip_kernel(h_ref, sw_ref, s_ref, ws):
    cw = sw_ref.shape[0]

    @pl.when(pl.program_id(0) == 0)
    def _():
        ws[...] = bd_inkernel(sw_ref[...], CHUNK // cw)

    skip_w = ws.shape[1]
    for j in range(h_ref.shape[1] // CHUNK):
        s_ref[:, j * skip_w : (j + 1) * skip_w] = jnp.dot(
            h_ref[:, j * CHUNK : (j + 1) * CHUNK], ws[...], preferred_element_type=f32
        ).astype(bf16)


def front_hidden(export_block, features, fgw):
    rows, cols = features.shape
    half = cols // 2
    return pl.pallas_call(
        hidden_kernel,
        in_specs=[smem(), vmem(), vmem()],
        out_specs=[vmem(), vmem()],
        out_shape=[
            jax.ShapeDtypeStruct((rows, half), bf16),
            jax.ShapeDtypeStruct((export_block.shape[1], BLK, half), bf16),
        ],
        compiler_params=pltpu.CompilerParams(vmem_limit_bytes=48 * 1024 * 1024),
        cost_estimate=pl.CostEstimate(
            flops=2 * rows * CHUNK * 4 * CHUNK * (half // CHUNK),
            transcendentals=rows * half * 2,
            bytes_accessed=2 * rows * (cols + half),
        ),
    )(export_block, features, fgw)


def front_skip(hidden, skip_weight):
    rows, width = hidden.shape
    chunks = width // CHUNK
    cw, s = skip_weight.shape
    per = CHUNK // cw
    skip_cols = s * per * chunks
    tile = min(ROW_TILE, rows)
    return pl.pallas_call(
        skip_kernel,
        grid=(rows // tile,),
        in_specs=[
            pl.BlockSpec((tile, width), lambda i: (i, 0)),
            pl.BlockSpec(skip_weight.shape, lambda i: (0, 0)),
        ],
        out_specs=pl.BlockSpec((tile, skip_cols), lambda i: (i, 0)),
        out_shape=jax.ShapeDtypeStruct((rows, skip_cols), bf16),
        scratch_shapes=[pltpu.VMEM((CHUNK, s * per), bf16)],
        compiler_params=pltpu.CompilerParams(vmem_limit_bytes=48 * 1024 * 1024),
        cost_estimate=pl.CostEstimate(
            flops=2 * rows * CHUNK * s * per * chunks,
            transcendentals=0,
            bytes_accessed=2 * rows * (CHUNK * chunks + skip_cols),
        ),
    )(hidden, skip_weight)


def fill_pad(field_ref, lo_ref, hi_ref, pad):
    nrows = field_ref.shape[0]
    pad[:BLK, :] = lo_ref[...]
    pad[BLK : BLK + nrows, :] = field_ref[...]
    pad[BLK + nrows :, :] = hi_ref[...]


def band_block(band_ref, pad, t):
    start = pl.multiple_of(t * BLK, BLK)
    return jnp.dot(
        band_ref[pl.ds(start, BLK), :], pad[pl.ds(start, 3 * BLK), :], preferred_element_type=f32
    )


def slot_product(col_ref, farw_ref, arr_ref, k):
    return jnp.dot(farw_ref[k], arr_ref[col_ref[0, k] // EXPORT], preferred_element_type=f32)


def accumulate(col_ref, ptr_ref, field_ref, lo_ref, hi_ref, arr_ref, band_ref, farw_ref, acc, pad):
    nblk = field_ref.shape[0] // BLK
    far_cap = farw_ref.shape[0]
    nptr = ptr_ref.shape[1]
    fill_pad(field_ref, lo_ref, hi_ref, pad)
    for r in range(nblk):
        acc[r * BLK : (r + 1) * BLK, :] = band_block(band_ref, pad, r)
    acc[nblk * BLK :, :] = jnp.zeros((BLK, acc.shape[1]), f32)

    def slot(k, carry):
        row = 0
        for r in range(1, nptr):
            row = row + jnp.where(ptr_ref[0, r] <= k, 1, 0)
        start = pl.multiple_of(row * BLK, BLK)
        acc[pl.ds(start, BLK), :] += slot_product(col_ref, farw_ref, arr_ref, k)
        return carry

    lax.fori_loop(0, far_cap, slot, 0)


def early_kernel(
    col_ref, ptr_ref, req_ref, exp_ref, field_ref, lo_ref, hi_ref, arr_ref, band_ref, farw_ref,
    send_ref, edge_ref, pad, blk, sems,
):
    nblk = field_ref.shape[0] // BLK
    own = lax.axis_index("node")
    fill_pad(field_ref, lo_ref, hi_ref, pad)
    targets = [exp_ref[own, 0], exp_ref[own, 1], 0, nblk - 1]
    for i, t in enumerate(targets):
        v = band_block(band_ref, pad, t)

        def slot(k, acc):
            return acc + slot_product(col_ref, farw_ref, arr_ref, k)

        v = lax.fori_loop(ptr_ref[0, t], ptr_ref[0, t + 1], slot, v)
        blk[i] = v.astype(bf16)

    def body(p, carry):
        pltpu.make_async_copy(blk.at[req_ref[p]], send_ref.at[p], sems.at[p]).start()
        return carry

    lax.fori_loop(0, send_ref.shape[0], body, 0)
    edge_ref[0] = blk[2]
    edge_ref[1] = blk[3]

    def finish(p, carry):
        pltpu.make_async_copy(blk.at[req_ref[p]], send_ref.at[p], sems.at[p]).wait()
        return carry

    lax.fori_loop(0, send_ref.shape[0], finish, 0)


def hop1_kernel(
    col_ref, ptr_ref, field_ref, lo_ref, hi_ref, arr_ref, band_ref, farw_ref, x_hbm, mix_ref,
    out_ref, part_ref, acc2_ref, acc, pad, xs, sems,
):
    nrows, width = field_ref.shape
    nblk = nrows // BLK
    half = x_hbm.shape[1] // 2
    x_copy = pltpu.make_async_copy(x_hbm.at[:, pl.ds(half, width)], xs, sems.at[0])
    x_copy.start()
    accumulate(col_ref, ptr_ref, field_ref, lo_ref, hi_ref, arr_ref, band_ref, farw_ref, acc, pad)
    out_ref[...] = acc[:nrows, :].astype(bf16)
    zero = jnp.zeros((BLK, width), bf16)
    fill_pad(out_ref, zero, zero, pad)
    for r in range(nblk):
        acc2_ref[r * BLK : (r + 1) * BLK, :] = band_block(band_ref, pad, r)
    cw = mix_ref.shape[1]
    per = CHUNK // cw
    mix = mix_ref[...]
    m0 = bd_inkernel(mix[:cw], per)
    m1 = bd_inkernel(mix[cw : 2 * cw], per)
    x_copy.wait()
    for j in range(width // CHUNK):
        cols = slice(j * CHUNK, (j + 1) * CHUNK)
        v = xs[:, cols].astype(f32)
        v = v + jnp.dot(field_ref[:, cols], m0, preferred_element_type=f32)
        v = v + jnp.dot(out_ref[:, cols], m1, preferred_element_type=f32)
        part_ref[:, cols] = v


def hop2_kernel(
    col_ref, ptr_ref, lo_ref, hi_ref, arr_ref, band_ref, farw_ref, acc2_hbm, part_hbm, mix_ref,
    out_ref, far, a2, ps, sems,
):
    nrows, width = out_ref.shape
    nblk = nrows // BLK
    chunks = width // CHUNK
    copies = []
    for j in range(chunks):
        cols = pl.ds(j * CHUNK, CHUNK)
        ca = pltpu.make_async_copy(acc2_hbm.at[:, cols], a2.at[:, cols], sems.at[2 * j])
        cp = pltpu.make_async_copy(part_hbm.at[:, cols], ps.at[:, cols], sems.at[2 * j + 1])
        ca.start()
        cp.start()
        copies.append((ca, cp))
    far[...] = jnp.zeros(far.shape, f32)
    far[:BLK, :] = jnp.dot(band_ref[:BLK, :BLK], lo_ref[...], preferred_element_type=f32)
    last = (nblk - 1) * BLK
    far[last : last + BLK, :] = jnp.dot(
        band_ref[last : last + BLK, 2 * BLK :], hi_ref[...], preferred_element_type=f32
    )
    far_cap = farw_ref.shape[0]
    nptr = ptr_ref.shape[1]

    def slot(k, carry):
        row = 0
        for r in range(1, nptr):
            row = row + jnp.where(ptr_ref[0, r] <= k, 1, 0)
        start = pl.multiple_of(row * BLK, BLK)
        far[pl.ds(start, BLK), :] += slot_product(col_ref, farw_ref, arr_ref, k)
        return carry

    lax.fori_loop(0, far_cap, slot, 0)
    cw = mix_ref.shape[1]
    m2 = bd_inkernel(mix_ref[2 * cw :], CHUNK // cw)
    for j in range(chunks):
        ca, cp = copies[j]
        ca.wait()
        cp.wait()
        cols = slice(j * CHUNK, (j + 1) * CHUNK)
        two = (a2[:, cols] + far[:nrows, cols]).astype(bf16)
        v = ps[:, cols] + jnp.dot(two, m2, preferred_element_type=f32)
        out_ref[:, cols] = v.astype(bf16)


def vmem():
    return pl.BlockSpec(memory_space=pltpu.VMEM)


def smem():
    return pl.BlockSpec(memory_space=pltpu.SMEM)


def hbm():
    return pl.BlockSpec(memory_space=pltpu.HBM)


BIG_VMEM = pltpu.CompilerParams(vmem_limit_bytes=48 * 1024 * 1024)


def scratch(field):
    nrows, width = field.shape
    return [pltpu.VMEM((nrows + BLK, width), f32), pltpu.VMEM((nrows + 2 * BLK, width), bf16)]


def early(far_col, far_ptr, requested, export_block, field, lo, hi, arrived, band, farw3):
    nrows, width = field.shape
    return pl.pallas_call(
        early_kernel,
        in_specs=[smem()] * 4 + [vmem()] * 6,
        out_specs=[hbm(), vmem()],
        out_shape=[
            jax.ShapeDtypeStruct(arrived.shape, bf16),
            jax.ShapeDtypeStruct((2, BLK, width), bf16),
        ],
        scratch_shapes=[
            pltpu.VMEM((nrows + 2 * BLK, width), bf16),
            pltpu.VMEM((4, BLK, width), bf16),
            pltpu.SemaphoreType.DMA((arrived.shape[0],)),
        ],
        compiler_params=pltpu.CompilerParams(),
        cost_estimate=pl.CostEstimate(
            flops=2 * BLK * BLK * width * (12 + farw3.shape[0]),
            transcendentals=0,
            bytes_accessed=2 * width * (nrows + 2 * arrived.shape[0] * BLK),
        ),
    )(far_col, far_ptr, requested, export_block, field, lo, hi, arrived, band, farw3)


def hop1(far_col, far_ptr, field, lo, hi, arrived, band, farw3, features, mix):
    nrows, width = field.shape
    return pl.pallas_call(
        hop1_kernel,
        in_specs=[smem(), smem()] + [vmem()] * 6 + [hbm(), vmem()],
        out_specs=[vmem(), vmem(), vmem()],
        out_shape=[
            jax.ShapeDtypeStruct((nrows, width), bf16),
            jax.ShapeDtypeStruct((nrows, width), f32),
            jax.ShapeDtypeStruct((nrows, width), f32),
        ],
        scratch_shapes=scratch(field)
        + [pltpu.VMEM((nrows, width), bf16), pltpu.SemaphoreType.DMA((1,))],
        compiler_params=pltpu.CompilerParams(),
        cost_estimate=pl.CostEstimate(
            flops=2 * BLK * BLK * width * (6 * nrows // BLK + farw3.shape[0])
            + 2 * nrows * width * CHUNK * 2,
            transcendentals=0,
            bytes_accessed=2 * width * (nrows * 9 + arrived.shape[0] * BLK),
        ),
    )(far_col, far_ptr, field, lo, hi, arrived, band, farw3, features, mix)


def hop2(far_col, far_ptr, lo, hi, arrived, band, farw3, acc2, part, mix):
    nrows, width = part.shape
    return pl.pallas_call(
        hop2_kernel,
        in_specs=[smem(), smem()] + [vmem()] * 5 + [hbm(), hbm(), vmem()],
        out_specs=vmem(),
        out_shape=jax.ShapeDtypeStruct((nrows, width), bf16),
        scratch_shapes=[
            pltpu.VMEM((nrows + BLK, width), f32),
            pltpu.VMEM((nrows, width), f32),
            pltpu.VMEM((nrows, width), f32),
            pltpu.SemaphoreType.DMA((2 * (width // CHUNK),)),
        ],
        compiler_params=pltpu.CompilerParams(),
        cost_estimate=pl.CostEstimate(
            flops=2 * BLK * BLK * width * (farw3.shape[0] + 2) + 2 * nrows * width * CHUNK,
            transcendentals=0,
            bytes_accessed=4 * width * nrows * 3,
        ),
    )(far_col, far_ptr, lo, hi, arrived, band, farw3, acc2, part, mix)


def halo(first, last):
    count = lax.axis_size("node")
    forward = [(i, i + 1) for i in range(count - 1)]
    backward = [(t, s) for s, t in forward]
    lo = lax.ppermute(last, "node", forward)
    hi = lax.ppermute(first, "node", backward)
    return lo, hi


def local(
    features,
    filter_gate_weight,
    skip_weight,
    mix_weight,
    band_weight,
    far_weight,
    far_ptr,
    far_col,
    export_block,
):
    node_rows = features.shape[0]
    blocks = node_rows // BLK
    far_cap = far_col.shape[1]

    own_index = lax.axis_index("node")
    own_exports = lax.dynamic_slice_in_dim(export_block, own_index, 1, 0)[0].astype(jnp.int32)
    peer_count = far_cap + 1
    info_all = lax.all_to_all(prep(far_col, far_ptr), "node", split_axis=0, concat_axis=0, tiled=True)
    slot_ids = jnp.arange(far_cap, dtype=jnp.int32)
    cols_all = info_all[:, :far_cap]
    hits = (cols_all // EXPORT == own_index) & (slot_ids[None, :] < info_all[:, far_cap:])
    requested = jnp.sum(jnp.where(hits, cols_all % EXPORT, 0), axis=1).astype(jnp.int32)
    hidden, ex2 = front_hidden(export_block, features, filter_gate_weight)
    blocks = node_rows // BLK
    width = hidden.shape[1]
    farw3 = far_weight.reshape(BLK, far_cap, BLK).transpose(1, 0, 2)

    def exchange(send):
        return lax.all_to_all(send, "node", split_axis=0, concat_axis=0, tiled=True)

    arrived1 = exchange(jnp.where((requested == 0)[:, None, None], ex2[0][None], ex2[1][None]))
    lo1, hi1 = halo(hidden[:BLK], hidden[node_rows - BLK :])
    skip_out = front_skip(hidden, skip_weight)
    send2, edge = early(
        far_col, far_ptr, requested, export_block, hidden, lo1, hi1, arrived1, band_weight, farw3
    )
    arrived2 = exchange(send2)
    lo2, hi2 = halo(edge[0], edge[1])
    hop_one, part, acc2 = hop1(
        far_col, far_ptr, hidden, lo1, hi1, arrived1, band_weight, farw3, features, mix_weight
    )
    residual = hop2(
        far_col, far_ptr, lo2, hi2, arrived2, band_weight, farw3, acc2, part, mix_weight
    )
    return residual, skip_out


def solution(mesh):
    placed = (
        P(("groups", "node"), None),
        P(),
        P(),
        P(),
        P("node", None),
        P(None, "node"),
        P("node", None),
        P("node", None),
        P(),
    )
    return jax.shard_map(
        local,
        mesh=mesh,
        in_specs=placed,
        out_specs=(P(("groups", "node"), None), P(("groups", "node"), None)),
        check_vma=False,
    )
```

```python
import functools

import jax
import jax.numpy as jnp
from jax import lax
from jax.experimental import pallas as pl
from jax.experimental.pallas import tpu as pltpu
from jax.sharding import PartitionSpec as P

BLK = 64
TOUT = 16
DILATION_STEP = 16
EXPORT = 2
CHANNEL_WIDTH = 32
S = 256
TIN = 32
CHUNK = 256
ROW_TILE = 256

f32 = jnp.float32
bf16 = jnp.bfloat16


def bd_inkernel(w, reps):
    r, c = w.shape
    shape_r = (reps * r, r)
    rep_r = jnp.where(
        lax.broadcasted_iota(jnp.int32, shape_r, 0) % r == lax.broadcasted_iota(jnp.int32, shape_r, 1),
        1.0, 0.0,
    ).astype(bf16)
    shape_c = (c, reps * c)
    rep_c = jnp.where(
        lax.broadcasted_iota(jnp.int32, shape_c, 1) % c == lax.broadcasted_iota(jnp.int32, shape_c, 0),
        1.0, 0.0,
    ).astype(bf16)
    rows = jnp.dot(rep_r, w, preferred_element_type=f32).astype(bf16)
    tiled = jnp.dot(rows, rep_c, preferred_element_type=f32)
    shape = tiled.shape
    mask = lax.broadcasted_iota(jnp.int32, shape, 0) // r == lax.broadcasted_iota(jnp.int32, shape, 1) // c
    return jnp.where(mask, tiled, 0.0).astype(bf16)


def hidden_kernel(exp_ref, x_hbm, fgw_ref, h_ref, ex_ref, xbuf, sems):
    rows, cols = x_hbm.shape
    half = cols // 2
    cw = fgw_ref.shape[0] // 2
    per = CHUNK // cw
    tile = min(ROW_TILE, rows)
    tiles = rows // tile

    def load(t):
        return pltpu.make_async_copy(
            x_hbm.at[pl.ds(t * tile, tile)], xbuf.at[t % 2], sems.at[t % 2]
        )

    load(0).start()
    w = fgw_ref[...]
    wlo = jnp.concatenate([bd_inkernel(w[:cw, :cw], per), bd_inkernel(w[:cw, cw:], per)], axis=1)
    whi = jnp.concatenate([bd_inkernel(w[cw:, :cw], per), bd_inkernel(w[cw:, cw:], per)], axis=1)
    for t in range(tiles):
        if t + 1 < tiles:
            load(t + 1).start()
        load(t).wait()
        x_ref = xbuf.at[t % 2]
        rs = slice(t * tile, (t + 1) * tile)
        for j in range(half // CHUNK):
            x0 = x_ref[:, j * CHUNK : (j + 1) * CHUNK]
            x1 = x_ref[:, half + j * CHUNK : half + (j + 1) * CHUNK]
            pre = jnp.dot(x0, wlo, preferred_element_type=f32)
            pre = pre + jnp.dot(x1, whi, preferred_element_type=f32)
            h_ref[rs, j * CHUNK : (j + 1) * CHUNK] = (
                jnp.tanh(pre[:, :CHUNK]) * jax.nn.sigmoid(pre[:, CHUNK:])
            ).astype(bf16)
    own = lax.axis_index("node")
    for e in range(ex_ref.shape[0]):
        ex_ref[e] = h_ref[pl.ds(pl.multiple_of(exp_ref[own, e] * BLK, BLK), BLK), :]


def prep_kernel(col_ref, ptr_ref, out_ref):
    far_cap = col_ref.shape[1]
    peers = out_ref.shape[0]
    used = jnp.max(ptr_ref[...], axis=1, keepdims=True)
    out_ref[:, :far_cap] = jnp.broadcast_to(col_ref[...], (peers, far_cap))
    out_ref[:, far_cap:] = jnp.broadcast_to(used, (peers, 1))


def prep(far_col, far_ptr):
    far_cap = far_col.shape[1]
    return pl.pallas_call(
        prep_kernel,
        in_specs=[vmem(), vmem()],
        out_specs=vmem(),
        out_shape=jax.ShapeDtypeStruct((far_cap + 1, far_cap + 1), jnp.int32),
    )(far_col, far_ptr)


def skip_kernel(h_ref, sw_ref, s_ref, ws):
    cw = sw_ref.shape[0]

    @pl.when(pl.program_id(0) == 0)
    def _():
        ws[...] = bd_inkernel(sw_ref[...], CHUNK // cw)

    skip_w = ws.shape[1]
    for j in range(h_ref.shape[1] // CHUNK):
        s_ref[:, j * skip_w : (j + 1) * skip_w] = jnp.dot(
            h_ref[:, j * CHUNK : (j + 1) * CHUNK], ws[...], preferred_element_type=f32
        ).astype(bf16)


def front_hidden(export_block, features, fgw):
    rows, cols = features.shape
    half = cols // 2
    return pl.pallas_call(
        hidden_kernel,
        in_specs=[smem(), hbm(), vmem()],
        out_specs=[vmem(), vmem()],
        out_shape=[
            jax.ShapeDtypeStruct((rows, half), bf16),
            jax.ShapeDtypeStruct((export_block.shape[1], BLK, half), bf16),
        ],
        scratch_shapes=[
            pltpu.VMEM((2, min(ROW_TILE, rows), cols), bf16),
            pltpu.SemaphoreType.DMA((2,)),
        ],
        compiler_params=pltpu.CompilerParams(),
        cost_estimate=pl.CostEstimate(
            flops=2 * rows * CHUNK * 4 * CHUNK * (half // CHUNK),
            transcendentals=rows * half * 2,
            bytes_accessed=2 * rows * (cols + half),
        ),
    )(export_block, features, fgw)


def front_skip(hidden, skip_weight):
    rows, width = hidden.shape
    chunks = width // CHUNK
    cw, s = skip_weight.shape
    per = CHUNK // cw
    skip_cols = s * per * chunks
    tile = min(ROW_TILE, rows)
    return pl.pallas_call(
        skip_kernel,
        grid=(rows // tile,),
        in_specs=[
            pl.BlockSpec((tile, width), lambda i: (i, 0)),
            pl.BlockSpec(skip_weight.shape, lambda i: (0, 0)),
        ],
        out_specs=pl.BlockSpec((tile, skip_cols), lambda i: (i, 0)),
        out_shape=jax.ShapeDtypeStruct((rows, skip_cols), bf16),
        scratch_shapes=[pltpu.VMEM((CHUNK, s * per), bf16)],
        compiler_params=pltpu.CompilerParams(vmem_limit_bytes=48 * 1024 * 1024),
        cost_estimate=pl.CostEstimate(
            flops=2 * rows * CHUNK * s * per * chunks,
            transcendentals=0,
            bytes_accessed=2 * rows * (CHUNK * chunks + skip_cols),
        ),
    )(hidden, skip_weight)


def fill_pad(field_ref, lo_ref, hi_ref, pad):
    nrows = field_ref.shape[0]
    pad[:BLK, :] = lo_ref[...]
    pad[BLK : BLK + nrows, :] = field_ref[...]
    pad[BLK + nrows :, :] = hi_ref[...]


def band_block(band_ref, pad, t):
    start = pl.multiple_of(t * BLK, BLK)
    return jnp.dot(
        band_ref[pl.ds(start, BLK), :], pad[pl.ds(start, 3 * BLK), :], preferred_element_type=f32
    )


def slot_product(col_ref, farw_ref, arr_ref, k):
    return jnp.dot(farw_ref[k], arr_ref[col_ref[0, k] // EXPORT], preferred_element_type=f32)


def accumulate(col_ref, ptr_ref, field_ref, lo_ref, hi_ref, arr_ref, band_ref, farw_ref, acc, pad):
    nblk = field_ref.shape[0] // BLK
    far_cap = farw_ref.shape[0]
    nptr = ptr_ref.shape[1]
    fill_pad(field_ref, lo_ref, hi_ref, pad)
    for r in range(nblk):
        acc[r * BLK : (r + 1) * BLK, :] = band_block(band_ref, pad, r)
    acc[nblk * BLK :, :] = jnp.zeros((BLK, acc.shape[1]), f32)

    def slot(k, carry):
        row = 0
        for r in range(1, nptr):
            row = row + jnp.where(ptr_ref[0, r] <= k, 1, 0)
        start = pl.multiple_of(row * BLK, BLK)
        acc[pl.ds(start, BLK), :] += slot_product(col_ref, farw_ref, arr_ref, k)
        return carry

    lax.fori_loop(0, far_cap, slot, 0)


def early_kernel(
    col_ref, ptr_ref, req_ref, exp_ref, field_ref, lo_ref, hi_ref, arr_ref, band_ref, farw_ref,
    send_ref, edge_ref, pad, blk,
):
    nblk = field_ref.shape[0] // BLK
    own = lax.axis_index("node")
    fill_pad(field_ref, lo_ref, hi_ref, pad)
    targets = [exp_ref[own, 0], exp_ref[own, 1], 0, nblk - 1]
    for i, t in enumerate(targets):
        v = band_block(band_ref, pad, t)

        def slot(k, acc):
            return acc + slot_product(col_ref, farw_ref, arr_ref, k)

        v = lax.fori_loop(ptr_ref[0, t], ptr_ref[0, t + 1], slot, v)
        blk[i] = v.astype(bf16)

    def body(p, carry):
        send_ref[p] = blk[req_ref[p]]
        return carry

    lax.fori_loop(0, send_ref.shape[0], body, 0)
    edge_ref[0] = blk[2]
    edge_ref[1] = blk[3]


def hop1_kernel(
    col_ref, ptr_ref, field_ref, lo_ref, hi_ref, arr_ref, band_ref, farw_ref, x_hbm, mix_ref,
    out_ref, part_ref, acc2_ref, acc, pad, xs, sems,
):
    nrows, width = field_ref.shape
    nblk = nrows // BLK
    half = x_hbm.shape[1] // 2
    x_copy = pltpu.make_async_copy(x_hbm.at[:, pl.ds(half, width)], xs, sems.at[0])
    x_copy.start()
    accumulate(col_ref, ptr_ref, field_ref, lo_ref, hi_ref, arr_ref, band_ref, farw_ref, acc, pad)
    out_ref[...] = acc[:nrows, :].astype(bf16)
    zero = jnp.zeros((BLK, width), bf16)
    fill_pad(out_ref, zero, zero, pad)
    for r in range(nblk):
        acc2_ref[r * BLK : (r + 1) * BLK, :] = band_block(band_ref, pad, r)
    cw = mix_ref.shape[1]
    per = CHUNK // cw
    mix = mix_ref[...]
    m0 = bd_inkernel(mix[:cw], per)
    m1 = bd_inkernel(mix[cw : 2 * cw], per)
    x_copy.wait()
    for j in range(width // CHUNK):
        cols = slice(j * CHUNK, (j + 1) * CHUNK)
        v = xs[:, cols].astype(f32)
        v = v + jnp.dot(field_ref[:, cols], m0, preferred_element_type=f32)
        v = v + jnp.dot(out_ref[:, cols], m1, preferred_element_type=f32)
        part_ref[:, cols] = v


def hop2_kernel(
    col_ref, ptr_ref, lo_ref, hi_ref, arr_ref, band_ref, farw_ref, acc2_hbm, part_hbm, mix_ref,
    out_ref, far, a2, ps, sems,
):
    nrows, width = out_ref.shape
    nblk = nrows // BLK
    chunks = width // CHUNK
    copies = []
    for j in range(chunks):
        cols = pl.ds(j * CHUNK, CHUNK)
        ca = pltpu.make_async_copy(acc2_hbm.at[:, cols], a2.at[:, cols], sems.at[2 * j])
        cp = pltpu.make_async_copy(part_hbm.at[:, cols], ps.at[:, cols], sems.at[2 * j + 1])
        ca.start()
        cp.start()
        copies.append((ca, cp))
    far[...] = jnp.zeros(far.shape, f32)
    far[:BLK, :] = jnp.dot(band_ref[:BLK, :BLK], lo_ref[...], preferred_element_type=f32)
    last = (nblk - 1) * BLK
    far[last : last + BLK, :] = jnp.dot(
        band_ref[last : last + BLK, 2 * BLK :], hi_ref[...], preferred_element_type=f32
    )
    far_cap = farw_ref.shape[0]
    nptr = ptr_ref.shape[1]

    def slot(k, carry):
        row = 0
        for r in range(1, nptr):
            row = row + jnp.where(ptr_ref[0, r] <= k, 1, 0)
        start = pl.multiple_of(row * BLK, BLK)
        far[pl.ds(start, BLK), :] += slot_product(col_ref, farw_ref, arr_ref, k)
        return carry

    lax.fori_loop(0, far_cap, slot, 0)
    cw = mix_ref.shape[1]
    m2 = bd_inkernel(mix_ref[2 * cw :], CHUNK // cw)
    for j in range(chunks):
        ca, cp = copies[j]
        ca.wait()
        cp.wait()
        cols = slice(j * CHUNK, (j + 1) * CHUNK)
        two = (a2[:, cols] + far[:nrows, cols]).astype(bf16)
        v = ps[:, cols] + jnp.dot(two, m2, preferred_element_type=f32)
        out_ref[:, cols] = v.astype(bf16)


def vmem():
    return pl.BlockSpec(memory_space=pltpu.VMEM)


def smem():
    return pl.BlockSpec(memory_space=pltpu.SMEM)


def hbm():
    return pl.BlockSpec(memory_space=pltpu.HBM)


BIG_VMEM = pltpu.CompilerParams(vmem_limit_bytes=48 * 1024 * 1024)


def scratch(field):
    nrows, width = field.shape
    return [pltpu.VMEM((nrows + BLK, width), f32), pltpu.VMEM((nrows + 2 * BLK, width), bf16)]


def early(far_col, far_ptr, requested, export_block, field, lo, hi, arrived, band, farw3):
    nrows, width = field.shape
    return pl.pallas_call(
        early_kernel,
        in_specs=[smem()] * 4 + [vmem()] * 6,
        out_specs=[vmem(), vmem()],
        out_shape=[
            jax.ShapeDtypeStruct(arrived.shape, bf16),
            jax.ShapeDtypeStruct((2, BLK, width), bf16),
        ],
        scratch_shapes=[pltpu.VMEM((nrows + 2 * BLK, width), bf16), pltpu.VMEM((4, BLK, width), bf16)],
        compiler_params=BIG_VMEM,
        cost_estimate=pl.CostEstimate(
            flops=2 * BLK * BLK * width * (12 + farw3.shape[0]),
            transcendentals=0,
            bytes_accessed=2 * width * (nrows + 2 * arrived.shape[0] * BLK),
        ),
    )(far_col, far_ptr, requested, export_block, field, lo, hi, arrived, band, farw3)


def hop1(far_col, far_ptr, field, lo, hi, arrived, band, farw3, features, mix):
    nrows, width = field.shape
    return pl.pallas_call(
        hop1_kernel,
        in_specs=[smem(), smem()] + [vmem()] * 6 + [hbm(), vmem()],
        out_specs=[vmem(), vmem(), vmem()],
        out_shape=[
            jax.ShapeDtypeStruct((nrows, width), bf16),
            jax.ShapeDtypeStruct((nrows, width), f32),
            jax.ShapeDtypeStruct((nrows, width), f32),
        ],
        scratch_shapes=scratch(field)
        + [pltpu.VMEM((nrows, width), bf16), pltpu.SemaphoreType.DMA((1,))],
        compiler_params=pltpu.CompilerParams(),
        cost_estimate=pl.CostEstimate(
            flops=2 * BLK * BLK * width * (6 * nrows // BLK + farw3.shape[0])
            + 2 * nrows * width * CHUNK * 2,
            transcendentals=0,
            bytes_accessed=2 * width * (nrows * 9 + arrived.shape[0] * BLK),
        ),
    )(far_col, far_ptr, field, lo, hi, arrived, band, farw3, features, mix)


def hop2(far_col, far_ptr, lo, hi, arrived, band, farw3, acc2, part, mix):
    nrows, width = part.shape
    return pl.pallas_call(
        hop2_kernel,
        in_specs=[smem(), smem()] + [vmem()] * 5 + [hbm(), hbm(), vmem()],
        out_specs=vmem(),
        out_shape=jax.ShapeDtypeStruct((nrows, width), bf16),
        scratch_shapes=[
            pltpu.VMEM((nrows + BLK, width), f32),
            pltpu.VMEM((nrows, width), f32),
            pltpu.VMEM((nrows, width), f32),
            pltpu.SemaphoreType.DMA((2 * (width // CHUNK),)),
        ],
        compiler_params=pltpu.CompilerParams(),
        cost_estimate=pl.CostEstimate(
            flops=2 * BLK * BLK * width * (farw3.shape[0] + 2) + 2 * nrows * width * CHUNK,
            transcendentals=0,
            bytes_accessed=4 * width * nrows * 3,
        ),
    )(far_col, far_ptr, lo, hi, arrived, band, farw3, acc2, part, mix)


def halo(first, last):
    count = lax.axis_size("node")
    forward = [(i, i + 1) for i in range(count - 1)]
    backward = [(t, s) for s, t in forward]
    lo = lax.ppermute(last, "node", forward)
    hi = lax.ppermute(first, "node", backward)
    return lo, hi


def local(
    features,
    filter_gate_weight,
    skip_weight,
    mix_weight,
    band_weight,
    far_weight,
    far_ptr,
    far_col,
    export_block,
):
    node_rows = features.shape[0]
    blocks = node_rows // BLK
    far_cap = far_col.shape[1]

    own_index = lax.axis_index("node")
    own_exports = lax.dynamic_slice_in_dim(export_block, own_index, 1, 0)[0].astype(jnp.int32)
    peer_count = far_cap + 1
    info_all = lax.all_to_all(prep(far_col, far_ptr), "node", split_axis=0, concat_axis=0, tiled=True)
    slot_ids = jnp.arange(far_cap, dtype=jnp.int32)
    cols_all = info_all[:, :far_cap]
    hits = (cols_all // EXPORT == own_index) & (slot_ids[None, :] < info_all[:, far_cap:])
    requested = jnp.sum(jnp.where(hits, cols_all % EXPORT, 0), axis=1).astype(jnp.int32)
    hidden, ex2 = front_hidden(export_block, features, filter_gate_weight)
    blocks = node_rows // BLK
    width = hidden.shape[1]
    farw3 = far_weight.reshape(BLK, far_cap, BLK).transpose(1, 0, 2)

    def exchange(send):
        return lax.all_to_all(send, "node", split_axis=0, concat_axis=0, tiled=True)

    arrived1 = exchange(jnp.where((requested == 0)[:, None, None], ex2[0][None], ex2[1][None]))
    lo1, hi1 = halo(hidden[:BLK], hidden[node_rows - BLK :])
    skip_out = front_skip(hidden, skip_weight)
    send2, edge = early(
        far_col, far_ptr, requested, export_block, hidden, lo1, hi1, arrived1, band_weight, farw3
    )
    arrived2 = exchange(send2)
    lo2, hi2 = halo(edge[0], edge[1])
    hop_one, part, acc2 = hop1(
        far_col, far_ptr, hidden, lo1, hi1, arrived1, band_weight, farw3, features, mix_weight
    )
    residual = hop2(
        far_col, far_ptr, lo2, hi2, arrived2, band_weight, farw3, acc2, part, mix_weight
    )
    return residual, skip_out


def solution(mesh):
    placed = (
        P(("groups", "node"), None),
        P(),
        P(),
        P(),
        P("node", None),
        P(None, "node"),
        P("node", None),
        P("node", None),
        P(),
    )
    return jax.shard_map(
        local,
        mesh=mesh,
        in_specs=placed,
        out_specs=(P(("groups", "node"), None), P(("groups", "node"), None)),
        check_vma=False,
    )
```

```python
import functools

import jax
import jax.numpy as jnp
from jax import lax
from jax.experimental import pallas as pl
from jax.experimental.pallas import tpu as pltpu
from jax.sharding import PartitionSpec as P

BLK = 64
TOUT = 16
DILATION_STEP = 16
EXPORT = 2
CHANNEL_WIDTH = 32
S = 256
TIN = 32
CHUNK = 256
ROW_TILE = 256

f32 = jnp.float32
bf16 = jnp.bfloat16


def bd_inkernel(w, reps):
    r, c = w.shape
    shape_r = (reps * r, r)
    rep_r = jnp.where(
        lax.broadcasted_iota(jnp.int32, shape_r, 0) % r == lax.broadcasted_iota(jnp.int32, shape_r, 1),
        1.0, 0.0,
    ).astype(bf16)
    shape_c = (c, reps * c)
    rep_c = jnp.where(
        lax.broadcasted_iota(jnp.int32, shape_c, 1) % c == lax.broadcasted_iota(jnp.int32, shape_c, 0),
        1.0, 0.0,
    ).astype(bf16)
    rows = jnp.dot(rep_r, w, preferred_element_type=f32).astype(bf16)
    tiled = jnp.dot(rows, rep_c, preferred_element_type=f32)
    shape = tiled.shape
    mask = lax.broadcasted_iota(jnp.int32, shape, 0) // r == lax.broadcasted_iota(jnp.int32, shape, 1) // c
    return jnp.where(mask, tiled, 0.0).astype(bf16)


def hidden_kernel(exp_ref, x_ref, fgw_ref, h_ref, ex_ref):
    rows, cols = x_ref.shape
    half = cols // 2
    cw = fgw_ref.shape[0] // 2
    per = CHUNK // cw
    w = fgw_ref[...]
    wlo = jnp.concatenate([bd_inkernel(w[:cw, :cw], per), bd_inkernel(w[:cw, cw:], per)], axis=1)
    whi = jnp.concatenate([bd_inkernel(w[cw:, :cw], per), bd_inkernel(w[cw:, cw:], per)], axis=1)
    tile = min(ROW_TILE, rows)
    for t in range(rows // tile):
        rs = slice(t * tile, (t + 1) * tile)
        for j in range(half // CHUNK):
            x0 = x_ref[rs, j * CHUNK : (j + 1) * CHUNK]
            x1 = x_ref[rs, half + j * CHUNK : half + (j + 1) * CHUNK]
            pre = jnp.dot(x0, wlo, preferred_element_type=f32)
            pre = pre + jnp.dot(x1, whi, preferred_element_type=f32)
            h_ref[rs, j * CHUNK : (j + 1) * CHUNK] = (
                jnp.tanh(pre[:, :CHUNK]) * jax.nn.sigmoid(pre[:, CHUNK:])
            ).astype(bf16)
    own = lax.axis_index("node")
    for e in range(ex_ref.shape[0]):
        ex_ref[e] = h_ref[pl.ds(pl.multiple_of(exp_ref[own, e] * BLK, BLK), BLK), :]


def prep_kernel(col_ref, ptr_ref, out_ref):
    far_cap = col_ref.shape[1]
    peers = out_ref.shape[0]
    used = jnp.max(ptr_ref[...], axis=1, keepdims=True)
    out_ref[:, :far_cap] = jnp.broadcast_to(col_ref[...], (peers, far_cap))
    out_ref[:, far_cap:] = jnp.broadcast_to(used, (peers, 1))


def prep(far_col, far_ptr):
    far_cap = far_col.shape[1]
    return pl.pallas_call(
        prep_kernel,
        in_specs=[vmem(), vmem()],
        out_specs=vmem(),
        out_shape=jax.ShapeDtypeStruct((far_cap + 1, far_cap + 1), jnp.int32),
    )(far_col, far_ptr)


def skip_kernel(h_ref, sw_ref, s_ref, ws):
    cw = sw_ref.shape[0]

    @pl.when(pl.program_id(0) == 0)
    def _():
        ws[...] = bd_inkernel(sw_ref[...], CHUNK // cw)

    skip_w = ws.shape[1]
    for j in range(h_ref.shape[1] // CHUNK):
        s_ref[:, j * skip_w : (j + 1) * skip_w] = jnp.dot(
            h_ref[:, j * CHUNK : (j + 1) * CHUNK], ws[...], preferred_element_type=f32
        ).astype(bf16)


def front_hidden(export_block, features, fgw):
    rows, cols = features.shape
    half = cols // 2
    return pl.pallas_call(
        hidden_kernel,
        in_specs=[smem(), vmem(), vmem()],
        out_specs=[vmem(), vmem()],
        out_shape=[
            jax.ShapeDtypeStruct((rows, half), bf16),
            jax.ShapeDtypeStruct((export_block.shape[1], BLK, half), bf16),
        ],
        compiler_params=pltpu.CompilerParams(vmem_limit_bytes=48 * 1024 * 1024),
        cost_estimate=pl.CostEstimate(
            flops=2 * rows * CHUNK * 4 * CHUNK * (half // CHUNK),
            transcendentals=rows * half * 2,
            bytes_accessed=2 * rows * (cols + half),
        ),
    )(export_block, features, fgw)


def front_skip(hidden, skip_weight):
    rows, width = hidden.shape
    chunks = width // CHUNK
    cw, s = skip_weight.shape
    per = CHUNK // cw
    skip_cols = s * per * chunks
    tile = min(ROW_TILE, rows)
    return pl.pallas_call(
        skip_kernel,
        grid=(rows // tile,),
        in_specs=[
            pl.BlockSpec((tile, width), lambda i: (i, 0)),
            pl.BlockSpec(skip_weight.shape, lambda i: (0, 0)),
        ],
        out_specs=pl.BlockSpec((tile, skip_cols), lambda i: (i, 0)),
        out_shape=jax.ShapeDtypeStruct((rows, skip_cols), bf16),
        scratch_shapes=[pltpu.VMEM((CHUNK, s * per), bf16)],
        compiler_params=pltpu.CompilerParams(vmem_limit_bytes=48 * 1024 * 1024),
        cost_estimate=pl.CostEstimate(
            flops=2 * rows * CHUNK * s * per * chunks,
            transcendentals=0,
            bytes_accessed=2 * rows * (CHUNK * chunks + skip_cols),
        ),
    )(hidden, skip_weight)


def fill_pad(field_ref, lo_ref, hi_ref, pad):
    nrows = field_ref.shape[0]
    pad[:BLK, :] = lo_ref[...]
    pad[BLK : BLK + nrows, :] = field_ref[...]
    pad[BLK + nrows :, :] = hi_ref[...]


def band_block(band_ref, pad, t):
    start = pl.multiple_of(t * BLK, BLK)
    return jnp.dot(
        band_ref[pl.ds(start, BLK), :], pad[pl.ds(start, 3 * BLK), :], preferred_element_type=f32
    )


def slot_product(col_ref, farw_ref, arr_ref, k):
    return jnp.dot(farw_ref[k], arr_ref[col_ref[0, k] // EXPORT], preferred_element_type=f32)


def accumulate(col_ref, ptr_ref, field_ref, lo_ref, hi_ref, arr_ref, band_ref, farw_ref, acc, pad):
    nblk = field_ref.shape[0] // BLK
    far_cap = farw_ref.shape[0]
    nptr = ptr_ref.shape[1]
    fill_pad(field_ref, lo_ref, hi_ref, pad)
    for r in range(nblk):
        acc[r * BLK : (r + 1) * BLK, :] = band_block(band_ref, pad, r)
    acc[nblk * BLK :, :] = jnp.zeros((BLK, acc.shape[1]), f32)

    def slot(k, carry):
        row = 0
        for r in range(1, nptr):
            row = row + jnp.where(ptr_ref[0, r] <= k, 1, 0)
        start = pl.multiple_of(row * BLK, BLK)
        acc[pl.ds(start, BLK), :] += slot_product(col_ref, farw_ref, arr_ref, k)
        return carry

    lax.fori_loop(0, far_cap, slot, 0)


def early_kernel(
    col_ref, ptr_ref, req_ref, exp_ref, field_ref, lo_ref, hi_ref, arr_ref, band_ref, farw_ref,
    send_ref, edge_ref, blk,
):
    nblk = field_ref.shape[0] // BLK
    own = lax.axis_index("node")
    targets = [exp_ref[own, 0], exp_ref[own, 1], 0, nblk - 1]
    for i, t in enumerate(targets):
        pieces = []
        for s in range(3):
            b = jnp.clip(t - 1 + s, 0, nblk - 1)
            v = field_ref[pl.ds(pl.multiple_of(b * BLK, BLK), BLK), :]
            if s == 0:
                v = jnp.where(t == 0, lo_ref[...], v)
            if s == 2:
                v = jnp.where(t == nblk - 1, hi_ref[...], v)
            pieces.append(v)
        win = jnp.concatenate(pieces, axis=0)
        start = pl.multiple_of(t * BLK, BLK)
        v = jnp.dot(band_ref[pl.ds(start, BLK), :], win, preferred_element_type=f32)

        def slot(k, acc):
            return acc + slot_product(col_ref, farw_ref, arr_ref, k)

        v = lax.fori_loop(ptr_ref[0, t], ptr_ref[0, t + 1], slot, v)
        blk[i] = v.astype(bf16)

    def body(p, carry):
        send_ref[p] = blk[req_ref[p]]
        return carry

    lax.fori_loop(0, send_ref.shape[0], body, 0)
    edge_ref[0] = blk[2]
    edge_ref[1] = blk[3]


def hop1_kernel(
    col_ref, ptr_ref, field_ref, lo_ref, hi_ref, arr_ref, band_ref, farw_ref, x_hbm, mix_ref,
    out_ref, part_ref, acc2_ref, acc, pad, xs, sems,
):
    nrows, width = field_ref.shape
    nblk = nrows // BLK
    half = x_hbm.shape[1] // 2
    x_copy = pltpu.make_async_copy(x_hbm.at[:, pl.ds(half, width)], xs, sems.at[0])
    x_copy.start()
    accumulate(col_ref, ptr_ref, field_ref, lo_ref, hi_ref, arr_ref, band_ref, farw_ref, acc, pad)
    out_ref[...] = acc[:nrows, :].astype(bf16)
    zero = jnp.zeros((BLK, width), bf16)
    fill_pad(out_ref, zero, zero, pad)
    for r in range(nblk):
        acc2_ref[r * BLK : (r + 1) * BLK, :] = band_block(band_ref, pad, r)
    cw = mix_ref.shape[1]
    per = CHUNK // cw
    mix = mix_ref[...]
    m0 = bd_inkernel(mix[:cw], per)
    m1 = bd_inkernel(mix[cw : 2 * cw], per)
    x_copy.wait()
    for j in range(width // CHUNK):
        cols = slice(j * CHUNK, (j + 1) * CHUNK)
        v = xs[:, cols].astype(f32)
        v = v + jnp.dot(field_ref[:, cols], m0, preferred_element_type=f32)
        v = v + jnp.dot(out_ref[:, cols], m1, preferred_element_type=f32)
        part_ref[:, cols] = v


def hop2_kernel(
    col_ref, ptr_ref, lo_ref, hi_ref, arr_ref, band_ref, farw_ref, acc2_hbm, part_hbm, mix_ref,
    out_ref, far, a2, ps, sems,
):
    nrows, width = out_ref.shape
    nblk = nrows // BLK
    chunks = width // CHUNK
    copies = []
    for j in range(chunks):
        cols = pl.ds(j * CHUNK, CHUNK)
        ca = pltpu.make_async_copy(acc2_hbm.at[:, cols], a2.at[:, cols], sems.at[2 * j])
        cp = pltpu.make_async_copy(part_hbm.at[:, cols], ps.at[:, cols], sems.at[2 * j + 1])
        ca.start()
        cp.start()
        copies.append((ca, cp))
    far[...] = jnp.zeros(far.shape, f32)
    far[:BLK, :] = jnp.dot(band_ref[:BLK, :BLK], lo_ref[...], preferred_element_type=f32)
    last = (nblk - 1) * BLK
    far[last : last + BLK, :] = jnp.dot(
        band_ref[last : last + BLK, 2 * BLK :], hi_ref[...], preferred_element_type=f32
    )
    far_cap = farw_ref.shape[0]
    nptr = ptr_ref.shape[1]

    def slot(k, carry):
        row = 0
        for r in range(1, nptr):
            row = row + jnp.where(ptr_ref[0, r] <= k, 1, 0)
        start = pl.multiple_of(row * BLK, BLK)
        far[pl.ds(start, BLK), :] += slot_product(col_ref, farw_ref, arr_ref, k)
        return carry

    lax.fori_loop(0, far_cap, slot, 0)
    cw = mix_ref.shape[1]
    m2 = bd_inkernel(mix_ref[2 * cw :], CHUNK // cw)
    for j in range(chunks):
        ca, cp = copies[j]
        ca.wait()
        cp.wait()
        cols = slice(j * CHUNK, (j + 1) * CHUNK)
        two = (a2[:, cols] + far[:nrows, cols]).astype(bf16)
        v = ps[:, cols] + jnp.dot(two, m2, preferred_element_type=f32)
        out_ref[:, cols] = v.astype(bf16)


def vmem():
    return pl.BlockSpec(memory_space=pltpu.VMEM)


def smem():
    return pl.BlockSpec(memory_space=pltpu.SMEM)


def hbm():
    return pl.BlockSpec(memory_space=pltpu.HBM)


BIG_VMEM = pltpu.CompilerParams(vmem_limit_bytes=48 * 1024 * 1024)


def scratch(field):
    nrows, width = field.shape
    return [pltpu.VMEM((nrows + BLK, width), f32), pltpu.VMEM((nrows + 2 * BLK, width), bf16)]


def early(far_col, far_ptr, requested, export_block, field, lo, hi, arrived, band, farw3):
    nrows, width = field.shape
    return pl.pallas_call(
        early_kernel,
        in_specs=[smem()] * 4 + [vmem()] * 6,
        out_specs=[vmem(), vmem()],
        out_shape=[
            jax.ShapeDtypeStruct(arrived.shape, bf16),
            jax.ShapeDtypeStruct((2, BLK, width), bf16),
        ],
        scratch_shapes=[pltpu.VMEM((4, BLK, width), bf16)],
        compiler_params=BIG_VMEM,
        cost_estimate=pl.CostEstimate(
            flops=2 * BLK * BLK * width * (12 + farw3.shape[0]),
            transcendentals=0,
            bytes_accessed=2 * width * (nrows + 2 * arrived.shape[0] * BLK),
        ),
    )(far_col, far_ptr, requested, export_block, field, lo, hi, arrived, band, farw3)


def hop1(far_col, far_ptr, field, lo, hi, arrived, band, farw3, features, mix):
    nrows, width = field.shape
    return pl.pallas_call(
        hop1_kernel,
        in_specs=[smem(), smem()] + [vmem()] * 6 + [hbm(), vmem()],
        out_specs=[vmem(), vmem(), vmem()],
        out_shape=[
            jax.ShapeDtypeStruct((nrows, width), bf16),
            jax.ShapeDtypeStruct((nrows, width), f32),
            jax.ShapeDtypeStruct((nrows, width), f32),
        ],
        scratch_shapes=scratch(field)
        + [pltpu.VMEM((nrows, width), bf16), pltpu.SemaphoreType.DMA((1,))],
        compiler_params=pltpu.CompilerParams(),
        cost_estimate=pl.CostEstimate(
            flops=2 * BLK * BLK * width * (6 * nrows // BLK + farw3.shape[0])
            + 2 * nrows * width * CHUNK * 2,
            transcendentals=0,
            bytes_accessed=2 * width * (nrows * 9 + arrived.shape[0] * BLK),
        ),
    )(far_col, far_ptr, field, lo, hi, arrived, band, farw3, features, mix)


def hop2(far_col, far_ptr, lo, hi, arrived, band, farw3, acc2, part, mix):
    nrows, width = part.shape
    return pl.pallas_call(
        hop2_kernel,
        in_specs=[smem(), smem()] + [vmem()] * 5 + [hbm(), hbm(), vmem()],
        out_specs=vmem(),
        out_shape=jax.ShapeDtypeStruct((nrows, width), bf16),
        scratch_shapes=[
            pltpu.VMEM((nrows + BLK, width), f32),
            pltpu.VMEM((nrows, width), f32),
            pltpu.VMEM((nrows, width), f32),
            pltpu.SemaphoreType.DMA((2 * (width // CHUNK),)),
        ],
        compiler_params=pltpu.CompilerParams(),
        cost_estimate=pl.CostEstimate(
            flops=2 * BLK * BLK * width * (farw3.shape[0] + 2) + 2 * nrows * width * CHUNK,
            transcendentals=0,
            bytes_accessed=4 * width * nrows * 3,
        ),
    )(far_col, far_ptr, lo, hi, arrived, band, farw3, acc2, part, mix)


def halo(first, last):
    count = lax.axis_size("node")
    forward = [(i, i + 1) for i in range(count - 1)]
    backward = [(t, s) for s, t in forward]
    lo = lax.ppermute(last, "node", forward)
    hi = lax.ppermute(first, "node", backward)
    return lo, hi


def local(
    features,
    filter_gate_weight,
    skip_weight,
    mix_weight,
    band_weight,
    far_weight,
    far_ptr,
    far_col,
    export_block,
):
    node_rows = features.shape[0]
    blocks = node_rows // BLK
    far_cap = far_col.shape[1]

    own_index = lax.axis_index("node")
    own_exports = lax.dynamic_slice_in_dim(export_block, own_index, 1, 0)[0].astype(jnp.int32)
    peer_count = far_cap + 1
    info_all = lax.all_to_all(prep(far_col, far_ptr), "node", split_axis=0, concat_axis=0, tiled=True)
    slot_ids = jnp.arange(far_cap, dtype=jnp.int32)
    cols_all = info_all[:, :far_cap]
    hits = (cols_all // EXPORT == own_index) & (slot_ids[None, :] < info_all[:, far_cap:])
    requested = jnp.sum(jnp.where(hits, cols_all % EXPORT, 0), axis=1).astype(jnp.int32)
    hidden, ex2 = front_hidden(export_block, features, filter_gate_weight)
    blocks = node_rows // BLK
    width = hidden.shape[1]
    farw3 = far_weight.reshape(BLK, far_cap, BLK).transpose(1, 0, 2)

    def exchange(send):
        return lax.all_to_all(send, "node", split_axis=0, concat_axis=0, tiled=True)

    arrived1 = exchange(jnp.where((requested == 0)[:, None, None], ex2[0][None], ex2[1][None]))
    lo1, hi1 = halo(hidden[:BLK], hidden[node_rows - BLK :])
    skip_out = front_skip(hidden, skip_weight)
    send2, edge = early(
        far_col, far_ptr, requested, export_block, hidden, lo1, hi1, arrived1, band_weight, farw3
    )
    arrived2 = exchange(send2)
    lo2, hi2 = halo(edge[0], edge[1])
    hop_one, part, acc2 = hop1(
        far_col, far_ptr, hidden, lo1, hi1, arrived1, band_weight, farw3, features, mix_weight
    )
    residual = hop2(
        far_col, far_ptr, lo2, hi2, arrived2, band_weight, farw3, acc2, part, mix_weight
    )
    return residual, skip_out


def solution(mesh):
    placed = (
        P(("groups", "node"), None),
        P(),
        P(),
        P(),
        P("node", None),
        P(None, "node"),
        P("node", None),
        P("node", None),
        P(),
    )
    return jax.shard_map(
        local,
        mesh=mesh,
        in_specs=placed,
        out_specs=(P(("groups", "node"), None), P(("groups", "node"), None)),
        check_vma=False,
    )
```

```python
import functools

import jax
import jax.numpy as jnp
from jax import lax
from jax.experimental import pallas as pl
from jax.experimental.pallas import tpu as pltpu
from jax.sharding import PartitionSpec as P

BLK = 64
TOUT = 16
DILATION_STEP = 16
EXPORT = 2
CHANNEL_WIDTH = 32
S = 256
TIN = 32
CHUNK = 256
ROW_TILE = 256

f32 = jnp.float32
bf16 = jnp.bfloat16


def bd_inkernel(w, reps):
    r, c = w.shape
    shape_r = (reps * r, r)
    rep_r = jnp.where(
        lax.broadcasted_iota(jnp.int32, shape_r, 0) % r == lax.broadcasted_iota(jnp.int32, shape_r, 1),
        1.0, 0.0,
    ).astype(bf16)
    shape_c = (c, reps * c)
    rep_c = jnp.where(
        lax.broadcasted_iota(jnp.int32, shape_c, 1) % c == lax.broadcasted_iota(jnp.int32, shape_c, 0),
        1.0, 0.0,
    ).astype(bf16)
    rows = jnp.dot(rep_r, w, preferred_element_type=f32).astype(bf16)
    tiled = jnp.dot(rows, rep_c, preferred_element_type=f32)
    shape = tiled.shape
    mask = lax.broadcasted_iota(jnp.int32, shape, 0) // r == lax.broadcasted_iota(jnp.int32, shape, 1) // c
    return jnp.where(mask, tiled, 0.0).astype(bf16)


def hidden_kernel(exp_ref, x_ref, fgw_ref, h_ref, ex_ref):
    rows, cols = x_ref.shape
    half = cols // 2
    cw = fgw_ref.shape[0] // 2
    per = CHUNK // cw
    w = fgw_ref[...]
    wlo = jnp.concatenate([bd_inkernel(w[:cw, :cw], per), bd_inkernel(w[:cw, cw:], per)], axis=1)
    whi = jnp.concatenate([bd_inkernel(w[cw:, :cw], per), bd_inkernel(w[cw:, cw:], per)], axis=1)
    tile = min(ROW_TILE, rows)
    for t in range(rows // tile):
        rs = slice(t * tile, (t + 1) * tile)
        for j in range(half // CHUNK):
            x0 = x_ref[rs, j * CHUNK : (j + 1) * CHUNK]
            x1 = x_ref[rs, half + j * CHUNK : half + (j + 1) * CHUNK]
            pre = jnp.dot(x0, wlo, preferred_element_type=f32)
            pre = pre + jnp.dot(x1, whi, preferred_element_type=f32)
            h_ref[rs, j * CHUNK : (j + 1) * CHUNK] = (
                jnp.tanh(pre[:, :CHUNK]) * jax.nn.sigmoid(pre[:, CHUNK:])
            ).astype(bf16)
    own = lax.axis_index("node")
    for e in range(ex_ref.shape[0]):
        ex_ref[e] = h_ref[pl.ds(pl.multiple_of(exp_ref[own, e] * BLK, BLK), BLK), :]


def prep_kernel(col_ref, ptr_ref, out_ref):
    far_cap = col_ref.shape[1]
    peers = out_ref.shape[0]
    used = jnp.max(ptr_ref[...], axis=1, keepdims=True)
    out_ref[:, :far_cap] = jnp.broadcast_to(col_ref[...], (peers, far_cap))
    out_ref[:, far_cap:] = jnp.broadcast_to(used, (peers, 1))


def prep(far_col, far_ptr):
    far_cap = far_col.shape[1]
    return pl.pallas_call(
        prep_kernel,
        in_specs=[vmem(), vmem()],
        out_specs=vmem(),
        out_shape=jax.ShapeDtypeStruct((far_cap + 1, far_cap + 1), jnp.int32),
    )(far_col, far_ptr)


def skip_kernel(h_ref, sw_ref, s_ref, ws):
    cw = sw_ref.shape[0]

    @pl.when(pl.program_id(0) == 0)
    def _():
        ws[...] = bd_inkernel(sw_ref[...], CHUNK // cw)

    skip_w = ws.shape[1]
    for j in range(h_ref.shape[1] // CHUNK):
        s_ref[:, j * skip_w : (j + 1) * skip_w] = jnp.dot(
            h_ref[:, j * CHUNK : (j + 1) * CHUNK], ws[...], preferred_element_type=f32
        ).astype(bf16)


def front_hidden(export_block, features, fgw):
    rows, cols = features.shape
    half = cols // 2
    return pl.pallas_call(
        hidden_kernel,
        in_specs=[smem(), vmem(), vmem()],
        out_specs=[vmem(), vmem()],
        out_shape=[
            jax.ShapeDtypeStruct((rows, half), bf16),
            jax.ShapeDtypeStruct((export_block.shape[1], BLK, half), bf16),
        ],
        compiler_params=pltpu.CompilerParams(vmem_limit_bytes=48 * 1024 * 1024),
        cost_estimate=pl.CostEstimate(
            flops=2 * rows * CHUNK * 4 * CHUNK * (half // CHUNK),
            transcendentals=rows * half * 2,
            bytes_accessed=2 * rows * (cols + half),
        ),
    )(export_block, features, fgw)


def front_skip(hidden, skip_weight):
    rows, width = hidden.shape
    chunks = width // CHUNK
    cw, s = skip_weight.shape
    per = CHUNK // cw
    skip_cols = s * per * chunks
    tile = min(ROW_TILE, rows)
    return pl.pallas_call(
        skip_kernel,
        grid=(rows // tile,),
        in_specs=[
            pl.BlockSpec((tile, width), lambda i: (i, 0)),
            pl.BlockSpec(skip_weight.shape, lambda i: (0, 0)),
        ],
        out_specs=pl.BlockSpec((tile, skip_cols), lambda i: (i, 0)),
        out_shape=jax.ShapeDtypeStruct((rows, skip_cols), bf16),
        scratch_shapes=[pltpu.VMEM((CHUNK, s * per), bf16)],
        compiler_params=pltpu.CompilerParams(vmem_limit_bytes=48 * 1024 * 1024),
        cost_estimate=pl.CostEstimate(
            flops=2 * rows * CHUNK * s * per * chunks,
            transcendentals=0,
            bytes_accessed=2 * rows * (CHUNK * chunks + skip_cols),
        ),
    )(hidden, skip_weight)


def fill_pad(field_ref, lo_ref, hi_ref, pad):
    nrows = field_ref.shape[0]
    pad[:BLK, :] = lo_ref[...]
    pad[BLK : BLK + nrows, :] = field_ref[...]
    pad[BLK + nrows :, :] = hi_ref[...]


def band_block(band_ref, pad, t):
    start = pl.multiple_of(t * BLK, BLK)
    return jnp.dot(
        band_ref[pl.ds(start, BLK), :], pad[pl.ds(start, 3 * BLK), :], preferred_element_type=f32
    )


def slot_product(col_ref, farw_ref, arr_ref, k):
    return jnp.dot(farw_ref[k], arr_ref[col_ref[0, k] // EXPORT], preferred_element_type=f32)


def accumulate(col_ref, ptr_ref, field_ref, lo_ref, hi_ref, arr_ref, band_ref, farw_ref, acc, pad):
    nblk = field_ref.shape[0] // BLK
    far_cap = farw_ref.shape[0]
    nptr = ptr_ref.shape[1]
    fill_pad(field_ref, lo_ref, hi_ref, pad)
    for r in range(nblk):
        acc[r * BLK : (r + 1) * BLK, :] = band_block(band_ref, pad, r)
    acc[nblk * BLK :, :] = jnp.zeros((BLK, acc.shape[1]), f32)

    def slot(k, carry):
        row = 0
        for r in range(1, nptr):
            row = row + jnp.where(ptr_ref[0, r] <= k, 1, 0)
        start = pl.multiple_of(row * BLK, BLK)
        acc[pl.ds(start, BLK), :] += slot_product(col_ref, farw_ref, arr_ref, k)
        return carry

    lax.fori_loop(0, far_cap, slot, 0)


def early_kernel(
    col_ref, ptr_ref, req_ref, exp_ref, field_ref, lo_ref, hi_ref, arr_ref, band_ref, farw_ref,
    send_ref, edge_ref, pad, blk,
):
    nblk = field_ref.shape[0] // BLK
    own = lax.axis_index("node")
    fill_pad(field_ref, lo_ref, hi_ref, pad)
    targets = [exp_ref[own, 0], exp_ref[own, 1], 0, nblk - 1]
    for i, t in enumerate(targets):
        v = band_block(band_ref, pad, t)

        def slot(k, acc):
            return acc + slot_product(col_ref, farw_ref, arr_ref, k)

        v = lax.fori_loop(ptr_ref[0, t], ptr_ref[0, t + 1], slot, v)
        blk[i] = v.astype(bf16)

    def body(p, carry):
        send_ref[p] = blk[req_ref[p]]
        return carry

    lax.fori_loop(0, send_ref.shape[0], body, 0)
    edge_ref[0] = blk[2]
    edge_ref[1] = blk[3]


def hop1_kernel(
    col_ref, ptr_ref, field_ref, lo_ref, hi_ref, arr_ref, band_ref, farw_ref, x_hbm, mix_ref,
    out_ref, part_ref, acc2_ref, m2_ref, acc, pad, xs, sems,
):
    nrows, width = field_ref.shape
    nblk = nrows // BLK
    half = x_hbm.shape[1] // 2
    x_copy = pltpu.make_async_copy(x_hbm.at[:, pl.ds(half, width)], xs, sems.at[0])
    x_copy.start()
    accumulate(col_ref, ptr_ref, field_ref, lo_ref, hi_ref, arr_ref, band_ref, farw_ref, acc, pad)
    out_ref[...] = acc[:nrows, :].astype(bf16)
    zero = jnp.zeros((BLK, width), bf16)
    fill_pad(out_ref, zero, zero, pad)
    for r in range(nblk):
        acc2_ref[r * BLK : (r + 1) * BLK, :] = band_block(band_ref, pad, r)
    cw = mix_ref.shape[1]
    per = CHUNK // cw
    mix = mix_ref[...]
    m0 = bd_inkernel(mix[:cw], per)
    m1 = bd_inkernel(mix[cw : 2 * cw], per)
    m2_ref[...] = bd_inkernel(mix[2 * cw :], per)
    x_copy.wait()
    for j in range(width // CHUNK):
        cols = slice(j * CHUNK, (j + 1) * CHUNK)
        v = xs[:, cols].astype(f32)
        v = v + jnp.dot(field_ref[:, cols], m0, preferred_element_type=f32)
        v = v + jnp.dot(out_ref[:, cols], m1, preferred_element_type=f32)
        part_ref[:, cols] = v


def hop2_kernel(
    col_ref, ptr_ref, lo_ref, hi_ref, arr_ref, band_ref, farw_ref, acc2_hbm, part_hbm, m2_ref,
    out_ref, far, a2, ps, sems,
):
    nrows, width = out_ref.shape
    nblk = nrows // BLK
    chunks = width // CHUNK
    copies = []
    for j in range(chunks):
        cols = pl.ds(j * CHUNK, CHUNK)
        ca = pltpu.make_async_copy(acc2_hbm.at[:, cols], a2.at[:, cols], sems.at[2 * j])
        cp = pltpu.make_async_copy(part_hbm.at[:, cols], ps.at[:, cols], sems.at[2 * j + 1])
        ca.start()
        cp.start()
        copies.append((ca, cp))
    far[...] = jnp.zeros(far.shape, f32)
    far[:BLK, :] = jnp.dot(band_ref[:BLK, :BLK], lo_ref[...], preferred_element_type=f32)
    last = (nblk - 1) * BLK
    far[last : last + BLK, :] = jnp.dot(
        band_ref[last : last + BLK, 2 * BLK :], hi_ref[...], preferred_element_type=f32
    )
    far_cap = farw_ref.shape[0]
    nptr = ptr_ref.shape[1]

    def slot(k, carry):
        row = 0
        for r in range(1, nptr):
            row = row + jnp.where(ptr_ref[0, r] <= k, 1, 0)
        start = pl.multiple_of(row * BLK, BLK)
        far[pl.ds(start, BLK), :] += slot_product(col_ref, farw_ref, arr_ref, k)
        return carry

    lax.fori_loop(0, far_cap, slot, 0)
    m2 = m2_ref[...]
    for j in range(chunks):
        ca, cp = copies[j]
        ca.wait()
        cp.wait()
        cols = slice(j * CHUNK, (j + 1) * CHUNK)
        two = (a2[:, cols] + far[:nrows, cols]).astype(bf16)
        v = ps[:, cols] + jnp.dot(two, m2, preferred_element_type=f32)
        out_ref[:, cols] = v.astype(bf16)


def vmem():
    return pl.BlockSpec(memory_space=pltpu.VMEM)


def smem():
    return pl.BlockSpec(memory_space=pltpu.SMEM)


def hbm():
    return pl.BlockSpec(memory_space=pltpu.HBM)


BIG_VMEM = pltpu.CompilerParams(vmem_limit_bytes=48 * 1024 * 1024)


def scratch(field):
    nrows, width = field.shape
    return [pltpu.VMEM((nrows + BLK, width), f32), pltpu.VMEM((nrows + 2 * BLK, width), bf16)]


def early(far_col, far_ptr, requested, export_block, field, lo, hi, arrived, band, farw3):
    nrows, width = field.shape
    return pl.pallas_call(
        early_kernel,
        in_specs=[smem()] * 4 + [vmem()] * 6,
        out_specs=[vmem(), vmem()],
        out_shape=[
            jax.ShapeDtypeStruct(arrived.shape, bf16),
            jax.ShapeDtypeStruct((2, BLK, width), bf16),
        ],
        scratch_shapes=[pltpu.VMEM((nrows + 2 * BLK, width), bf16), pltpu.VMEM((4, BLK, width), bf16)],
        compiler_params=BIG_VMEM,
        cost_estimate=pl.CostEstimate(
            flops=2 * BLK * BLK * width * (12 + farw3.shape[0]),
            transcendentals=0,
            bytes_accessed=2 * width * (nrows + 2 * arrived.shape[0] * BLK),
        ),
    )(far_col, far_ptr, requested, export_block, field, lo, hi, arrived, band, farw3)


def hop1(far_col, far_ptr, field, lo, hi, arrived, band, farw3, features, mix):
    nrows, width = field.shape
    return pl.pallas_call(
        hop1_kernel,
        in_specs=[smem(), smem()] + [vmem()] * 6 + [hbm(), vmem()],
        out_specs=[vmem(), vmem(), vmem(), vmem()],
        out_shape=[
            jax.ShapeDtypeStruct((nrows, width), bf16),
            jax.ShapeDtypeStruct((nrows, width), f32),
            jax.ShapeDtypeStruct((nrows, width), f32),
            jax.ShapeDtypeStruct((CHUNK, CHUNK), bf16),
        ],
        scratch_shapes=scratch(field)
        + [pltpu.VMEM((nrows, width), bf16), pltpu.SemaphoreType.DMA((1,))],
        compiler_params=pltpu.CompilerParams(),
        cost_estimate=pl.CostEstimate(
            flops=2 * BLK * BLK * width * (6 * nrows // BLK + farw3.shape[0])
            + 2 * nrows * width * CHUNK * 2,
            transcendentals=0,
            bytes_accessed=2 * width * (nrows * 9 + arrived.shape[0] * BLK),
        ),
    )(far_col, far_ptr, field, lo, hi, arrived, band, farw3, features, mix)


def hop2(far_col, far_ptr, lo, hi, arrived, band, farw3, acc2, part, m2):
    nrows, width = part.shape
    return pl.pallas_call(
        hop2_kernel,
        in_specs=[smem(), smem()] + [vmem()] * 5 + [hbm(), hbm(), vmem()],
        out_specs=vmem(),
        out_shape=jax.ShapeDtypeStruct((nrows, width), bf16),
        scratch_shapes=[
            pltpu.VMEM((nrows + BLK, width), f32),
            pltpu.VMEM((nrows, width), f32),
            pltpu.VMEM((nrows, width), f32),
            pltpu.SemaphoreType.DMA((2 * (width // CHUNK),)),
        ],
        compiler_params=pltpu.CompilerParams(),
        cost_estimate=pl.CostEstimate(
            flops=2 * BLK * BLK * width * (farw3.shape[0] + 2) + 2 * nrows * width * CHUNK,
            transcendentals=0,
            bytes_accessed=4 * width * nrows * 3,
        ),
    )(far_col, far_ptr, lo, hi, arrived, band, farw3, acc2, part, m2)


def halo(first, last):
    count = lax.axis_size("node")
    forward = [(i, i + 1) for i in range(count - 1)]
    backward = [(t, s) for s, t in forward]
    lo = lax.ppermute(last, "node", forward)
    hi = lax.ppermute(first, "node", backward)
    return lo, hi


def local(
    features,
    filter_gate_weight,
    skip_weight,
    mix_weight,
    band_weight,
    far_weight,
    far_ptr,
    far_col,
    export_block,
):
    node_rows = features.shape[0]
    blocks = node_rows // BLK
    far_cap = far_col.shape[1]

    own_index = lax.axis_index("node")
    own_exports = lax.dynamic_slice_in_dim(export_block, own_index, 1, 0)[0].astype(jnp.int32)
    peer_count = far_cap + 1
    info_all = lax.all_to_all(prep(far_col, far_ptr), "node", split_axis=0, concat_axis=0, tiled=True)
    slot_ids = jnp.arange(far_cap, dtype=jnp.int32)
    cols_all = info_all[:, :far_cap]
    hits = (cols_all // EXPORT == own_index) & (slot_ids[None, :] < info_all[:, far_cap:])
    requested = jnp.sum(jnp.where(hits, cols_all % EXPORT, 0), axis=1).astype(jnp.int32)
    hidden, ex2 = front_hidden(export_block, features, filter_gate_weight)
    blocks = node_rows // BLK
    width = hidden.shape[1]
    farw3 = far_weight.reshape(BLK, far_cap, BLK).transpose(1, 0, 2)

    def exchange(send):
        return lax.all_to_all(send, "node", split_axis=0, concat_axis=0, tiled=True)

    arrived1 = exchange(jnp.where((requested == 0)[:, None, None], ex2[0][None], ex2[1][None]))
    lo1, hi1 = halo(hidden[:BLK], hidden[node_rows - BLK :])
    skip_out = front_skip(hidden, skip_weight)
    send2, edge = early(
        far_col, far_ptr, requested, export_block, hidden, lo1, hi1, arrived1, band_weight, farw3
    )
    arrived2 = exchange(send2)
    lo2, hi2 = halo(edge[0], edge[1])
    hop_one, part, acc2, m2 = hop1(
        far_col, far_ptr, hidden, lo1, hi1, arrived1, band_weight, farw3, features, mix_weight
    )
    residual = hop2(
        far_col, far_ptr, lo2, hi2, arrived2, band_weight, farw3, acc2, part, m2
    )
    return residual, skip_out


def solution(mesh):
    placed = (
        P(("groups", "node"), None),
        P(),
        P(),
        P(),
        P("node", None),
        P(None, "node"),
        P("node", None),
        P("node", None),
        P(),
    )
    return jax.shard_map(
        local,
        mesh=mesh,
        in_specs=placed,
        out_specs=(P(("groups", "node"), None), P(("groups", "node"), None)),
        check_vma=False,
    )
```

```python
import functools

import jax
import jax.numpy as jnp
from jax import lax
from jax.experimental import pallas as pl
from jax.experimental.pallas import tpu as pltpu
from jax.sharding import PartitionSpec as P

BLK = 64
TOUT = 16
DILATION_STEP = 16
EXPORT = 2
CHANNEL_WIDTH = 32
S = 256
TIN = 32
CHUNK = 256
ROW_TILE = 256

f32 = jnp.float32
bf16 = jnp.bfloat16


def bd_inkernel(w, reps):
    r, c = w.shape
    shape_r = (reps * r, r)
    rep_r = jnp.where(
        lax.broadcasted_iota(jnp.int32, shape_r, 0) % r == lax.broadcasted_iota(jnp.int32, shape_r, 1),
        1.0, 0.0,
    ).astype(bf16)
    shape_c = (c, reps * c)
    rep_c = jnp.where(
        lax.broadcasted_iota(jnp.int32, shape_c, 1) % c == lax.broadcasted_iota(jnp.int32, shape_c, 0),
        1.0, 0.0,
    ).astype(bf16)
    rows = jnp.dot(rep_r, w, preferred_element_type=f32).astype(bf16)
    tiled = jnp.dot(rows, rep_c, preferred_element_type=f32)
    shape = tiled.shape
    mask = lax.broadcasted_iota(jnp.int32, shape, 0) // r == lax.broadcasted_iota(jnp.int32, shape, 1) // c
    return jnp.where(mask, tiled, 0.0).astype(bf16)


def hidden_kernel(exp_ref, x_ref, fgw_ref, h_ref, ex_ref):
    rows, cols = x_ref.shape
    half = cols // 2
    cw = fgw_ref.shape[0] // 2
    per = CHUNK // cw
    w = fgw_ref[...]
    wlo = jnp.concatenate([bd_inkernel(w[:cw, :cw], per), bd_inkernel(w[:cw, cw:], per)], axis=1)
    whi = jnp.concatenate([bd_inkernel(w[cw:, :cw], per), bd_inkernel(w[cw:, cw:], per)], axis=1)
    tile = min(ROW_TILE, rows)
    for t in range(rows // tile):
        rs = slice(t * tile, (t + 1) * tile)
        for j in range(half // CHUNK):
            x0 = x_ref[rs, j * CHUNK : (j + 1) * CHUNK]
            x1 = x_ref[rs, half + j * CHUNK : half + (j + 1) * CHUNK]
            pre = jnp.dot(x0, wlo, preferred_element_type=f32)
            pre = pre + jnp.dot(x1, whi, preferred_element_type=f32)
            h_ref[rs, j * CHUNK : (j + 1) * CHUNK] = (
                jnp.tanh(pre[:, :CHUNK]) * jax.nn.sigmoid(pre[:, CHUNK:])
            ).astype(bf16)
    own = lax.axis_index("node")
    for e in range(ex_ref.shape[0]):
        ex_ref[e] = h_ref[pl.ds(pl.multiple_of(exp_ref[own, e] * BLK, BLK), BLK), :]


def prep_kernel(col_ref, ptr_ref, out_ref):
    far_cap = col_ref.shape[1]
    peers = out_ref.shape[0]
    used = jnp.max(ptr_ref[...], axis=1, keepdims=True)
    out_ref[:, :far_cap] = jnp.broadcast_to(col_ref[...], (peers, far_cap))
    out_ref[:, far_cap:] = jnp.broadcast_to(used, (peers, 1))


def prep(far_col, far_ptr):
    far_cap = far_col.shape[1]
    return pl.pallas_call(
        prep_kernel,
        in_specs=[vmem(), vmem()],
        out_specs=vmem(),
        out_shape=jax.ShapeDtypeStruct((far_cap + 1, far_cap + 1), jnp.int32),
    )(far_col, far_ptr)


def skip_kernel(h_ref, sw_ref, s_ref, ws):
    cw = sw_ref.shape[0]

    @pl.when(pl.program_id(0) == 0)
    def _():
        ws[...] = bd_inkernel(sw_ref[...], CHUNK // cw)

    skip_w = ws.shape[1]
    for j in range(h_ref.shape[1] // CHUNK):
        s_ref[:, j * skip_w : (j + 1) * skip_w] = jnp.dot(
            h_ref[:, j * CHUNK : (j + 1) * CHUNK], ws[...], preferred_element_type=f32
        ).astype(bf16)


def front_hidden(export_block, features, fgw):
    rows, cols = features.shape
    half = cols // 2
    return pl.pallas_call(
        hidden_kernel,
        in_specs=[smem(), vmem(), vmem()],
        out_specs=[vmem(), vmem()],
        out_shape=[
            jax.ShapeDtypeStruct((rows, half), bf16),
            jax.ShapeDtypeStruct((export_block.shape[1], BLK, half), bf16),
        ],
        compiler_params=pltpu.CompilerParams(vmem_limit_bytes=48 * 1024 * 1024),
        cost_estimate=pl.CostEstimate(
            flops=2 * rows * CHUNK * 4 * CHUNK * (half // CHUNK),
            transcendentals=rows * half * 2,
            bytes_accessed=2 * rows * (cols + half),
        ),
    )(export_block, features, fgw)


def front_skip(hidden, skip_weight):
    rows, width = hidden.shape
    chunks = width // CHUNK
    cw, s = skip_weight.shape
    per = CHUNK // cw
    skip_cols = s * per * chunks
    tile = min(ROW_TILE, rows)
    return pl.pallas_call(
        skip_kernel,
        grid=(rows // tile,),
        in_specs=[
            pl.BlockSpec((tile, width), lambda i: (i, 0)),
            pl.BlockSpec(skip_weight.shape, lambda i: (0, 0)),
        ],
        out_specs=pl.BlockSpec((tile, skip_cols), lambda i: (i, 0)),
        out_shape=jax.ShapeDtypeStruct((rows, skip_cols), bf16),
        scratch_shapes=[pltpu.VMEM((CHUNK, s * per), bf16)],
        compiler_params=pltpu.CompilerParams(vmem_limit_bytes=48 * 1024 * 1024),
        cost_estimate=pl.CostEstimate(
            flops=2 * rows * CHUNK * s * per * chunks,
            transcendentals=0,
            bytes_accessed=2 * rows * (CHUNK * chunks + skip_cols),
        ),
    )(hidden, skip_weight)


def fill_pad(field_ref, lo_ref, hi_ref, pad):
    nrows = field_ref.shape[0]
    pad[:BLK, :] = lo_ref[...]
    pad[BLK : BLK + nrows, :] = field_ref[...]
    pad[BLK + nrows :, :] = hi_ref[...]


def band_block(band_ref, pad, t):
    start = pl.multiple_of(t * BLK, BLK)
    return jnp.dot(
        band_ref[pl.ds(start, BLK), :], pad[pl.ds(start, 3 * BLK), :], preferred_element_type=f32
    )


def slot_product(col_ref, farw_ref, arr_ref, k):
    return jnp.dot(farw_ref[k], arr_ref[col_ref[0, k] // EXPORT], preferred_element_type=f32)


def accumulate(col_ref, ptr_ref, field_ref, lo_ref, hi_ref, arr_ref, band_ref, farw_ref, acc, pad):
    nblk = field_ref.shape[0] // BLK
    far_cap = farw_ref.shape[0]
    nptr = ptr_ref.shape[1]
    fill_pad(field_ref, lo_ref, hi_ref, pad)
    for r in range(nblk):
        acc[r * BLK : (r + 1) * BLK, :] = band_block(band_ref, pad, r)
    acc[nblk * BLK :, :] = jnp.zeros((BLK, acc.shape[1]), f32)

    def slot(k, carry):
        row = 0
        for r in range(1, nptr):
            row = row + jnp.where(ptr_ref[0, r] <= k, 1, 0)
        start = pl.multiple_of(row * BLK, BLK)
        acc[pl.ds(start, BLK), :] += slot_product(col_ref, farw_ref, arr_ref, k)
        return carry

    lax.fori_loop(0, far_cap, slot, 0)


def early_kernel(
    col_ref, ptr_ref, req_ref, exp_ref, field_ref, lo_ref, hi_ref, arr_ref, band_ref, farw_ref,
    send_ref, edge_ref, blk,
):
    nblk = field_ref.shape[0] // BLK
    own = lax.axis_index("node")
    targets = [exp_ref[own, 0], exp_ref[own, 1], 0, nblk - 1]
    for i, t in enumerate(targets):
        pieces = []
        for s in range(3):
            b = jnp.clip(t - 1 + s, 0, nblk - 1)
            v = field_ref[pl.ds(pl.multiple_of(b * BLK, BLK), BLK), :]
            if s == 0:
                v = jnp.where(t == 0, lo_ref[...], v)
            if s == 2:
                v = jnp.where(t == nblk - 1, hi_ref[...], v)
            pieces.append(v)
        win = jnp.concatenate(pieces, axis=0)
        start = pl.multiple_of(t * BLK, BLK)
        v = jnp.dot(band_ref[pl.ds(start, BLK), :], win, preferred_element_type=f32)

        def slot(k, acc):
            return acc + slot_product(col_ref, farw_ref, arr_ref, k)

        v = lax.fori_loop(ptr_ref[0, t], ptr_ref[0, t + 1], slot, v)
        blk[i] = v.astype(bf16)

    def body(p, carry):
        send_ref[p] = blk[req_ref[p]]
        return carry

    lax.fori_loop(0, send_ref.shape[0], body, 0)
    edge_ref[0] = blk[2]
    edge_ref[1] = blk[3]


def hop1_kernel(
    col_ref, ptr_ref, field_ref, lo_ref, hi_ref, arr_ref, band_ref, farw_ref, x_hbm, mix_ref,
    out_ref, part_ref, acc2_ref, m2_ref, acc, pad, xs, sems,
):
    nrows, width = field_ref.shape
    nblk = nrows // BLK
    half = x_hbm.shape[1] // 2
    x_copy = pltpu.make_async_copy(x_hbm.at[:, pl.ds(half, width)], xs, sems.at[0])
    x_copy.start()
    accumulate(col_ref, ptr_ref, field_ref, lo_ref, hi_ref, arr_ref, band_ref, farw_ref, acc, pad)
    out_ref[...] = acc[:nrows, :].astype(bf16)
    zero = jnp.zeros((BLK, width), bf16)
    fill_pad(out_ref, zero, zero, pad)
    for r in range(nblk):
        acc2_ref[r * BLK : (r + 1) * BLK, :] = band_block(band_ref, pad, r)
    cw = mix_ref.shape[1]
    per = CHUNK // cw
    mix = mix_ref[...]
    m0 = bd_inkernel(mix[:cw], per)
    m1 = bd_inkernel(mix[cw : 2 * cw], per)
    m2_ref[...] = bd_inkernel(mix[2 * cw :], per)
    x_copy.wait()
    for j in range(width // CHUNK):
        cols = slice(j * CHUNK, (j + 1) * CHUNK)
        v = xs[:, cols].astype(f32)
        v = v + jnp.dot(field_ref[:, cols], m0, preferred_element_type=f32)
        v = v + jnp.dot(out_ref[:, cols], m1, preferred_element_type=f32)
        part_ref[:, cols] = v


def hop2_kernel(
    col_ref, ptr_ref, lo_ref, hi_ref, arr_ref, band_ref, farw_ref, acc2_hbm, part_hbm, m2_ref,
    out_ref, far, a2, ps, sems,
):
    nrows, width = out_ref.shape
    nblk = nrows // BLK
    chunks = width // CHUNK
    copies = []
    for j in range(chunks):
        cols = pl.ds(j * CHUNK, CHUNK)
        ca = pltpu.make_async_copy(acc2_hbm.at[:, cols], a2.at[:, cols], sems.at[2 * j])
        cp = pltpu.make_async_copy(part_hbm.at[:, cols], ps.at[:, cols], sems.at[2 * j + 1])
        ca.start()
        cp.start()
        copies.append((ca, cp))
    far[...] = jnp.zeros(far.shape, f32)
    far[:BLK, :] = jnp.dot(band_ref[:BLK, :BLK], lo_ref[...], preferred_element_type=f32)
    last = (nblk - 1) * BLK
    far[last : last + BLK, :] = jnp.dot(
        band_ref[last : last + BLK, 2 * BLK :], hi_ref[...], preferred_element_type=f32
    )
    far_cap = farw_ref.shape[0]
    nptr = ptr_ref.shape[1]

    def slot(k, carry):
        row = 0
        for r in range(1, nptr):
            row = row + jnp.where(ptr_ref[0, r] <= k, 1, 0)
        start = pl.multiple_of(row * BLK, BLK)
        far[pl.ds(start, BLK), :] += slot_product(col_ref, farw_ref, arr_ref, k)
        return carry

    lax.fori_loop(0, far_cap, slot, 0)
    m2 = m2_ref[...]
    for j in range(chunks):
        ca, cp = copies[j]
        ca.wait()
        cp.wait()
        cols = slice(j * CHUNK, (j + 1) * CHUNK)
        two = (a2[:, cols] + far[:nrows, cols]).astype(bf16)
        v = ps[:, cols] + jnp.dot(two, m2, preferred_element_type=f32)
        out_ref[:, cols] = v.astype(bf16)


def vmem():
    return pl.BlockSpec(memory_space=pltpu.VMEM)


def smem():
    return pl.BlockSpec(memory_space=pltpu.SMEM)


def hbm():
    return pl.BlockSpec(memory_space=pltpu.HBM)


BIG_VMEM = pltpu.CompilerParams(vmem_limit_bytes=48 * 1024 * 1024)


def scratch(field):
    nrows, width = field.shape
    return [pltpu.VMEM((nrows + BLK, width), f32), pltpu.VMEM((nrows + 2 * BLK, width), bf16)]


def early(far_col, far_ptr, requested, export_block, field, lo, hi, arrived, band, farw3):
    nrows, width = field.shape
    return pl.pallas_call(
        early_kernel,
        in_specs=[smem()] * 4 + [vmem()] * 6,
        out_specs=[vmem(), vmem()],
        out_shape=[
            jax.ShapeDtypeStruct(arrived.shape, bf16),
            jax.ShapeDtypeStruct((2, BLK, width), bf16),
        ],
        scratch_shapes=[pltpu.VMEM((4, BLK, width), bf16)],
        compiler_params=BIG_VMEM,
        cost_estimate=pl.CostEstimate(
            flops=2 * BLK * BLK * width * (12 + farw3.shape[0]),
            transcendentals=0,
            bytes_accessed=2 * width * (nrows + 2 * arrived.shape[0] * BLK),
        ),
    )(far_col, far_ptr, requested, export_block, field, lo, hi, arrived, band, farw3)


def hop1(far_col, far_ptr, field, lo, hi, arrived, band, farw3, features, mix):
    nrows, width = field.shape
    return pl.pallas_call(
        hop1_kernel,
        in_specs=[smem(), smem()] + [vmem()] * 6 + [hbm(), vmem()],
        out_specs=[vmem(), vmem(), vmem(), vmem()],
        out_shape=[
            jax.ShapeDtypeStruct((nrows, width), bf16),
            jax.ShapeDtypeStruct((nrows, width), f32),
            jax.ShapeDtypeStruct((nrows, width), f32),
            jax.ShapeDtypeStruct((CHUNK, CHUNK), bf16),
        ],
        scratch_shapes=scratch(field)
        + [pltpu.VMEM((nrows, width), bf16), pltpu.SemaphoreType.DMA((1,))],
        compiler_params=pltpu.CompilerParams(),
        cost_estimate=pl.CostEstimate(
            flops=2 * BLK * BLK * width * (6 * nrows // BLK + farw3.shape[0])
            + 2 * nrows * width * CHUNK * 2,
            transcendentals=0,
            bytes_accessed=2 * width * (nrows * 9 + arrived.shape[0] * BLK),
        ),
    )(far_col, far_ptr, field, lo, hi, arrived, band, farw3, features, mix)


def hop2(far_col, far_ptr, lo, hi, arrived, band, farw3, acc2, part, m2):
    nrows, width = part.shape
    return pl.pallas_call(
        hop2_kernel,
        in_specs=[smem(), smem()] + [vmem()] * 5 + [hbm(), hbm(), vmem()],
        out_specs=vmem(),
        out_shape=jax.ShapeDtypeStruct((nrows, width), bf16),
        scratch_shapes=[
            pltpu.VMEM((nrows + BLK, width), f32),
            pltpu.VMEM((nrows, width), f32),
            pltpu.VMEM((nrows, width), f32),
            pltpu.SemaphoreType.DMA((2 * (width // CHUNK),)),
        ],
        compiler_params=pltpu.CompilerParams(),
        cost_estimate=pl.CostEstimate(
            flops=2 * BLK * BLK * width * (farw3.shape[0] + 2) + 2 * nrows * width * CHUNK,
            transcendentals=0,
            bytes_accessed=4 * width * nrows * 3,
        ),
    )(far_col, far_ptr, lo, hi, arrived, band, farw3, acc2, part, m2)


def halo(first, last):
    count = lax.axis_size("node")
    forward = [(i, i + 1) for i in range(count - 1)]
    backward = [(t, s) for s, t in forward]
    lo = lax.ppermute(last, "node", forward)
    hi = lax.ppermute(first, "node", backward)
    return lo, hi


def local(
    features,
    filter_gate_weight,
    skip_weight,
    mix_weight,
    band_weight,
    far_weight,
    far_ptr,
    far_col,
    export_block,
):
    node_rows = features.shape[0]
    blocks = node_rows // BLK
    far_cap = far_col.shape[1]

    own_index = lax.axis_index("node")
    own_exports = lax.dynamic_slice_in_dim(export_block, own_index, 1, 0)[0].astype(jnp.int32)
    peer_count = far_cap + 1
    info_all = lax.all_to_all(prep(far_col, far_ptr), "node", split_axis=0, concat_axis=0, tiled=True)
    slot_ids = jnp.arange(far_cap, dtype=jnp.int32)
    cols_all = info_all[:, :far_cap]
    hits = (cols_all // EXPORT == own_index) & (slot_ids[None, :] < info_all[:, far_cap:])
    requested = jnp.sum(jnp.where(hits, cols_all % EXPORT, 0), axis=1).astype(jnp.int32)
    hidden, ex2 = front_hidden(export_block, features, filter_gate_weight)
    blocks = node_rows // BLK
    width = hidden.shape[1]
    farw3 = far_weight.reshape(BLK, far_cap, BLK).transpose(1, 0, 2)

    def exchange(send):
        return lax.all_to_all(send, "node", split_axis=0, concat_axis=0, tiled=True)

    arrived1 = exchange(jnp.where((requested == 0)[:, None, None], ex2[0][None], ex2[1][None]))
    lo1, hi1 = halo(hidden[:BLK], hidden[node_rows - BLK :])
    skip_out = front_skip(hidden, skip_weight)
    send2, edge = early(
        far_col, far_ptr, requested, export_block, hidden, lo1, hi1, arrived1, band_weight, farw3
    )
    arrived2 = exchange(send2)
    lo2, hi2 = halo(edge[0], edge[1])
    hop_one, part, acc2, m2 = hop1(
        far_col, far_ptr, hidden, lo1, hi1, arrived1, band_weight, farw3, features, mix_weight
    )
    residual = hop2(
        far_col, far_ptr, lo2, hi2, arrived2, band_weight, farw3, acc2, part, m2
    )
    return residual, skip_out


def solution(mesh):
    placed = (
        P(("groups", "node"), None),
        P(),
        P(),
        P(),
        P("node", None),
        P(None, "node"),
        P("node", None),
        P("node", None),
        P(),
    )
    return jax.shard_map(
        local,
        mesh=mesh,
        in_specs=placed,
        out_specs=(P(("groups", "node"), None), P(("groups", "node"), None)),
        check_vma=False,
    )
```

```python
import functools

import jax
import jax.numpy as jnp
from jax import lax
from jax.experimental import pallas as pl
from jax.experimental.pallas import tpu as pltpu
from jax.sharding import PartitionSpec as P

BLK = 64
TOUT = 16
DILATION_STEP = 16
EXPORT = 2
CHANNEL_WIDTH = 32
S = 256
TIN = 32
CHUNK = 256
ROW_TILE = 256

f32 = jnp.float32
bf16 = jnp.bfloat16


def bd_inkernel(w, reps):
    r, c = w.shape
    shape_r = (reps * r, r)
    rep_r = jnp.where(
        lax.broadcasted_iota(jnp.int32, shape_r, 0) % r == lax.broadcasted_iota(jnp.int32, shape_r, 1),
        1.0, 0.0,
    ).astype(bf16)
    shape_c = (c, reps * c)
    rep_c = jnp.where(
        lax.broadcasted_iota(jnp.int32, shape_c, 1) % c == lax.broadcasted_iota(jnp.int32, shape_c, 0),
        1.0, 0.0,
    ).astype(bf16)
    rows = jnp.dot(rep_r, w, preferred_element_type=f32).astype(bf16)
    tiled = jnp.dot(rows, rep_c, preferred_element_type=f32)
    shape = tiled.shape
    mask = lax.broadcasted_iota(jnp.int32, shape, 0) // r == lax.broadcasted_iota(jnp.int32, shape, 1) // c
    return jnp.where(mask, tiled, 0.0).astype(bf16)


def hidden_kernel(exp_ref, x_ref, fgw_ref, h_ref, ex_ref):
    rows, cols = x_ref.shape
    half = cols // 2
    cw = fgw_ref.shape[0] // 2
    per = CHUNK // cw
    w = fgw_ref[...]
    wlo = jnp.concatenate([bd_inkernel(w[:cw, :cw], per), bd_inkernel(w[:cw, cw:], per)], axis=1)
    whi = jnp.concatenate([bd_inkernel(w[cw:, :cw], per), bd_inkernel(w[cw:, cw:], per)], axis=1)
    tile = min(ROW_TILE, rows)
    for t in range(rows // tile):
        rs = slice(t * tile, (t + 1) * tile)
        for j in range(half // CHUNK):
            x0 = x_ref[rs, j * CHUNK : (j + 1) * CHUNK]
            x1 = x_ref[rs, half + j * CHUNK : half + (j + 1) * CHUNK]
            pre = jnp.dot(x0, wlo, preferred_element_type=f32)
            pre = pre + jnp.dot(x1, whi, preferred_element_type=f32)
            h_ref[rs, j * CHUNK : (j + 1) * CHUNK] = (
                jnp.tanh(pre[:, :CHUNK]) * jax.nn.sigmoid(pre[:, CHUNK:])
            ).astype(bf16)
    own = lax.axis_index("node")
    for e in range(ex_ref.shape[0]):
        ex_ref[e] = h_ref[pl.ds(pl.multiple_of(exp_ref[e, own] * BLK, BLK), BLK), :]


def prep_kernel(col_ref, ptr_ref, out_ref):
    far_cap = col_ref.shape[1]
    peers = out_ref.shape[0]
    used = jnp.max(ptr_ref[...], axis=1, keepdims=True)
    out_ref[:, :far_cap] = jnp.broadcast_to(col_ref[...], (peers, far_cap))
    out_ref[:, far_cap:] = jnp.broadcast_to(used, (peers, 1))


def prep(far_col, far_ptr):
    far_cap = far_col.shape[1]
    return pl.pallas_call(
        prep_kernel,
        in_specs=[vmem(), vmem()],
        out_specs=vmem(),
        out_shape=jax.ShapeDtypeStruct((far_cap + 1, far_cap + 1), jnp.int32),
    )(far_col, far_ptr)


def skip_kernel(h_ref, sw_ref, s_ref, ws):
    cw = sw_ref.shape[0]

    @pl.when(pl.program_id(0) == 0)
    def _():
        ws[...] = bd_inkernel(sw_ref[...], CHUNK // cw)

    skip_w = ws.shape[1]
    for j in range(h_ref.shape[1] // CHUNK):
        s_ref[:, j * skip_w : (j + 1) * skip_w] = jnp.dot(
            h_ref[:, j * CHUNK : (j + 1) * CHUNK], ws[...], preferred_element_type=f32
        ).astype(bf16)


def front_hidden(export_block, features, fgw):
    rows, cols = features.shape
    half = cols // 2
    return pl.pallas_call(
        hidden_kernel,
        in_specs=[smem(), vmem(), vmem()],
        out_specs=[vmem(), vmem()],
        out_shape=[
            jax.ShapeDtypeStruct((rows, half), bf16),
            jax.ShapeDtypeStruct((export_block.shape[0], BLK, half), bf16),
        ],
        compiler_params=pltpu.CompilerParams(vmem_limit_bytes=48 * 1024 * 1024),
        cost_estimate=pl.CostEstimate(
            flops=2 * rows * CHUNK * 4 * CHUNK * (half // CHUNK),
            transcendentals=rows * half * 2,
            bytes_accessed=2 * rows * (cols + half),
        ),
    )(export_block, features, fgw)


def front_skip(hidden, skip_weight):
    rows, width = hidden.shape
    chunks = width // CHUNK
    cw, s = skip_weight.shape
    per = CHUNK // cw
    skip_cols = s * per * chunks
    tile = min(ROW_TILE, rows)
    return pl.pallas_call(
        skip_kernel,
        grid=(rows // tile,),
        in_specs=[
            pl.BlockSpec((tile, width), lambda i: (i, 0)),
            pl.BlockSpec(skip_weight.shape, lambda i: (0, 0)),
        ],
        out_specs=pl.BlockSpec((tile, skip_cols), lambda i: (i, 0)),
        out_shape=jax.ShapeDtypeStruct((rows, skip_cols), bf16),
        scratch_shapes=[pltpu.VMEM((CHUNK, s * per), bf16)],
        compiler_params=pltpu.CompilerParams(vmem_limit_bytes=48 * 1024 * 1024),
        cost_estimate=pl.CostEstimate(
            flops=2 * rows * CHUNK * s * per * chunks,
            transcendentals=0,
            bytes_accessed=2 * rows * (CHUNK * chunks + skip_cols),
        ),
    )(hidden, skip_weight)


def fill_pad(field_ref, lo_ref, hi_ref, pad):
    nrows = field_ref.shape[0]
    pad[:BLK, :] = lo_ref[...]
    pad[BLK : BLK + nrows, :] = field_ref[...]
    pad[BLK + nrows :, :] = hi_ref[...]


def band_block(band_ref, pad, t):
    start = pl.multiple_of(t * BLK, BLK)
    return jnp.dot(
        band_ref[pl.ds(start, BLK), :], pad[pl.ds(start, 3 * BLK), :], preferred_element_type=f32
    )


def slot_product(col_ref, farw_ref, arr_ref, k):
    return jnp.dot(farw_ref[k], arr_ref[col_ref[0, k] // EXPORT], preferred_element_type=f32)


def accumulate(col_ref, ptr_ref, field_ref, lo_ref, hi_ref, arr_ref, band_ref, farw_ref, acc, pad):
    nblk = field_ref.shape[0] // BLK
    far_cap = farw_ref.shape[0]
    nptr = ptr_ref.shape[1]
    fill_pad(field_ref, lo_ref, hi_ref, pad)
    for r in range(nblk):
        acc[r * BLK : (r + 1) * BLK, :] = band_block(band_ref, pad, r)
    acc[nblk * BLK :, :] = jnp.zeros((BLK, acc.shape[1]), f32)

    def slot(k, carry):
        row = 0
        for r in range(1, nptr):
            row = row + jnp.where(ptr_ref[0, r] <= k, 1, 0)
        start = pl.multiple_of(row * BLK, BLK)
        acc[pl.ds(start, BLK), :] += slot_product(col_ref, farw_ref, arr_ref, k)
        return carry

    lax.fori_loop(0, far_cap, slot, 0)


def early_kernel(
    col_ref, ptr_ref, req_ref, exp_ref, field_ref, lo_ref, hi_ref, arr_ref, band_ref, farw_ref,
    send_ref, edge_ref, pad, blk,
):
    nblk = field_ref.shape[0] // BLK
    own = lax.axis_index("node")
    fill_pad(field_ref, lo_ref, hi_ref, pad)
    targets = [exp_ref[own, 0], exp_ref[own, 1], 0, nblk - 1]
    for i, t in enumerate(targets):
        v = band_block(band_ref, pad, t)

        def slot(k, acc):
            return acc + slot_product(col_ref, farw_ref, arr_ref, k)

        v = lax.fori_loop(ptr_ref[0, t], ptr_ref[0, t + 1], slot, v)
        blk[i] = v.astype(bf16)

    def body(p, carry):
        send_ref[p] = blk[req_ref[p]]
        return carry

    lax.fori_loop(0, send_ref.shape[0], body, 0)
    edge_ref[0] = blk[2]
    edge_ref[1] = blk[3]


def hop1_kernel(
    col_ref, ptr_ref, field_ref, lo_ref, hi_ref, arr_ref, band_ref, farw_ref, x_hbm, mix_ref,
    out_ref, part_ref, acc2_ref, m2_ref, acc, pad, xs, sems,
):
    nrows, width = field_ref.shape
    nblk = nrows // BLK
    half = x_hbm.shape[1] // 2
    x_copy = pltpu.make_async_copy(x_hbm.at[:, pl.ds(half, width)], xs, sems.at[0])
    x_copy.start()
    accumulate(col_ref, ptr_ref, field_ref, lo_ref, hi_ref, arr_ref, band_ref, farw_ref, acc, pad)
    out_ref[...] = acc[:nrows, :].astype(bf16)
    zero = jnp.zeros((BLK, width), bf16)
    fill_pad(out_ref, zero, zero, pad)
    for r in range(nblk):
        acc2_ref[r * BLK : (r + 1) * BLK, :] = band_block(band_ref, pad, r)
    cw = mix_ref.shape[1]
    per = CHUNK // cw
    mix = mix_ref[...]
    m0 = bd_inkernel(mix[:cw], per)
    m1 = bd_inkernel(mix[cw : 2 * cw], per)
    m2_ref[...] = bd_inkernel(mix[2 * cw :], per)
    x_copy.wait()
    for j in range(width // CHUNK):
        cols = slice(j * CHUNK, (j + 1) * CHUNK)
        v = xs[:, cols].astype(f32)
        v = v + jnp.dot(field_ref[:, cols], m0, preferred_element_type=f32)
        v = v + jnp.dot(out_ref[:, cols], m1, preferred_element_type=f32)
        part_ref[:, cols] = v


def hop2_kernel(
    col_ref, ptr_ref, lo_ref, hi_ref, arr_ref, band_ref, farw_ref, acc2_hbm, part_hbm, m2_ref,
    out_ref, far, a2, ps, sems,
):
    nrows, width = out_ref.shape
    nblk = nrows // BLK
    chunks = width // CHUNK
    copies = []
    for j in range(chunks):
        cols = pl.ds(j * CHUNK, CHUNK)
        ca = pltpu.make_async_copy(acc2_hbm.at[:, cols], a2.at[:, cols], sems.at[2 * j])
        cp = pltpu.make_async_copy(part_hbm.at[:, cols], ps.at[:, cols], sems.at[2 * j + 1])
        ca.start()
        cp.start()
        copies.append((ca, cp))
    far[...] = jnp.zeros(far.shape, f32)
    far[:BLK, :] = jnp.dot(band_ref[:BLK, :BLK], lo_ref[...], preferred_element_type=f32)
    last = (nblk - 1) * BLK
    far[last : last + BLK, :] = jnp.dot(
        band_ref[last : last + BLK, 2 * BLK :], hi_ref[...], preferred_element_type=f32
    )
    far_cap = farw_ref.shape[0]
    nptr = ptr_ref.shape[1]

    def slot(k, carry):
        row = 0
        for r in range(1, nptr):
            row = row + jnp.where(ptr_ref[0, r] <= k, 1, 0)
        start = pl.multiple_of(row * BLK, BLK)
        far[pl.ds(start, BLK), :] += slot_product(col_ref, farw_ref, arr_ref, k)
        return carry

    lax.fori_loop(0, far_cap, slot, 0)
    m2 = m2_ref[...]
    for j in range(chunks):
        ca, cp = copies[j]
        ca.wait()
        cp.wait()
        cols = slice(j * CHUNK, (j + 1) * CHUNK)
        two = (a2[:, cols] + far[:nrows, cols]).astype(bf16)
        v = ps[:, cols] + jnp.dot(two, m2, preferred_element_type=f32)
        out_ref[:, cols] = v.astype(bf16)


def vmem():
    return pl.BlockSpec(memory_space=pltpu.VMEM)


def smem():
    return pl.BlockSpec(memory_space=pltpu.SMEM)


def hbm():
    return pl.BlockSpec(memory_space=pltpu.HBM)


BIG_VMEM = pltpu.CompilerParams(vmem_limit_bytes=48 * 1024 * 1024)


def scratch(field):
    nrows, width = field.shape
    return [pltpu.VMEM((nrows + BLK, width), f32), pltpu.VMEM((nrows + 2 * BLK, width), bf16)]


def early(far_col, far_ptr, requested, export_block, field, lo, hi, arrived, band, farw3):
    nrows, width = field.shape
    return pl.pallas_call(
        early_kernel,
        in_specs=[smem()] * 4 + [vmem()] * 6,
        out_specs=[vmem(), vmem()],
        out_shape=[
            jax.ShapeDtypeStruct(arrived.shape, bf16),
            jax.ShapeDtypeStruct((2, BLK, width), bf16),
        ],
        scratch_shapes=[pltpu.VMEM((nrows + 2 * BLK, width), bf16), pltpu.VMEM((4, BLK, width), bf16)],
        compiler_params=BIG_VMEM,
        cost_estimate=pl.CostEstimate(
            flops=2 * BLK * BLK * width * (12 + farw3.shape[0]),
            transcendentals=0,
            bytes_accessed=2 * width * (nrows + 2 * arrived.shape[0] * BLK),
        ),
    )(far_col, far_ptr, requested, export_block, field, lo, hi, arrived, band, farw3)


def hop1(far_col, far_ptr, field, lo, hi, arrived, band, farw3, features, mix):
    nrows, width = field.shape
    return pl.pallas_call(
        hop1_kernel,
        in_specs=[smem(), smem()] + [vmem()] * 6 + [hbm(), vmem()],
        out_specs=[vmem(), vmem(), vmem(), vmem()],
        out_shape=[
            jax.ShapeDtypeStruct((nrows, width), bf16),
            jax.ShapeDtypeStruct((nrows, width), f32),
            jax.ShapeDtypeStruct((nrows, width), f32),
            jax.ShapeDtypeStruct((CHUNK, CHUNK), bf16),
        ],
        scratch_shapes=scratch(field)
        + [pltpu.VMEM((nrows, width), bf16), pltpu.SemaphoreType.DMA((1,))],
        compiler_params=pltpu.CompilerParams(),
        cost_estimate=pl.CostEstimate(
            flops=2 * BLK * BLK * width * (6 * nrows // BLK + farw3.shape[0])
            + 2 * nrows * width * CHUNK * 2,
            transcendentals=0,
            bytes_accessed=2 * width * (nrows * 9 + arrived.shape[0] * BLK),
        ),
    )(far_col, far_ptr, field, lo, hi, arrived, band, farw3, features, mix)


def hop2(far_col, far_ptr, lo, hi, arrived, band, farw3, acc2, part, m2):
    nrows, width = part.shape
    return pl.pallas_call(
        hop2_kernel,
        in_specs=[smem(), smem()] + [vmem()] * 5 + [hbm(), hbm(), vmem()],
        out_specs=vmem(),
        out_shape=jax.ShapeDtypeStruct((nrows, width), bf16),
        scratch_shapes=[
            pltpu.VMEM((nrows + BLK, width), f32),
            pltpu.VMEM((nrows, width), f32),
            pltpu.VMEM((nrows, width), f32),
            pltpu.SemaphoreType.DMA((2 * (width // CHUNK),)),
        ],
        compiler_params=pltpu.CompilerParams(),
        cost_estimate=pl.CostEstimate(
            flops=2 * BLK * BLK * width * (farw3.shape[0] + 2) + 2 * nrows * width * CHUNK,
            transcendentals=0,
            bytes_accessed=4 * width * nrows * 3,
        ),
    )(far_col, far_ptr, lo, hi, arrived, band, farw3, acc2, part, m2)


def halo(first, last):
    count = lax.axis_size("node")
    forward = [(i, i + 1) for i in range(count - 1)]
    backward = [(t, s) for s, t in forward]
    lo = lax.ppermute(last, "node", forward)
    hi = lax.ppermute(first, "node", backward)
    return lo, hi


def local(
    features,
    filter_gate_weight,
    skip_weight,
    mix_weight,
    band_weight,
    far_weight,
    far_ptr,
    far_col,
    export_block,
):
    node_rows = features.shape[0]
    blocks = node_rows // BLK
    far_cap = far_col.shape[1]

    own_index = lax.axis_index("node")
    own_exports = lax.dynamic_slice_in_dim(export_block, own_index, 1, 0)[0].astype(jnp.int32)
    peer_count = far_cap + 1
    info_all = lax.all_to_all(prep(far_col, far_ptr), "node", split_axis=0, concat_axis=0, tiled=True)
    slot_ids = jnp.arange(far_cap, dtype=jnp.int32)
    cols_all = info_all[:, :far_cap]
    hits = (cols_all // EXPORT == own_index) & (slot_ids[None, :] < info_all[:, far_cap:])
    requested = jnp.sum(jnp.where(hits, cols_all % EXPORT, 0), axis=1).astype(jnp.int32)
    hidden, ex2 = front_hidden(export_block.T, features, filter_gate_weight)
    blocks = node_rows // BLK
    width = hidden.shape[1]
    farw3 = far_weight.reshape(BLK, far_cap, BLK).transpose(1, 0, 2)

    def exchange(send):
        return lax.all_to_all(send, "node", split_axis=0, concat_axis=0, tiled=True)

    arrived1 = exchange(jnp.where((requested == 0)[:, None, None], ex2[0][None], ex2[1][None]))
    lo1, hi1 = halo(hidden[:BLK], hidden[node_rows - BLK :])
    skip_out = front_skip(hidden, skip_weight)
    send2, edge = early(
        far_col, far_ptr, requested, export_block, hidden, lo1, hi1, arrived1, band_weight, farw3
    )
    arrived2 = exchange(send2)
    lo2, hi2 = halo(edge[0], edge[1])
    hop_one, part, acc2, m2 = hop1(
        far_col, far_ptr, hidden, lo1, hi1, arrived1, band_weight, farw3, features, mix_weight
    )
    residual = hop2(
        far_col, far_ptr, lo2, hi2, arrived2, band_weight, farw3, acc2, part, m2
    )
    return residual, skip_out


def solution(mesh):
    placed = (
        P(("groups", "node"), None),
        P(),
        P(),
        P(),
        P("node", None),
        P(None, "node"),
        P("node", None),
        P("node", None),
        P(),
    )
    return jax.shard_map(
        local,
        mesh=mesh,
        in_specs=placed,
        out_specs=(P(("groups", "node"), None), P(("groups", "node"), None)),
        check_vma=False,
    )
```

```python
import functools

import jax
import jax.numpy as jnp
from jax import lax
from jax.experimental import pallas as pl
from jax.experimental.pallas import tpu as pltpu
from jax.sharding import PartitionSpec as P

BLK = 64
TOUT = 16
DILATION_STEP = 16
EXPORT = 2
CHANNEL_WIDTH = 32
S = 256
TIN = 32
CHUNK = 256
ROW_TILE = 256

f32 = jnp.float32
bf16 = jnp.bfloat16


def bd_inkernel(w, reps):
    r, c = w.shape
    shape_r = (reps * r, r)
    rep_r = jnp.where(
        lax.broadcasted_iota(jnp.int32, shape_r, 0) % r == lax.broadcasted_iota(jnp.int32, shape_r, 1),
        1.0, 0.0,
    ).astype(bf16)
    shape_c = (c, reps * c)
    rep_c = jnp.where(
        lax.broadcasted_iota(jnp.int32, shape_c, 1) % c == lax.broadcasted_iota(jnp.int32, shape_c, 0),
        1.0, 0.0,
    ).astype(bf16)
    rows = jnp.dot(rep_r, w, preferred_element_type=f32).astype(bf16)
    tiled = jnp.dot(rows, rep_c, preferred_element_type=f32)
    shape = tiled.shape
    mask = lax.broadcasted_iota(jnp.int32, shape, 0) // r == lax.broadcasted_iota(jnp.int32, shape, 1) // c
    return jnp.where(mask, tiled, 0.0).astype(bf16)


def hidden_kernel(exp_ref, x_ref, fgw_ref, h_ref, ex_ref):
    rows, cols = x_ref.shape
    half = cols // 2
    cw = fgw_ref.shape[0] // 2
    per = CHUNK // cw
    w = fgw_ref[...]
    wlo = jnp.concatenate([bd_inkernel(w[:cw, :cw], per), bd_inkernel(w[:cw, cw:], per)], axis=1)
    whi = jnp.concatenate([bd_inkernel(w[cw:, :cw], per), bd_inkernel(w[cw:, cw:], per)], axis=1)
    tile = min(ROW_TILE, rows)
    for t in range(rows // tile):
        rs = slice(t * tile, (t + 1) * tile)
        for j in range(half // CHUNK):
            x0 = x_ref[rs, j * CHUNK : (j + 1) * CHUNK]
            x1 = x_ref[rs, half + j * CHUNK : half + (j + 1) * CHUNK]
            pre = jnp.dot(x0, wlo, preferred_element_type=f32)
            pre = pre + jnp.dot(x1, whi, preferred_element_type=f32)
            h_ref[rs, j * CHUNK : (j + 1) * CHUNK] = (
                jnp.tanh(pre[:, :CHUNK]) * jax.nn.sigmoid(pre[:, CHUNK:])
            ).astype(bf16)
    own = lax.axis_index("node")
    for e in range(ex_ref.shape[0]):
        ex_ref[e] = h_ref[pl.ds(pl.multiple_of(exp_ref[e, own] * BLK, BLK), BLK), :]


def prep_kernel(col_ref, ptr_ref, out_ref):
    far_cap = col_ref.shape[1]
    peers = out_ref.shape[0]
    used = jnp.max(ptr_ref[...], axis=1, keepdims=True)
    out_ref[:, :far_cap] = jnp.broadcast_to(col_ref[...], (peers, far_cap))
    out_ref[:, far_cap:] = jnp.broadcast_to(used, (peers, 1))


def prep(far_col, far_ptr):
    far_cap = far_col.shape[1]
    return pl.pallas_call(
        prep_kernel,
        in_specs=[vmem(), vmem()],
        out_specs=vmem(),
        out_shape=jax.ShapeDtypeStruct((far_cap + 1, far_cap + 1), jnp.int32),
    )(far_col, far_ptr)


def skip_kernel(h_ref, sw_ref, s_ref, ws):
    cw = sw_ref.shape[0]

    @pl.when(pl.program_id(0) == 0)
    def _():
        ws[...] = bd_inkernel(sw_ref[...], CHUNK // cw)

    skip_w = ws.shape[1]
    for j in range(h_ref.shape[1] // CHUNK):
        s_ref[:, j * skip_w : (j + 1) * skip_w] = jnp.dot(
            h_ref[:, j * CHUNK : (j + 1) * CHUNK], ws[...], preferred_element_type=f32
        ).astype(bf16)


def front_hidden(export_block, features, fgw):
    rows, cols = features.shape
    half = cols // 2
    return pl.pallas_call(
        hidden_kernel,
        in_specs=[smem(), vmem(), vmem()],
        out_specs=[vmem(), vmem()],
        out_shape=[
            jax.ShapeDtypeStruct((rows, half), bf16),
            jax.ShapeDtypeStruct((export_block.shape[0], BLK, half), bf16),
        ],
        compiler_params=pltpu.CompilerParams(vmem_limit_bytes=48 * 1024 * 1024),
        cost_estimate=pl.CostEstimate(
            flops=2 * rows * CHUNK * 4 * CHUNK * (half // CHUNK),
            transcendentals=rows * half * 2,
            bytes_accessed=2 * rows * (cols + half),
        ),
    )(export_block, features, fgw)


def front_skip(hidden, skip_weight):
    rows, width = hidden.shape
    chunks = width // CHUNK
    cw, s = skip_weight.shape
    per = CHUNK // cw
    skip_cols = s * per * chunks
    tile = min(ROW_TILE, rows)
    return pl.pallas_call(
        skip_kernel,
        grid=(rows // tile,),
        in_specs=[
            pl.BlockSpec((tile, width), lambda i: (i, 0)),
            pl.BlockSpec(skip_weight.shape, lambda i: (0, 0)),
        ],
        out_specs=pl.BlockSpec((tile, skip_cols), lambda i: (i, 0)),
        out_shape=jax.ShapeDtypeStruct((rows, skip_cols), bf16),
        scratch_shapes=[pltpu.VMEM((CHUNK, s * per), bf16)],
        compiler_params=pltpu.CompilerParams(vmem_limit_bytes=48 * 1024 * 1024),
        cost_estimate=pl.CostEstimate(
            flops=2 * rows * CHUNK * s * per * chunks,
            transcendentals=0,
            bytes_accessed=2 * rows * (CHUNK * chunks + skip_cols),
        ),
    )(hidden, skip_weight)


def fill_pad(field_ref, lo_ref, hi_ref, pad):
    nrows = field_ref.shape[0]
    pad[:BLK, :] = lo_ref[...]
    pad[BLK : BLK + nrows, :] = field_ref[...]
    pad[BLK + nrows :, :] = hi_ref[...]


def band_block(band_ref, pad, t):
    start = pl.multiple_of(t * BLK, BLK)
    return jnp.dot(
        band_ref[pl.ds(start, BLK), :], pad[pl.ds(start, 3 * BLK), :], preferred_element_type=f32
    )


def slot_product(col_ref, farw_ref, arr_ref, k):
    return jnp.dot(farw_ref[k], arr_ref[col_ref[0, k] // EXPORT], preferred_element_type=f32)


def accumulate(col_ref, ptr_ref, field_ref, lo_ref, hi_ref, arr_ref, band_ref, farw_ref, acc, pad):
    nblk = field_ref.shape[0] // BLK
    far_cap = farw_ref.shape[0]
    nptr = ptr_ref.shape[1]
    fill_pad(field_ref, lo_ref, hi_ref, pad)
    for r in range(nblk):
        acc[r * BLK : (r + 1) * BLK, :] = band_block(band_ref, pad, r)
    acc[nblk * BLK :, :] = jnp.zeros((BLK, acc.shape[1]), f32)

    def slot(k, carry):
        row = 0
        for r in range(1, nptr):
            row = row + jnp.where(ptr_ref[0, r] <= k, 1, 0)
        start = pl.multiple_of(row * BLK, BLK)
        acc[pl.ds(start, BLK), :] += slot_product(col_ref, farw_ref, arr_ref, k)
        return carry

    lax.fori_loop(0, far_cap, slot, 0)


def early_kernel(
    col_ref, ptr_ref, req_ref, exp_ref, field_ref, lo_ref, hi_ref, arr_ref, band_ref, farw_ref,
    send_ref, edge_ref, blk,
):
    nblk = field_ref.shape[0] // BLK
    own = lax.axis_index("node")
    targets = [exp_ref[own, 0], exp_ref[own, 1], 0, nblk - 1]
    for i, t in enumerate(targets):
        pieces = []
        for s in range(3):
            b = jnp.clip(t - 1 + s, 0, nblk - 1)
            v = field_ref[pl.ds(pl.multiple_of(b * BLK, BLK), BLK), :]
            if s == 0:
                v = jnp.where(t == 0, lo_ref[...], v)
            if s == 2:
                v = jnp.where(t == nblk - 1, hi_ref[...], v)
            pieces.append(v)
        win = jnp.concatenate(pieces, axis=0)
        start = pl.multiple_of(t * BLK, BLK)
        v = jnp.dot(band_ref[pl.ds(start, BLK), :], win, preferred_element_type=f32)

        def slot(k, acc):
            return acc + slot_product(col_ref, farw_ref, arr_ref, k)

        v = lax.fori_loop(ptr_ref[0, t], ptr_ref[0, t + 1], slot, v)
        blk[i] = v.astype(bf16)

    def body(p, carry):
        send_ref[p] = blk[req_ref[p]]
        return carry

    lax.fori_loop(0, send_ref.shape[0], body, 0)
    edge_ref[0] = blk[2]
    edge_ref[1] = blk[3]


def hop1_kernel(
    col_ref, ptr_ref, field_ref, lo_ref, hi_ref, arr_ref, band_ref, farw_ref, x_hbm, mix_ref,
    out_ref, part_ref, acc2_ref, m2_ref, acc, pad, xs, sems,
):
    nrows, width = field_ref.shape
    nblk = nrows // BLK
    half = x_hbm.shape[1] // 2
    x_copy = pltpu.make_async_copy(x_hbm.at[:, pl.ds(half, width)], xs, sems.at[0])
    x_copy.start()
    accumulate(col_ref, ptr_ref, field_ref, lo_ref, hi_ref, arr_ref, band_ref, farw_ref, acc, pad)
    out_ref[...] = acc[:nrows, :].astype(bf16)
    zero = jnp.zeros((BLK, width), bf16)
    fill_pad(out_ref, zero, zero, pad)
    for r in range(nblk):
        acc2_ref[r * BLK : (r + 1) * BLK, :] = band_block(band_ref, pad, r)
    cw = mix_ref.shape[1]
    per = CHUNK // cw
    mix = mix_ref[...]
    m0 = bd_inkernel(mix[:cw], per)
    m1 = bd_inkernel(mix[cw : 2 * cw], per)
    m2_ref[...] = bd_inkernel(mix[2 * cw :], per)
    x_copy.wait()
    for j in range(width // CHUNK):
        cols = slice(j * CHUNK, (j + 1) * CHUNK)
        v = xs[:, cols].astype(f32)
        v = v + jnp.dot(field_ref[:, cols], m0, preferred_element_type=f32)
        v = v + jnp.dot(out_ref[:, cols], m1, preferred_element_type=f32)
        part_ref[:, cols] = v


def hop2_kernel(
    col_ref, ptr_ref, lo_ref, hi_ref, arr_ref, band_ref, farw_ref, acc2_hbm, part_hbm, m2_ref,
    out_ref, far, a2, ps, sems,
):
    nrows, width = out_ref.shape
    nblk = nrows // BLK
    chunks = width // CHUNK
    copies = []
    for j in range(chunks):
        cols = pl.ds(j * CHUNK, CHUNK)
        ca = pltpu.make_async_copy(acc2_hbm.at[:, cols], a2.at[:, cols], sems.at[2 * j])
        cp = pltpu.make_async_copy(part_hbm.at[:, cols], ps.at[:, cols], sems.at[2 * j + 1])
        ca.start()
        cp.start()
        copies.append((ca, cp))
    far[...] = jnp.zeros(far.shape, f32)
    far[:BLK, :] = jnp.dot(band_ref[:BLK, :BLK], lo_ref[...], preferred_element_type=f32)
    last = (nblk - 1) * BLK
    far[last : last + BLK, :] = jnp.dot(
        band_ref[last : last + BLK, 2 * BLK :], hi_ref[...], preferred_element_type=f32
    )
    far_cap = farw_ref.shape[0]
    nptr = ptr_ref.shape[1]

    def slot(k, carry):
        row = 0
        for r in range(1, nptr):
            row = row + jnp.where(ptr_ref[0, r] <= k, 1, 0)
        start = pl.multiple_of(row * BLK, BLK)
        far[pl.ds(start, BLK), :] += slot_product(col_ref, farw_ref, arr_ref, k)
        return carry

    lax.fori_loop(0, far_cap, slot, 0)
    m2 = m2_ref[...]
    for j in range(chunks):
        ca, cp = copies[j]
        ca.wait()
        cp.wait()
        cols = slice(j * CHUNK, (j + 1) * CHUNK)
        two = (a2[:, cols] + far[:nrows, cols]).astype(bf16)
        v = ps[:, cols] + jnp.dot(two, m2, preferred_element_type=f32)
        out_ref[:, cols] = v.astype(bf16)


def vmem():
    return pl.BlockSpec(memory_space=pltpu.VMEM)


def smem():
    return pl.BlockSpec(memory_space=pltpu.SMEM)


def hbm():
    return pl.BlockSpec(memory_space=pltpu.HBM)


BIG_VMEM = pltpu.CompilerParams(vmem_limit_bytes=48 * 1024 * 1024)


def scratch(field):
    nrows, width = field.shape
    return [pltpu.VMEM((nrows + BLK, width), f32), pltpu.VMEM((nrows + 2 * BLK, width), bf16)]


def early(far_col, far_ptr, requested, export_block, field, lo, hi, arrived, band, farw3):
    nrows, width = field.shape
    return pl.pallas_call(
        early_kernel,
        in_specs=[smem()] * 4 + [vmem()] * 6,
        out_specs=[vmem(), vmem()],
        out_shape=[
            jax.ShapeDtypeStruct(arrived.shape, bf16),
            jax.ShapeDtypeStruct((2, BLK, width), bf16),
        ],
        scratch_shapes=[pltpu.VMEM((4, BLK, width), bf16)],
        compiler_params=BIG_VMEM,
        cost_estimate=pl.CostEstimate(
            flops=2 * BLK * BLK * width * (12 + farw3.shape[0]),
            transcendentals=0,
            bytes_accessed=2 * width * (nrows + 2 * arrived.shape[0] * BLK),
        ),
    )(far_col, far_ptr, requested, export_block, field, lo, hi, arrived, band, farw3)


def hop1(far_col, far_ptr, field, lo, hi, arrived, band, farw3, features, mix):
    nrows, width = field.shape
    return pl.pallas_call(
        hop1_kernel,
        in_specs=[smem(), smem()] + [vmem()] * 6 + [hbm(), vmem()],
        out_specs=[vmem(), vmem(), vmem(), vmem()],
        out_shape=[
            jax.ShapeDtypeStruct((nrows, width), bf16),
            jax.ShapeDtypeStruct((nrows, width), f32),
            jax.ShapeDtypeStruct((nrows, width), f32),
            jax.ShapeDtypeStruct((CHUNK, CHUNK), bf16),
        ],
        scratch_shapes=scratch(field)
        + [pltpu.VMEM((nrows, width), bf16), pltpu.SemaphoreType.DMA((1,))],
        compiler_params=pltpu.CompilerParams(),
        cost_estimate=pl.CostEstimate(
            flops=2 * BLK * BLK * width * (6 * nrows // BLK + farw3.shape[0])
            + 2 * nrows * width * CHUNK * 2,
            transcendentals=0,
            bytes_accessed=2 * width * (nrows * 9 + arrived.shape[0] * BLK),
        ),
    )(far_col, far_ptr, field, lo, hi, arrived, band, farw3, features, mix)


def hop2(far_col, far_ptr, lo, hi, arrived, band, farw3, acc2, part, m2):
    nrows, width = part.shape
    return pl.pallas_call(
        hop2_kernel,
        in_specs=[smem(), smem()] + [vmem()] * 5 + [hbm(), hbm(), vmem()],
        out_specs=vmem(),
        out_shape=jax.ShapeDtypeStruct((nrows, width), bf16),
        scratch_shapes=[
            pltpu.VMEM((nrows + BLK, width), f32),
            pltpu.VMEM((nrows, width), f32),
            pltpu.VMEM((nrows, width), f32),
            pltpu.SemaphoreType.DMA((2 * (width // CHUNK),)),
        ],
        compiler_params=pltpu.CompilerParams(),
        cost_estimate=pl.CostEstimate(
            flops=2 * BLK * BLK * width * (farw3.shape[0] + 2) + 2 * nrows * width * CHUNK,
            transcendentals=0,
            bytes_accessed=4 * width * nrows * 3,
        ),
    )(far_col, far_ptr, lo, hi, arrived, band, farw3, acc2, part, m2)


def halo(first, last):
    count = lax.axis_size("node")
    forward = [(i, i + 1) for i in range(count - 1)]
    backward = [(t, s) for s, t in forward]
    lo = lax.ppermute(last, "node", forward)
    hi = lax.ppermute(first, "node", backward)
    return lo, hi


def local(
    features,
    filter_gate_weight,
    skip_weight,
    mix_weight,
    band_weight,
    far_weight,
    far_ptr,
    far_col,
    export_block,
):
    node_rows = features.shape[0]
    blocks = node_rows // BLK
    far_cap = far_col.shape[1]

    own_index = lax.axis_index("node")
    own_exports = lax.dynamic_slice_in_dim(export_block, own_index, 1, 0)[0].astype(jnp.int32)
    peer_count = far_cap + 1
    info_all = lax.all_to_all(prep(far_col, far_ptr), "node", split_axis=0, concat_axis=0, tiled=True)
    slot_ids = jnp.arange(far_cap, dtype=jnp.int32)
    cols_all = info_all[:, :far_cap]
    hits = (cols_all // EXPORT == own_index) & (slot_ids[None, :] < info_all[:, far_cap:])
    requested = jnp.sum(jnp.where(hits, cols_all % EXPORT, 0), axis=1).astype(jnp.int32)
    hidden, ex2 = front_hidden(export_block.T, features, filter_gate_weight)
    blocks = node_rows // BLK
    width = hidden.shape[1]
    farw3 = far_weight.reshape(BLK, far_cap, BLK).transpose(1, 0, 2)

    def exchange(send):
        return lax.all_to_all(send, "node", split_axis=0, concat_axis=0, tiled=True)

    arrived1 = exchange(jnp.where((requested == 0)[:, None, None], ex2[0][None], ex2[1][None]))
    lo1, hi1 = halo(hidden[:BLK], hidden[node_rows - BLK :])
    skip_out = front_skip(hidden, skip_weight)
    send2, edge = early(
        far_col, far_ptr, requested, export_block, hidden, lo1, hi1, arrived1, band_weight, farw3
    )
    arrived2 = exchange(send2)
    lo2, hi2 = halo(edge[0], edge[1])
    hop_one, part, acc2, m2 = hop1(
        far_col, far_ptr, hidden, lo1, hi1, arrived1, band_weight, farw3, features, mix_weight
    )
    residual = hop2(
        far_col, far_ptr, lo2, hi2, arrived2, band_weight, farw3, acc2, part, m2
    )
    return residual, skip_out


def solution(mesh):
    placed = (
        P(("groups", "node"), None),
        P(),
        P(),
        P(),
        P("node", None),
        P(None, "node"),
        P("node", None),
        P("node", None),
        P(),
    )
    return jax.shard_map(
        local,
        mesh=mesh,
        in_specs=placed,
        out_specs=(P(("groups", "node"), None), P(("groups", "node"), None)),
        check_vma=False,
    )
```
